32 devices in a mesh: tm: 2 (over x), prow: 4 (over z), pcol: 4 (over y, core).
Axes of the slice: x: 2, y: 2, z: 4, core: 2. Of those that a mesh axis runs over, the one named last changes fastest.
Arguments:
- signal: bfloat16 [2048, 15360], P(('prow', 'pcol'), 'tm'), may hold values from -8 to 8
- offsets: int32 [4], replicated, may hold values from 0 to 511, as said below
- pair_list: int32 [4, 4, 4, 2], P('prow', 'pcol'), may hold values from 0 to 3, as said below
Outputs:
- correlations: bfloat16 [4, 4, 4, 128, 128, 256], P('prow', 'pcol', None, 'tm')
The draws below stay inside these ranges and needn't reach their ends.
Inputs may be any that keep to these rules, and one draw needn't show every extreme that they name: `offsets`: some window has the largest offset. `pair_list`: entry (a, b) of cell (r, c) pairs row block r n + a with column block b n + c, n the number of devices of pcol, and the row block's number is never above the column block's; pairs may repeat.
All inputs are finite; a program needn't handle non-finite values.
Results may differ from the reference program's by a relative error of at most 0.0058.
Values may be sent and summed in bfloat16 or wider, within the bound.
No kernel may reach another device: no remote copies, remote signals or barrier semaphores. Data moves between devices by JAX's collectives and lax.ppermute only.
A program may use at most 128 MiB of HBM per device.

```python
import math
import jax
import jax.numpy as jnp
from jax import lax

CB = 128
WIN = 7680
NF = 384
K0 = 32
LAGS = 256
SPAN = 4
MAXOFF = 512
NP = 4
STEP = 3840
HALO = 4352
WINDOWS = 4
SAMPLES = 15360
CHANNELS = 2048
N_PROW = 4
N_PCOL = 4


def draw_signal(key, part):
    key_level = jax.random.fold_in(key, 11)
    key_rough = jax.random.fold_in(key, 12)
    channel_level = jnp.exp(jax.random.uniform(key_level, (CHANNELS, 1), jnp.float32, math.log(0.25), math.log(2.0)))
    value = channel_level * jax.random.normal(key_rough, (CHANNELS, SAMPLES), jnp.float32)
    return jnp.clip(value, -8.0, 8.0).astype(jnp.bfloat16)


def draw_offsets(key, part):
    key_values = jax.random.fold_in(key, 21)
    key_place = jax.random.fold_in(key, 22)
    values = jax.random.randint(key_values, (WINDOWS,), 0, MAXOFF, dtype=jnp.int32)
    place = jax.random.randint(key_place, (), 0, WINDOWS, dtype=jnp.int32)
    marker = jnp.arange(WINDOWS, dtype=jnp.int32) == place
    return jnp.where(marker, MAXOFF - 1, values).astype(jnp.int32)


def draw_pair_list(key, part):
    key_col = jax.random.fold_in(key, 31)
    key_row = jax.random.fold_in(key, 32)
    grid_row = jnp.arange(N_PROW, dtype=jnp.int32)[:, None, None]
    grid_col = jnp.arange(N_PCOL, dtype=jnp.int32)[None, :, None]
    pair_idx = jnp.arange(NP, dtype=jnp.int32)[None, None, :]
    col_raw = jax.random.randint(key_col, (N_PROW, N_PCOL, NP), 0, 1 << 20, dtype=jnp.int32)
    col_pick = grid_row + col_raw % (N_PROW - grid_row)
    col_pick = jnp.where(pair_idx == 0, N_PROW - 1, col_pick)
    row_raw = jax.random.randint(key_row, (N_PROW, N_PCOL, NP), 0, 1 << 20, dtype=jnp.int32)
    row_pick = jnp.where(col_pick == grid_row, row_raw % (grid_col + 1), row_raw % N_PCOL)
    return jnp.stack([row_pick, col_pick], axis=-1).astype(jnp.int32)


def setup_inputs(seed: int = 0) -> dict:
    splits = jax.random.split(jax.random.key(seed), 4)
    signal = draw_signal(jax.random.fold_in(splits[3], 71), 0)
    offsets = draw_offsets(jax.random.fold_in(splits[3], 71), 0)
    pair_list = draw_pair_list(jax.random.fold_in(splits[3], 71), 0)
    return {"signal": signal, "offsets": offsets, "pair_list": pair_list}


two_pi = 2.0 * math.pi

def forward_table():
    sample_idx = jnp.arange(WIN, dtype=jnp.int32)
    freq_bins = K0 + jnp.arange(NF, dtype=jnp.int32)
    wrapped = sample_idx[:, None] * freq_bins[None, :] % WIN
    phase_angle = wrapped.astype(jnp.float32) * (two_pi / WIN)
    taper_curve = 0.5 - 0.5 * jnp.cos(sample_idx.astype(jnp.float32) * (two_pi / WIN))
    cosine = taper_curve[:, None] * jnp.cos(phase_angle)
    sine = -taper_curve[:, None] * jnp.sin(phase_angle)
    return jnp.concatenate([cosine, sine], axis=1).astype(jnp.bfloat16)

def lag_table(count):
    freq_bins = K0 + jnp.arange(NF, dtype=jnp.int32)
    shifted = (jnp.arange(LAGS, dtype=jnp.int32) - LAGS // 2) % WIN
    wrapped = freq_bins[:, None] * shifted[None, :] % WIN
    phase_angle = wrapped.astype(jnp.float32) * (two_pi / WIN)
    factor = 1.0 / math.sqrt(NF * count)
    return jnp.concatenate([jnp.cos(phase_angle) * factor, -jnp.sin(phase_angle) * factor], axis=0).astype(jnp.bfloat16)

def whiten(spectra):
    real_part = spectra[..., :NF]
    imag_part = spectra[..., NF:]
    power_sum = real_part * real_part + imag_part * imag_part
    freq_bins = jnp.arange(NF, dtype=jnp.int32)
    band_matrix = (jnp.abs(freq_bins[:, None] - freq_bins[None, :]) <= SPAN).astype(jnp.float32)
    smooth = jnp.einsum('...f,fg->...g', power_sum, band_matrix, precision=lax.Precision.HIGHEST) / (2 * SPAN + 1)
    water_level = lax.optimization_barrier(jnp.mean(power_sum, axis=-1, keepdims=True))
    weight = lax.rsqrt(smooth + 0.5 * water_level + 1e-06)
    return (spectra * jnp.concatenate([weight, weight], axis=-1)).astype(jnp.bfloat16)

def correlate(row_block, col_block, lags):
    row_real = row_block[..., :NF].astype(jnp.float32)
    row_imag = row_block[..., NF:].astype(jnp.float32)
    col_real = col_block[..., :NF].astype(jnp.float32)
    col_imag = col_block[..., NF:].astype(jnp.float32)
    high = lax.Precision.HIGHEST
    real_sum = jnp.einsum('wif,wjf->ijf', row_real, col_real, precision=high) + jnp.einsum('wif,wjf->ijf', row_imag, col_imag, precision=high)
    imag_sum = jnp.einsum('wif,wjf->ijf', row_imag, col_real, precision=high) - jnp.einsum('wif,wjf->ijf', row_real, col_imag, precision=high)
    cross = jnp.concatenate([real_sum, imag_sum], axis=-1).astype(jnp.bfloat16)
    flat = cross.reshape(-1, 2 * NF)
    result = jnp.dot(flat, lags, preferred_element_type=jnp.float32).astype(jnp.bfloat16)
    return result.reshape(row_block.shape[1], col_block.shape[1], LAGS)

def reference(signal, offsets, pair_list):
    dft_table = forward_table()
    extended = jnp.concatenate([signal, jnp.zeros((CHANNELS, HALO), jnp.bfloat16)], axis=1)

    def one_window(index):
        first_sample = (index * STEP + offsets[index]).astype(jnp.int32)
        segment = lax.dynamic_slice_in_dim(extended, first_sample, WIN, 1)
        return jnp.dot(segment, dft_table, preferred_element_type=jnp.float32)
    spectra = lax.map(one_window, jnp.arange(WINDOWS, dtype=jnp.int32))
    whitened = whiten(spectra)
    blocks = whitened.reshape(WINDOWS, N_PROW, N_PCOL, CB, 2 * NF)
    lags = lag_table(WINDOWS)
    block_rows = min(16, CB)
    flat_pairs = pair_list.reshape(-1, 2)

    def one_pair(index):
        grid_row = index // (N_PCOL * NP)
        grid_col = index // NP % N_PCOL
        row_pick = flat_pairs[index, 0]
        col_pick = flat_pairs[index, 1]
        row_whole = blocks[:, grid_row, row_pick]
        col_whole = blocks[:, col_pick, grid_col]

        def one_block(first_row):
            row_block = lax.dynamic_slice_in_dim(row_whole, first_row, block_rows, 1)
            return correlate(row_block, col_whole, lags)
        stacked = lax.map(one_block, jnp.arange(0, CB, block_rows, dtype=jnp.int32))
        return stacked.reshape(CB, CB, LAGS)
    result = lax.map(one_pair, jnp.arange(N_PROW * N_PCOL * NP, dtype=jnp.int32))
    return result.reshape(N_PROW, N_PCOL, NP, CB, CB, LAGS)
```

```python
import math

import jax
import jax.numpy as jnp
from jax import lax
from jax.sharding import PartitionSpec as P

WIN = 7680
NF = 384
K0 = 32
LAGS = 256
SPAN = 4
NP = 4
STEP = 3840
HALO = 4352


two_pi = 2.0 * math.pi


def from_behind(value, axis, steps):
    count = lax.axis_size(axis)
    initial, last = (max(0, -steps), min(count, count - steps))
    return lax.ppermute(value, axis, [(source, source + steps) for source in range(initial, last)])


def forward_table():
    coarse = 128
    n_coarse = WIN // coarse
    freq_bins = K0 + jnp.arange(NF, dtype=jnp.int32)
    scale = two_pi / WIN
    high_idx = (jnp.arange(n_coarse, dtype=jnp.int32) * coarse)[:, None] * freq_bins[None, :] % WIN
    low_idx = jnp.arange(coarse, dtype=jnp.int32)[:, None] * freq_bins[None, :] % WIN
    high_angle = high_idx.astype(jnp.float32) * scale
    low_angle = low_idx.astype(jnp.float32) * scale
    high_cos, high_sin = jnp.cos(high_angle)[:, None, :], jnp.sin(high_angle)[:, None, :]
    low_cos, low_sin = jnp.cos(low_angle)[None], jnp.sin(low_angle)[None]
    cos_full = (high_cos * low_cos - high_sin * low_sin).reshape(WIN, NF)
    sin_full = (high_sin * low_cos + high_cos * low_sin).reshape(WIN, NF)
    sample_idx = jnp.arange(WIN, dtype=jnp.int32)
    taper_curve = 0.5 - 0.5 * jnp.cos(sample_idx.astype(jnp.float32) * (two_pi / WIN))
    cosine = taper_curve[:, None] * cos_full
    sine = -taper_curve[:, None] * sin_full
    return jnp.concatenate([cosine, sine], axis=1).astype(jnp.bfloat16)


def lag_table(count):
    freq_bins = K0 + jnp.arange(NF, dtype=jnp.int32)
    shifted = (jnp.arange(LAGS, dtype=jnp.int32) - LAGS // 2) % WIN
    wrapped = freq_bins[:, None] * shifted[None, :] % WIN
    phase_angle = wrapped.astype(jnp.float32) * (two_pi / WIN)
    factor = 1.0 / math.sqrt(NF * count)
    return jnp.concatenate(
        [jnp.cos(phase_angle) * factor, -jnp.sin(phase_angle) * factor], axis=0
    ).astype(jnp.bfloat16)


def whiten(spectra):
    real_part = spectra[..., :NF]
    imag_part = spectra[..., NF:]
    power_sum = real_part * real_part + imag_part * imag_part
    freq_bins = jnp.arange(NF, dtype=jnp.int32)
    band_matrix = (jnp.abs(freq_bins[:, None] - freq_bins[None, :]) <= SPAN).astype(jnp.float32)
    smooth = jnp.einsum(
        "...f,fg->...g", power_sum, band_matrix, precision=lax.Precision.HIGHEST
    ) / (2 * SPAN + 1)
    water_level = jnp.mean(power_sum, axis=-1, keepdims=True)
    weight = lax.rsqrt(smooth + 0.5 * water_level + 1e-06)
    return (spectra * jnp.concatenate([weight, weight], axis=-1)).astype(jnp.bfloat16)


def cross_pair(row_block, col_block, lags):
    row_real = row_block[..., :NF].astype(jnp.float32)[:, :, None, :]
    row_imag = row_block[..., NF:].astype(jnp.float32)[:, :, None, :]
    col_real = col_block[..., :NF].astype(jnp.float32)[:, None, :, :]
    col_imag = col_block[..., NF:].astype(jnp.float32)[:, None, :, :]
    real_sum = jnp.sum(row_real * col_real + row_imag * col_imag, axis=0)
    imag_sum = jnp.sum(row_imag * col_real - row_real * col_imag, axis=0)
    cross = jnp.concatenate([real_sum, imag_sum], axis=-1).astype(jnp.bfloat16)
    flat = cross.reshape(-1, 2 * NF)
    result = jnp.dot(flat, lags, preferred_element_type=jnp.float32).astype(jnp.bfloat16)
    return result.reshape(row_block.shape[1], col_block.shape[1], LAGS)


def on_device(signal, offsets, pair_list):
    channels_here = signal.shape[0]
    samples_here = signal.shape[1]
    w_dev = samples_here // STEP
    n_tm = lax.axis_size("tm")
    tm_index = lax.axis_index("tm")
    dft_table = forward_table()
    head_samples = signal[:, :HALO]
    next_head = from_behind(head_samples, "tm", -1)
    extended = jnp.concatenate([signal, next_head], axis=1)

    def one_window(window):
        first_sample = window * STEP + offsets[tm_index * w_dev + window]
        segment = lax.dynamic_slice_in_dim(extended, first_sample, WIN, 1)
        return jnp.dot(segment, dft_table, preferred_element_type=jnp.float32)

    spectra = lax.map(one_window, jnp.arange(w_dev, dtype=jnp.int32))
    whitened = whiten(spectra)
    own_piece = whitened[None]
    row_gathered = lax.all_gather(own_piece, ("tm", "pcol"), axis=0, tiled=True)
    col_gathered = lax.all_gather(own_piece, ("tm", "prow"), axis=0, tiled=True)
    row_gathered = row_gathered.reshape(n_tm, -1, w_dev, channels_here, 2 * NF)
    col_gathered = col_gathered.reshape(n_tm, -1, w_dev, channels_here, 2 * NF)
    pick_dim = 1
    lags = lag_table(n_tm * w_dev)
    local_pairs = pair_list[0, 0]
    half_rows = channels_here // n_tm
    first_row = tm_index * half_rows

    def one_pair(pair_index):
        row_pick = local_pairs[pair_index, 0]
        col_pick = local_pairs[pair_index, 1]
        row_whole = lax.dynamic_index_in_dim(row_gathered, row_pick, pick_dim, keepdims=False)
        col_whole = lax.dynamic_index_in_dim(col_gathered, col_pick, pick_dim, keepdims=False)
        row_whole = row_whole.reshape(n_tm * w_dev, channels_here, 2 * NF)
        col_whole = col_whole.reshape(n_tm * w_dev, channels_here, 2 * NF)
        row_block = lax.dynamic_slice_in_dim(row_whole, first_row, half_rows, 1)
        return cross_pair(row_block, col_whole, lags)

    result = lax.map(one_pair, jnp.arange(NP, dtype=jnp.int32))
    return result.reshape(1, 1, NP, half_rows, channels_here, LAGS)


def solution(mesh):
    placed = (P(("prow", "pcol"), "tm"), P(), P("prow", "pcol", None, None))
    return jax.shard_map(
        on_device,
        mesh=mesh,
        in_specs=placed,
        out_specs=P("prow", "pcol", None, "tm", None, None),
        check_vma=False,
    )
```

```python
import math

import jax
import jax.numpy as jnp
from jax import lax
from jax.sharding import PartitionSpec as P
from jax.experimental import pallas as pl
from jax.experimental.pallas import tpu as pltpu

WIN = 7680
NF = 384
K0 = 32
LAGS = 256
SPAN = 4
NP = 4
STEP = 3840
HALO = 4352


two_pi = 2.0 * math.pi


def from_behind(value, axis, steps):
    count = lax.axis_size(axis)
    initial, last = (max(0, -steps), min(count, count - steps))
    return lax.ppermute(value, axis, [(source, source + steps) for source in range(initial, last)])


def forward_table():
    coarse = 128
    n_coarse = WIN // coarse
    freq_bins = K0 + jnp.arange(NF, dtype=jnp.int32)
    scale = two_pi / WIN
    high_idx = (jnp.arange(n_coarse, dtype=jnp.int32) * coarse)[:, None] * freq_bins[None, :] % WIN
    low_idx = jnp.arange(coarse, dtype=jnp.int32)[:, None] * freq_bins[None, :] % WIN
    high_angle = high_idx.astype(jnp.float32) * scale
    low_angle = low_idx.astype(jnp.float32) * scale
    high_cos, high_sin = jnp.cos(high_angle)[:, None, :], jnp.sin(high_angle)[:, None, :]
    low_cos, low_sin = jnp.cos(low_angle)[None], jnp.sin(low_angle)[None]
    cos_full = (high_cos * low_cos - high_sin * low_sin).reshape(WIN, NF)
    sin_full = (high_sin * low_cos + high_cos * low_sin).reshape(WIN, NF)
    sample_idx = jnp.arange(WIN, dtype=jnp.int32)
    taper_curve = 0.5 - 0.5 * jnp.cos(sample_idx.astype(jnp.float32) * (two_pi / WIN))
    cosine = taper_curve[:, None] * cos_full
    sine = -taper_curve[:, None] * sin_full
    return jnp.concatenate([cosine, sine], axis=1).astype(jnp.bfloat16)


def lag_table(count):
    freq_bins = K0 + jnp.arange(NF, dtype=jnp.int32)
    shifted = (jnp.arange(LAGS, dtype=jnp.int32) - LAGS // 2) % WIN
    wrapped = freq_bins[:, None] * shifted[None, :] % WIN
    phase_angle = wrapped.astype(jnp.float32) * (two_pi / WIN)
    factor = 1.0 / math.sqrt(NF * count)
    return jnp.concatenate(
        [jnp.cos(phase_angle) * factor, -jnp.sin(phase_angle) * factor], axis=0
    ).astype(jnp.bfloat16)


def whiten(spectra):
    real_part = spectra[..., :NF]
    imag_part = spectra[..., NF:]
    power_sum = real_part * real_part + imag_part * imag_part
    freq_bins = jnp.arange(NF, dtype=jnp.int32)
    band_matrix = (jnp.abs(freq_bins[:, None] - freq_bins[None, :]) <= SPAN).astype(jnp.float32)
    smooth = jnp.einsum(
        "...f,fg->...g", power_sum, band_matrix, precision=lax.Precision.HIGHEST
    ) / (2 * SPAN + 1)
    water_level = jnp.mean(power_sum, axis=-1, keepdims=True)
    weight = lax.rsqrt(smooth + 0.5 * water_level + 1e-06)
    return (spectra * jnp.concatenate([weight, weight], axis=-1)).astype(jnp.bfloat16)


ROW_TILE = 8
J_CHUNK = 64
F_CHUNK = 128


def pair_kernel(pairs_ref, row_ref, col_ref, lags_ref, out_ref, cross_ref):
    windows = row_ref.shape[1]
    cols = col_ref.shape[2]

    for i in range(row_ref.shape[2]):
        for jc in range(cols // J_CHUNK):
            js = pl.ds(jc * J_CHUNK, J_CHUNK)
            for fc in range(NF // F_CHUNK):
                fr = pl.ds(fc * F_CHUNK, F_CHUNK)
                fi = pl.ds(NF + fc * F_CHUNK, F_CHUNK)
                acc_re = jnp.zeros((J_CHUNK, F_CHUNK), jnp.float32)
                acc_im = jnp.zeros((J_CHUNK, F_CHUNK), jnp.float32)
                for w in range(windows):
                    xr = row_ref[0, w, i : i + 1, fr]
                    xi = row_ref[0, w, i : i + 1, fi]
                    yr = col_ref[0, w, js, fr]
                    yi = col_ref[0, w, js, fi]
                    acc_re = acc_re + xr * yr + xi * yi
                    acc_im = acc_im + xi * yr - xr * yi
                rows = pl.ds(i * cols + jc * J_CHUNK, J_CHUNK)
                cross_ref[rows, fr] = acc_re.astype(jnp.bfloat16)
                cross_ref[rows, fi] = acc_im.astype(jnp.bfloat16)
    result = jnp.dot(cross_ref[...], lags_ref[...], preferred_element_type=jnp.float32)
    out_ref[0] = result.reshape(out_ref.shape[1:]).astype(out_ref.dtype)


def all_pairs(pairs, row_all, col_all, lags):
    n_pairs = pairs.shape[0]
    windows, rows, cols = row_all.shape[1], row_all.shape[2], col_all.shape[2]
    tiles = rows // ROW_TILE
    grid_spec = pltpu.PrefetchScalarGridSpec(
        num_scalar_prefetch=1,
        grid=(n_pairs, tiles),
        in_specs=[
            pl.BlockSpec((1, windows, ROW_TILE, 2 * NF), lambda p, t, pr: (pr[p, 0], 0, t, 0)),
            pl.BlockSpec((1, windows, cols, 2 * NF), lambda p, t, pr: (pr[p, 1], 0, 0, 0)),
            pl.BlockSpec((2 * NF, LAGS), lambda p, t, pr: (0, 0)),
        ],
        out_specs=pl.BlockSpec((1, ROW_TILE, cols, LAGS), lambda p, t, pr: (p, t, 0, 0)),
        scratch_shapes=[pltpu.VMEM((ROW_TILE * cols, 2 * NF), jnp.bfloat16)],
    )
    flops = n_pairs * rows * cols * (2 * NF * windows * 4 + 2 * 2 * NF * LAGS)
    return pl.pallas_call(
        pair_kernel,
        grid_spec=grid_spec,
        out_shape=jax.ShapeDtypeStruct((n_pairs, rows, cols, LAGS), jnp.bfloat16),
        compiler_params=pltpu.CompilerParams(
            dimension_semantics=("arbitrary", "arbitrary"),
            vmem_limit_bytes=48 * 1024 * 1024,
        ),
        cost_estimate=pl.CostEstimate(
            flops=flops,
            transcendentals=0,
            bytes_accessed=n_pairs * (rows + cols) * windows * 2 * NF * 4 + n_pairs * rows * cols * LAGS * 2,
        ),
    )(pairs, row_all, col_all, lags)


def on_device(signal, offsets, pair_list):
    channels_here = signal.shape[0]
    samples_here = signal.shape[1]
    w_dev = samples_here // STEP
    n_tm = lax.axis_size("tm")
    tm_index = lax.axis_index("tm")
    dft_table = forward_table()
    head_samples = signal[:, :HALO]
    next_head = from_behind(head_samples, "tm", -1)
    extended = jnp.concatenate([signal, next_head], axis=1)

    def one_window(window):
        first_sample = window * STEP + offsets[tm_index * w_dev + window]
        segment = lax.dynamic_slice_in_dim(extended, first_sample, WIN, 1)
        return jnp.dot(segment, dft_table, preferred_element_type=jnp.float32)

    spectra = lax.map(one_window, jnp.arange(w_dev, dtype=jnp.int32))
    whitened = whiten(spectra)
    own_piece = whitened[None]
    row_gathered = lax.all_gather(own_piece, ("tm", "pcol"), axis=0, tiled=True)
    col_gathered = lax.all_gather(own_piece, ("tm", "prow"), axis=0, tiled=True)
    row_gathered = row_gathered.reshape(n_tm, -1, w_dev, channels_here, 2 * NF)
    col_gathered = col_gathered.reshape(n_tm, -1, w_dev, channels_here, 2 * NF)
    lags = lag_table(n_tm * w_dev)
    n_pcol = row_gathered.shape[1]
    n_prow = col_gathered.shape[1]
    half_rows = channels_here // n_tm
    row_part = lax.dynamic_slice_in_dim(row_gathered, tm_index * half_rows, half_rows, 3)
    row_all = jnp.transpose(row_part, (1, 0, 2, 3, 4)).reshape(n_pcol, n_tm * w_dev, half_rows, 2 * NF)
    col_all = jnp.transpose(col_gathered, (1, 0, 2, 3, 4)).reshape(n_prow, n_tm * w_dev, channels_here, 2 * NF)
    local_pairs = pair_list[0, 0]
    pairs = jnp.stack(
        [jnp.clip(local_pairs[:, 0], 0, n_pcol - 1), jnp.clip(local_pairs[:, 1], 0, n_prow - 1)], axis=1
    ).astype(jnp.int32)
    result = all_pairs(pairs, row_all.astype(jnp.float32), col_all.astype(jnp.float32), lags)
    return result.reshape(1, 1, NP, half_rows, channels_here, LAGS)


def solution(mesh):
    placed = (P(("prow", "pcol"), "tm"), P(), P("prow", "pcol", None, None))
    return jax.shard_map(
        on_device,
        mesh=mesh,
        in_specs=placed,
        out_specs=P("prow", "pcol", None, "tm", None, None),
        check_vma=False,
    )
```

```python
import itertools
import math

import jax
import jax.numpy as jnp
from jax import lax
from jax.sharding import PartitionSpec as P
from jax.experimental import pallas as pl
from jax.experimental.pallas import tpu as pltpu

WIN = 7680
NF = 384
K0 = 32
LAGS = 256
SPAN = 4
NP = 4
STEP = 3840
HALO = 4352


two_pi = 2.0 * math.pi


def from_behind(value, axis, steps):
    count = lax.axis_size(axis)
    initial, last = (max(0, -steps), min(count, count - steps))
    return lax.ppermute(value, axis, [(source, source + steps) for source in range(initial, last)])


def forward_table():
    coarse = 128
    n_coarse = WIN // coarse
    freq_bins = K0 + jnp.arange(NF, dtype=jnp.int32)
    scale = two_pi / WIN
    high_idx = (jnp.arange(n_coarse, dtype=jnp.int32) * coarse)[:, None] * freq_bins[None, :] % WIN
    low_idx = jnp.arange(coarse, dtype=jnp.int32)[:, None] * freq_bins[None, :] % WIN
    high_angle = high_idx.astype(jnp.float32) * scale
    low_angle = low_idx.astype(jnp.float32) * scale
    high_cos, high_sin, low_cos, low_sin = lax.optimization_barrier(
        (jnp.cos(high_angle), jnp.sin(high_angle), jnp.cos(low_angle), jnp.sin(low_angle))
    )
    high_cos, high_sin = high_cos[:, None, :], high_sin[:, None, :]
    low_cos, low_sin = low_cos[None], low_sin[None]
    cos_full = (high_cos * low_cos - high_sin * low_sin).reshape(WIN, NF)
    sin_full = (high_sin * low_cos + high_cos * low_sin).reshape(WIN, NF)
    sample_idx = jnp.arange(WIN, dtype=jnp.int32)
    taper_curve = 0.5 - 0.5 * jnp.cos(sample_idx.astype(jnp.float32) * (two_pi / WIN))
    cosine = taper_curve[:, None] * cos_full
    sine = -taper_curve[:, None] * sin_full
    return jnp.concatenate([cosine, sine], axis=1).astype(jnp.bfloat16)


def lag_table(count):
    freq_bins = K0 + jnp.arange(NF, dtype=jnp.int32)
    shifted = (jnp.arange(LAGS, dtype=jnp.int32) - LAGS // 2) % WIN
    wrapped = freq_bins[:, None] * shifted[None, :] % WIN
    phase_angle = wrapped.astype(jnp.float32) * (two_pi / WIN)
    factor = 1.0 / math.sqrt(NF * count)
    return jnp.concatenate(
        [jnp.cos(phase_angle) * factor, -jnp.sin(phase_angle) * factor], axis=0
    ).astype(jnp.bfloat16)


def whiten(spectra):
    real_part = spectra[..., :NF]
    imag_part = spectra[..., NF:]
    power_sum = real_part * real_part + imag_part * imag_part
    freq_bins = jnp.arange(NF, dtype=jnp.int32)
    band_matrix = (jnp.abs(freq_bins[:, None] - freq_bins[None, :]) <= SPAN).astype(jnp.float32)
    smooth = jnp.einsum(
        "...f,fg->...g", power_sum, band_matrix, precision=lax.Precision.HIGHEST
    ) / (2 * SPAN + 1)
    water_level = jnp.mean(power_sum, axis=-1, keepdims=True)
    weight = lax.rsqrt(smooth + 0.5 * water_level + 1e-06)
    return (spectra * jnp.concatenate([weight, weight], axis=-1)).astype(jnp.bfloat16)


ROW_TILE = 8
J_CHUNK = 64
F_CHUNK = 128


def pair_kernel(pairs_ref, row_ref, col_ref, lags_ref, out_ref, cross_ref):
    windows = row_ref.shape[1]
    cols = col_ref.shape[2]

    for i in range(row_ref.shape[2]):
        for jc in range(cols // J_CHUNK):
            js = pl.ds(jc * J_CHUNK, J_CHUNK)
            for fc in range(NF // F_CHUNK):
                fr = pl.ds(fc * F_CHUNK, F_CHUNK)
                fi = pl.ds(NF + fc * F_CHUNK, F_CHUNK)
                acc_re = jnp.zeros((J_CHUNK, F_CHUNK), jnp.float32)
                acc_im = jnp.zeros((J_CHUNK, F_CHUNK), jnp.float32)
                for w in range(windows):
                    xr = row_ref[0, w, i : i + 1, fr]
                    xi = row_ref[0, w, i : i + 1, fi]
                    yr = col_ref[0, w, js, fr]
                    yi = col_ref[0, w, js, fi]
                    acc_re = acc_re + xr * yr + xi * yi
                    acc_im = acc_im + xi * yr - xr * yi
                rows = pl.ds(i * cols + jc * J_CHUNK, J_CHUNK)
                cross_ref[rows, fr] = acc_re.astype(jnp.bfloat16)
                cross_ref[rows, fi] = acc_im.astype(jnp.bfloat16)
    result = jnp.dot(cross_ref[...], lags_ref[...], preferred_element_type=jnp.float32)
    out_ref[0] = result.reshape(out_ref.shape[1:]).astype(out_ref.dtype)


def all_pairs(pairs, row_all, col_all, lags):
    n_pairs = pairs.shape[0]
    windows, rows, cols = row_all.shape[1], row_all.shape[2], col_all.shape[2]
    tiles = rows // ROW_TILE
    grid_spec = pltpu.PrefetchScalarGridSpec(
        num_scalar_prefetch=1,
        grid=(n_pairs, tiles),
        in_specs=[
            pl.BlockSpec((1, windows, ROW_TILE, 2 * NF), lambda p, t, pr: (pr[p, 0], 0, t, 0)),
            pl.BlockSpec((1, windows, cols, 2 * NF), lambda p, t, pr: (pr[p, 1], 0, 0, 0)),
            pl.BlockSpec((2 * NF, LAGS), lambda p, t, pr: (0, 0)),
        ],
        out_specs=pl.BlockSpec((1, ROW_TILE, cols, LAGS), lambda p, t, pr: (p, t, 0, 0)),
        scratch_shapes=[pltpu.VMEM((ROW_TILE * cols, 2 * NF), jnp.bfloat16)],
    )
    flops = n_pairs * rows * cols * (2 * NF * windows * 4 + 2 * 2 * NF * LAGS)
    return pl.pallas_call(
        pair_kernel,
        grid_spec=grid_spec,
        out_shape=jax.ShapeDtypeStruct((n_pairs, rows, cols, LAGS), jnp.bfloat16),
        compiler_params=pltpu.CompilerParams(
            dimension_semantics=("arbitrary", "arbitrary"),
            vmem_limit_bytes=48 * 1024 * 1024,
        ),
        cost_estimate=pl.CostEstimate(
            flops=flops,
            transcendentals=0,
            bytes_accessed=n_pairs * (rows + cols) * windows * 2 * NF * 4 + n_pairs * rows * cols * LAGS * 2,
        ),
    )(pairs, row_all, col_all, lags)


def exchange(value, axes, sizes, moves):
    pairs = []
    for source in itertools.product(*[range(s) for s in sizes]):
        target = moves(source)
        if target is None:
            continue
        pairs.append((linear(source, sizes), linear(target, sizes)))
    if not pairs:
        return None
    return lax.ppermute(value, axes, pairs)


def linear(coord, sizes):
    index = 0
    for c, s in zip(coord, sizes):
        index = index * s + c
    return index


def on_device(signal, offsets, pair_list):
    channels_here = signal.shape[0]
    samples_here = signal.shape[1]
    w_dev = samples_here // STEP
    n_tm = lax.axis_size("tm")
    n_prow = lax.axis_size("prow")
    n_pcol = lax.axis_size("pcol")
    tm_index = lax.axis_index("tm")
    prow_index = lax.axis_index("prow")
    pcol_index = lax.axis_index("pcol")
    dft_table = forward_table()
    head_samples = signal[:, :HALO]
    next_head = from_behind(head_samples, "tm", -1)
    extended = jnp.concatenate([signal, next_head], axis=1)

    segments = [
        lax.dynamic_slice_in_dim(extended, window * STEP + offsets[tm_index * w_dev + window], WIN, 1)
        for window in range(w_dev)
    ]
    stacked = jnp.concatenate(segments, axis=0)
    spectra = jnp.dot(stacked, dft_table, preferred_element_type=jnp.float32)
    spectra = spectra.reshape(w_dev, channels_here, 2 * NF)
    whitened = whiten(spectra)
    half_rows = channels_here // n_tm

    row_slots = []
    for d in range(n_pcol):
        per_tm = []
        for e in range(n_tm):
            half = (tm_index - e + n_tm) % n_tm
            payload = lax.dynamic_slice_in_dim(whitened, half * half_rows, half_rows, 1)
            if d == 0 and e == 0:
                per_tm.append(payload)
                continue
            moved = exchange(
                payload, ("tm", "pcol"), (n_tm, n_pcol),
                lambda s, d=d, e=e: ((s[0] - e) % n_tm, (s[1] - d) % n_pcol),
            )
            per_tm.append(moved)
        row_slots.append(jnp.concatenate(per_tm, axis=0))
    row_all = jnp.stack(row_slots, axis=0)

    col_slots = []
    for d in range(n_prow):
        per_tm = []
        for e in range(n_tm):
            if d == 0 and e == 0:
                per_tm.append(whitened)
                continue
            moved = exchange(
                whitened, ("tm", "prow"), (n_tm, n_prow),
                lambda s, d=d, e=e: ((s[0] - e) % n_tm, s[1] - d) if s[1] - d >= 0 else None,
            )
            per_tm.append(moved)
        col_slots.append(jnp.concatenate(per_tm, axis=0))
    col_all = jnp.stack(col_slots, axis=0)

    lags = lag_table(n_tm * w_dev)
    local_pairs = pair_list[0, 0]
    row_slot = (local_pairs[:, 0] - pcol_index + n_pcol) % n_pcol
    col_slot = jnp.clip(local_pairs[:, 1] - prow_index, 0, n_prow - 1)
    pairs = jnp.stack([row_slot, col_slot], axis=1).astype(jnp.int32)
    result = all_pairs(pairs, row_all.astype(jnp.float32), col_all.astype(jnp.float32), lags)
    return result.reshape(1, 1, NP, half_rows, channels_here, LAGS)


def solution(mesh):
    placed = (P(("prow", "pcol"), "tm"), P(), P("prow", "pcol", None, None))
    return jax.shard_map(
        on_device,
        mesh=mesh,
        in_specs=placed,
        out_specs=P("prow", "pcol", None, "tm", None, None),
        check_vma=False,
    )
```

```python
import itertools
import math

import jax
import jax.numpy as jnp
from jax import lax
from jax.sharding import PartitionSpec as P
from jax.experimental import pallas as pl
from jax.experimental.pallas import tpu as pltpu

WIN = 7680
NF = 384
K0 = 32
LAGS = 256
SPAN = 4
NP = 4
STEP = 3840
HALO = 4352


two_pi = 2.0 * math.pi


def from_behind(value, axis, steps):
    count = lax.axis_size(axis)
    initial, last = (max(0, -steps), min(count, count - steps))
    return lax.ppermute(value, axis, [(source, source + steps) for source in range(initial, last)])


def forward_table():
    coarse = 128
    n_coarse = WIN // coarse
    freq_bins = K0 + jnp.arange(NF, dtype=jnp.int32)
    scale = two_pi / WIN
    high_idx = (jnp.arange(n_coarse, dtype=jnp.int32) * coarse)[:, None] * freq_bins[None, :] % WIN
    low_idx = jnp.arange(coarse, dtype=jnp.int32)[:, None] * freq_bins[None, :] % WIN
    high_angle = high_idx.astype(jnp.float32) * scale
    low_angle = low_idx.astype(jnp.float32) * scale
    high_cos, high_sin, low_cos, low_sin = lax.optimization_barrier(
        (jnp.cos(high_angle), jnp.sin(high_angle), jnp.cos(low_angle), jnp.sin(low_angle))
    )
    high_cos, high_sin = high_cos[:, None, :], high_sin[:, None, :]
    low_cos, low_sin = low_cos[None], low_sin[None]
    cos_full = high_cos * low_cos - high_sin * low_sin
    sin_full = high_sin * low_cos + high_cos * low_sin
    sample_idx = jnp.arange(WIN, dtype=jnp.int32)
    taper_curve = 0.5 - 0.5 * jnp.cos(sample_idx.astype(jnp.float32) * (two_pi / WIN))
    taper_curve = taper_curve.reshape(n_coarse, coarse, 1)
    table = jnp.concatenate([taper_curve * cos_full, -taper_curve * sin_full], axis=2).astype(jnp.bfloat16)
    return table.reshape(WIN, 2 * NF)


def lag_table(count):
    freq_bins = K0 + jnp.arange(NF, dtype=jnp.int32)
    shifted = (jnp.arange(LAGS, dtype=jnp.int32) - LAGS // 2) % WIN
    wrapped = freq_bins[:, None] * shifted[None, :] % WIN
    phase_angle = wrapped.astype(jnp.float32) * (two_pi / WIN)
    factor = 1.0 / math.sqrt(NF * count)
    return jnp.concatenate(
        [jnp.cos(phase_angle) * factor, -jnp.sin(phase_angle) * factor], axis=0
    ).astype(jnp.bfloat16)


def whiten(spectra):
    real_part = spectra[..., :NF]
    imag_part = spectra[..., NF:]
    power_sum = real_part * real_part + imag_part * imag_part
    freq_bins = jnp.arange(NF, dtype=jnp.int32)
    band_matrix = (jnp.abs(freq_bins[:, None] - freq_bins[None, :]) <= SPAN).astype(jnp.float32)
    smooth = jnp.einsum(
        "...f,fg->...g", power_sum, band_matrix, precision=lax.Precision.HIGHEST
    ) / (2 * SPAN + 1)
    water_level = jnp.mean(power_sum, axis=-1, keepdims=True)
    weight = lax.rsqrt(smooth + 0.5 * water_level + 1e-06)
    return (spectra * jnp.concatenate([weight, weight], axis=-1)).astype(jnp.bfloat16)


ROW_TILE = 8
J_CHUNK = 64
F_CHUNK = 128


def pair_kernel(pairs_ref, row_ref, col_ref, lags_ref, out_ref, cross_ref):
    windows = row_ref.shape[1]
    cols = col_ref.shape[2]

    for i in range(row_ref.shape[2]):
        for jc in range(cols // J_CHUNK):
            js = pl.ds(jc * J_CHUNK, J_CHUNK)
            for fc in range(NF // F_CHUNK):
                fr = pl.ds(fc * F_CHUNK, F_CHUNK)
                fi = pl.ds(NF + fc * F_CHUNK, F_CHUNK)
                acc_re = jnp.zeros((J_CHUNK, F_CHUNK), jnp.float32)
                acc_im = jnp.zeros((J_CHUNK, F_CHUNK), jnp.float32)
                for w in range(windows):
                    xr = row_ref[0, w, i : i + 1, fr]
                    xi = row_ref[0, w, i : i + 1, fi]
                    yr = col_ref[0, w, js, fr]
                    yi = col_ref[0, w, js, fi]
                    acc_re = acc_re + xr * yr + xi * yi
                    acc_im = acc_im + xi * yr - xr * yi
                rows = pl.ds(i * cols + jc * J_CHUNK, J_CHUNK)
                cross_ref[rows, fr] = acc_re.astype(jnp.bfloat16)
                cross_ref[rows, fi] = acc_im.astype(jnp.bfloat16)
    result = jnp.dot(cross_ref[...], lags_ref[...], preferred_element_type=jnp.float32)
    out_ref[0] = result.reshape(out_ref.shape[1:]).astype(out_ref.dtype)


def all_pairs(pairs, row_all, col_all, lags):
    n_pairs = pairs.shape[0]
    windows, rows, cols = row_all.shape[1], row_all.shape[2], col_all.shape[2]
    tiles = rows // ROW_TILE
    grid_spec = pltpu.PrefetchScalarGridSpec(
        num_scalar_prefetch=1,
        grid=(n_pairs, tiles),
        in_specs=[
            pl.BlockSpec((1, windows, ROW_TILE, 2 * NF), lambda p, t, pr: (pr[p, 0], 0, t, 0)),
            pl.BlockSpec((1, windows, cols, 2 * NF), lambda p, t, pr: (pr[p, 1], 0, 0, 0)),
            pl.BlockSpec((2 * NF, LAGS), lambda p, t, pr: (0, 0)),
        ],
        out_specs=pl.BlockSpec((1, ROW_TILE, cols, LAGS), lambda p, t, pr: (p, t, 0, 0)),
        scratch_shapes=[pltpu.VMEM((ROW_TILE * cols, 2 * NF), jnp.bfloat16)],
    )
    flops = n_pairs * rows * cols * (2 * NF * windows * 4 + 2 * 2 * NF * LAGS)
    return pl.pallas_call(
        pair_kernel,
        grid_spec=grid_spec,
        out_shape=jax.ShapeDtypeStruct((n_pairs, rows, cols, LAGS), jnp.bfloat16),
        compiler_params=pltpu.CompilerParams(
            dimension_semantics=("arbitrary", "arbitrary"),
            vmem_limit_bytes=48 * 1024 * 1024,
        ),
        cost_estimate=pl.CostEstimate(
            flops=flops,
            transcendentals=0,
            bytes_accessed=n_pairs * (rows + cols) * windows * 2 * NF * 4 + n_pairs * rows * cols * LAGS * 2,
        ),
    )(pairs, row_all, col_all, lags)


def exchange(value, axes, sizes, moves):
    pairs = []
    for source in itertools.product(*[range(s) for s in sizes]):
        target = moves(source)
        if target is None:
            continue
        pairs.append((linear(source, sizes), linear(target, sizes)))
    if not pairs:
        return None
    return lax.ppermute(value, axes, pairs)


def linear(coord, sizes):
    index = 0
    for c, s in zip(coord, sizes):
        index = index * s + c
    return index


def on_device(signal, offsets, pair_list):
    channels_here = signal.shape[0]
    samples_here = signal.shape[1]
    w_dev = samples_here // STEP
    n_tm = lax.axis_size("tm")
    n_prow = lax.axis_size("prow")
    n_pcol = lax.axis_size("pcol")
    tm_index = lax.axis_index("tm")
    prow_index = lax.axis_index("prow")
    pcol_index = lax.axis_index("pcol")
    dft_table = forward_table()
    head_samples = signal[:, :HALO]
    next_head = from_behind(head_samples, "tm", -1)
    extended = jnp.concatenate([signal, next_head], axis=1)

    segments = [
        lax.dynamic_slice_in_dim(extended, window * STEP + offsets[tm_index * w_dev + window], WIN, 1)
        for window in range(w_dev)
    ]
    stacked = jnp.concatenate(segments, axis=0)
    spectra = jnp.dot(stacked, dft_table, preferred_element_type=jnp.float32)
    spectra = spectra.reshape(w_dev, channels_here, 2 * NF)
    whitened = whiten(spectra)
    half_rows = channels_here // n_tm

    row_windows = [lax.dynamic_slice_in_dim(whitened, tm_index * half_rows, half_rows, 1)]
    for e in range(1, n_tm):
        half = (tm_index - e + n_tm) % n_tm
        payload = lax.dynamic_slice_in_dim(whitened, half * half_rows, half_rows, 1)
        row_windows.append(exchange(payload, ("tm",), (n_tm,), lambda s, e=e: ((s[0] - e) % n_tm,)))
    row_own = jnp.concatenate(row_windows, axis=0)
    row_slots = [row_own]
    for d in range(1, n_pcol):
        row_slots.append(exchange(row_own, ("pcol",), (n_pcol,), lambda s, d=d: ((s[0] - d) % n_pcol,)))
    row_all = jnp.stack(row_slots, axis=0)

    col_slots = []
    for d in range(n_prow):
        if d == 0:
            near = whitened
        else:
            near = exchange(whitened, ("prow",), (n_prow,), lambda s, d=d: (s[0] - d,) if s[0] - d >= 0 else None)
        per_tm = [near]
        for e in range(1, n_tm):
            per_tm.append(exchange(near, ("tm",), (n_tm,), lambda s, e=e: ((s[0] - e) % n_tm,)))
        col_slots.append(jnp.concatenate(per_tm, axis=0))
    col_all = jnp.stack(col_slots, axis=0)

    lags = lag_table(n_tm * w_dev)
    local_pairs = pair_list[0, 0]
    row_slot = (local_pairs[:, 0] - pcol_index + n_pcol) % n_pcol
    col_slot = jnp.clip(local_pairs[:, 1] - prow_index, 0, n_prow - 1)
    pairs = jnp.stack([row_slot, col_slot], axis=1).astype(jnp.int32)
    result = all_pairs(pairs, row_all.astype(jnp.float32), col_all.astype(jnp.float32), lags)
    return result.reshape(1, 1, NP, half_rows, channels_here, LAGS)


def solution(mesh):
    placed = (P(("prow", "pcol"), "tm"), P(), P("prow", "pcol", None, None))
    return jax.shard_map(
        on_device,
        mesh=mesh,
        in_specs=placed,
        out_specs=P("prow", "pcol", None, "tm", None, None),
        check_vma=False,
    )
```

```python
import itertools
import math

import jax
import jax.numpy as jnp
from jax import lax
from jax.sharding import PartitionSpec as P
from jax.experimental import pallas as pl
from jax.experimental.pallas import tpu as pltpu

WIN = 7680
NF = 384
K0 = 32
LAGS = 256
SPAN = 4
NP = 4
STEP = 3840
HALO = 4352


two_pi = 2.0 * math.pi


def from_behind(value, axis, steps):
    count = lax.axis_size(axis)
    initial, last = (max(0, -steps), min(count, count - steps))
    return lax.ppermute(value, axis, [(source, source + steps) for source in range(initial, last)])


def table_kernel(high_cos_ref, high_sin_ref, low_cos_ref, low_sin_ref, taper_ref, out_ref):
    hc = high_cos_ref[0]
    hs = high_sin_ref[0]
    lc = low_cos_ref[...]
    ls = low_sin_ref[...]
    taper = taper_ref[...]
    out_ref[:, :NF] = (taper * (hc * lc - hs * ls)).astype(out_ref.dtype)
    out_ref[:, NF:] = (-(taper * (hs * lc + hc * ls))).astype(out_ref.dtype)


def forward_table():
    coarse = 128
    n_coarse = WIN // coarse
    freq_bins = K0 + jnp.arange(NF, dtype=jnp.int32)
    scale = two_pi / WIN
    high_idx = (jnp.arange(n_coarse, dtype=jnp.int32) * coarse)[:, None] * freq_bins[None, :] % WIN
    low_idx = jnp.arange(coarse, dtype=jnp.int32)[:, None] * freq_bins[None, :] % WIN
    high_angle = high_idx.astype(jnp.float32) * scale
    low_angle = low_idx.astype(jnp.float32) * scale
    high_cos = jnp.cos(high_angle).reshape(n_coarse, 1, NF)
    high_sin = jnp.sin(high_angle).reshape(n_coarse, 1, NF)
    low_cos, low_sin = jnp.cos(low_angle), jnp.sin(low_angle)
    sample_idx = jnp.arange(WIN, dtype=jnp.int32)
    taper_curve = 0.5 - 0.5 * jnp.cos(sample_idx.astype(jnp.float32) * (two_pi / WIN))
    taper_curve = taper_curve[:, None]
    return pl.pallas_call(
        table_kernel,
        grid=(n_coarse,),
        in_specs=[
            pl.BlockSpec((1, 1, NF), lambda q: (q, 0, 0)),
            pl.BlockSpec((1, 1, NF), lambda q: (q, 0, 0)),
            pl.BlockSpec((coarse, NF), lambda q: (0, 0)),
            pl.BlockSpec((coarse, NF), lambda q: (0, 0)),
            pl.BlockSpec((coarse, 1), lambda q: (q, 0)),
        ],
        out_specs=pl.BlockSpec((coarse, 2 * NF), lambda q: (q, 0)),
        out_shape=jax.ShapeDtypeStruct((WIN, 2 * NF), jnp.bfloat16),
    )(high_cos, high_sin, low_cos, low_sin, taper_curve)


def lag_table(count):
    freq_bins = K0 + jnp.arange(NF, dtype=jnp.int32)
    shifted = (jnp.arange(LAGS, dtype=jnp.int32) - LAGS // 2) % WIN
    wrapped = freq_bins[:, None] * shifted[None, :] % WIN
    phase_angle = wrapped.astype(jnp.float32) * (two_pi / WIN)
    factor = 1.0 / math.sqrt(NF * count)
    return jnp.concatenate(
        [jnp.cos(phase_angle) * factor, -jnp.sin(phase_angle) * factor], axis=0
    ).astype(jnp.bfloat16)


def whiten(spectra):
    real_part = spectra[..., :NF]
    imag_part = spectra[..., NF:]
    power_sum = real_part * real_part + imag_part * imag_part
    freq_bins = jnp.arange(NF, dtype=jnp.int32)
    band_matrix = (jnp.abs(freq_bins[:, None] - freq_bins[None, :]) <= SPAN).astype(jnp.float32)
    smooth = jnp.einsum(
        "...f,fg->...g", power_sum, band_matrix, precision=lax.Precision.HIGHEST
    ) / (2 * SPAN + 1)
    water_level = jnp.mean(power_sum, axis=-1, keepdims=True)
    weight = lax.rsqrt(smooth + 0.5 * water_level + 1e-06)
    return (spectra * jnp.concatenate([weight, weight], axis=-1)).astype(jnp.bfloat16)


ROW_TILE = 8
J_CHUNK = 64
F_CHUNK = 128


def pair_kernel(pairs_ref, row_ref, col_ref, lags_ref, out_ref, cross_ref):
    windows = row_ref.shape[1]
    cols = col_ref.shape[2]

    for i in range(row_ref.shape[2]):
        for jc in range(cols // J_CHUNK):
            js = pl.ds(jc * J_CHUNK, J_CHUNK)
            for fc in range(NF // F_CHUNK):
                fr = pl.ds(fc * F_CHUNK, F_CHUNK)
                fi = pl.ds(NF + fc * F_CHUNK, F_CHUNK)
                acc_re = jnp.zeros((J_CHUNK, F_CHUNK), jnp.float32)
                acc_im = jnp.zeros((J_CHUNK, F_CHUNK), jnp.float32)
                for w in range(windows):
                    xr = row_ref[0, w, i : i + 1, fr]
                    xi = row_ref[0, w, i : i + 1, fi]
                    yr = col_ref[0, w, js, fr]
                    yi = col_ref[0, w, js, fi]
                    acc_re = acc_re + xr * yr + xi * yi
                    acc_im = acc_im + xi * yr - xr * yi
                rows = pl.ds(i * cols + jc * J_CHUNK, J_CHUNK)
                cross_ref[rows, fr] = acc_re.astype(jnp.bfloat16)
                cross_ref[rows, fi] = acc_im.astype(jnp.bfloat16)
    result = jnp.dot(cross_ref[...], lags_ref[...], preferred_element_type=jnp.float32)
    out_ref[0] = result.reshape(out_ref.shape[1:]).astype(out_ref.dtype)


def all_pairs(pairs, row_all, col_all, lags):
    n_pairs = pairs.shape[0]
    windows, rows, cols = row_all.shape[1], row_all.shape[2], col_all.shape[2]
    tiles = rows // ROW_TILE
    grid_spec = pltpu.PrefetchScalarGridSpec(
        num_scalar_prefetch=1,
        grid=(n_pairs, tiles),
        in_specs=[
            pl.BlockSpec((1, windows, ROW_TILE, 2 * NF), lambda p, t, pr: (pr[p, 0], 0, t, 0)),
            pl.BlockSpec((1, windows, cols, 2 * NF), lambda p, t, pr: (pr[p, 1], 0, 0, 0)),
            pl.BlockSpec((2 * NF, LAGS), lambda p, t, pr: (0, 0)),
        ],
        out_specs=pl.BlockSpec((1, ROW_TILE, cols, LAGS), lambda p, t, pr: (p, t, 0, 0)),
        scratch_shapes=[pltpu.VMEM((ROW_TILE * cols, 2 * NF), jnp.bfloat16)],
    )
    flops = n_pairs * rows * cols * (2 * NF * windows * 4 + 2 * 2 * NF * LAGS)
    return pl.pallas_call(
        pair_kernel,
        grid_spec=grid_spec,
        out_shape=jax.ShapeDtypeStruct((n_pairs, rows, cols, LAGS), jnp.bfloat16),
        compiler_params=pltpu.CompilerParams(
            dimension_semantics=("arbitrary", "arbitrary"),
            vmem_limit_bytes=48 * 1024 * 1024,
        ),
        cost_estimate=pl.CostEstimate(
            flops=flops,
            transcendentals=0,
            bytes_accessed=n_pairs * (rows + cols) * windows * 2 * NF * 4 + n_pairs * rows * cols * LAGS * 2,
        ),
    )(pairs, row_all, col_all, lags)


def exchange(value, axes, sizes, moves):
    pairs = []
    for source in itertools.product(*[range(s) for s in sizes]):
        target = moves(source)
        if target is None:
            continue
        pairs.append((linear(source, sizes), linear(target, sizes)))
    if not pairs:
        return None
    return lax.ppermute(value, axes, pairs)


def linear(coord, sizes):
    index = 0
    for c, s in zip(coord, sizes):
        index = index * s + c
    return index


def on_device(signal, offsets, pair_list):
    channels_here = signal.shape[0]
    samples_here = signal.shape[1]
    w_dev = samples_here // STEP
    n_tm = lax.axis_size("tm")
    n_prow = lax.axis_size("prow")
    n_pcol = lax.axis_size("pcol")
    tm_index = lax.axis_index("tm")
    prow_index = lax.axis_index("prow")
    pcol_index = lax.axis_index("pcol")
    dft_table = forward_table()
    head_samples = signal[:, :HALO]
    next_head = from_behind(head_samples, "tm", -1)
    extended = jnp.concatenate([signal, next_head], axis=1)

    segments = [
        lax.dynamic_slice_in_dim(extended, window * STEP + offsets[tm_index * w_dev + window], WIN, 1)
        for window in range(w_dev)
    ]
    stacked = jnp.concatenate(segments, axis=0)
    spectra = jnp.dot(stacked, dft_table, preferred_element_type=jnp.float32)
    spectra = spectra.reshape(w_dev, channels_here, 2 * NF)
    whitened = whiten(spectra)
    half_rows = channels_here // n_tm

    row_windows = [lax.dynamic_slice_in_dim(whitened, tm_index * half_rows, half_rows, 1)]
    for e in range(1, n_tm):
        half = (tm_index - e + n_tm) % n_tm
        payload = lax.dynamic_slice_in_dim(whitened, half * half_rows, half_rows, 1)
        row_windows.append(exchange(payload, ("tm",), (n_tm,), lambda s, e=e: ((s[0] - e) % n_tm,)))
    row_own = jnp.concatenate(row_windows, axis=0)
    row_slots = [row_own]
    for d in range(1, n_pcol):
        row_slots.append(exchange(row_own, ("pcol",), (n_pcol,), lambda s, d=d: ((s[0] - d) % n_pcol,)))
    row_all = jnp.stack(row_slots, axis=0)

    col_slots = []
    for d in range(n_prow):
        if d == 0:
            near = whitened
        else:
            near = exchange(whitened, ("prow",), (n_prow,), lambda s, d=d: (s[0] - d,) if s[0] - d >= 0 else None)
        per_tm = [near]
        for e in range(1, n_tm):
            per_tm.append(exchange(near, ("tm",), (n_tm,), lambda s, e=e: ((s[0] - e) % n_tm,)))
        col_slots.append(jnp.concatenate(per_tm, axis=0))
    col_all = jnp.stack(col_slots, axis=0)

    lags = lag_table(n_tm * w_dev)
    local_pairs = pair_list[0, 0]
    row_slot = (local_pairs[:, 0] - pcol_index + n_pcol) % n_pcol
    col_slot = jnp.clip(local_pairs[:, 1] - prow_index, 0, n_prow - 1)
    pairs = jnp.stack([row_slot, col_slot], axis=1).astype(jnp.int32)
    result = all_pairs(pairs, row_all.astype(jnp.float32), col_all.astype(jnp.float32), lags)
    return result.reshape(1, 1, NP, half_rows, channels_here, LAGS)


def solution(mesh):
    placed = (P(("prow", "pcol"), "tm"), P(), P("prow", "pcol", None, None))
    return jax.shard_map(
        on_device,
        mesh=mesh,
        in_specs=placed,
        out_specs=P("prow", "pcol", None, "tm", None, None),
        check_vma=False,
    )
```

```python
import itertools
import math

import jax
import jax.numpy as jnp
from jax import lax
from jax.sharding import PartitionSpec as P
from jax.experimental import pallas as pl
from jax.experimental.pallas import tpu as pltpu

WIN = 7680
NF = 384
K0 = 32
LAGS = 256
SPAN = 4
NP = 4
STEP = 3840
HALO = 4352


two_pi = 2.0 * math.pi


def from_behind(value, axis, steps):
    count = lax.axis_size(axis)
    initial, last = (max(0, -steps), min(count, count - steps))
    return lax.ppermute(value, axis, [(source, source + steps) for source in range(initial, last)])


TABLE_Q = 12


def table_kernel(high_cos_ref, high_sin_ref, low_cos_ref, low_sin_ref, out_ref):
    coarse = low_cos_ref.shape[0]
    lc = low_cos_ref[...]
    ls = low_sin_ref[...]
    for qq in range(TABLE_Q):
        hc = high_cos_ref[qq]
        hs = high_sin_ref[qq]
        first = (pl.program_id(0) * TABLE_Q + qq) * coarse
        sample = (first + lax.broadcasted_iota(jnp.int32, (coarse, 1), 0)).astype(jnp.float32)
        taper = 0.5 - 0.5 * jnp.cos(sample * (two_pi / WIN))
        rows = pl.ds(qq * coarse, coarse)
        out_ref[rows, :NF] = (taper * (hc * lc - hs * ls)).astype(out_ref.dtype)
        out_ref[rows, NF:] = (-(taper * (hs * lc + hc * ls))).astype(out_ref.dtype)


def forward_table():
    coarse = 128
    n_coarse = WIN // coarse
    freq_bins = K0 + jnp.arange(NF, dtype=jnp.int32)
    scale = two_pi / WIN
    high_idx = (jnp.arange(n_coarse, dtype=jnp.int32) * coarse)[:, None] * freq_bins[None, :] % WIN
    low_idx = jnp.arange(coarse, dtype=jnp.int32)[:, None] * freq_bins[None, :] % WIN
    high_angle = high_idx.astype(jnp.float32) * scale
    low_angle = low_idx.astype(jnp.float32) * scale
    high_cos = jnp.cos(high_angle).reshape(n_coarse, 1, NF)
    high_sin = jnp.sin(high_angle).reshape(n_coarse, 1, NF)
    low_cos, low_sin = jnp.cos(low_angle), jnp.sin(low_angle)
    return pl.pallas_call(
        table_kernel,
        grid=(n_coarse // TABLE_Q,),
        in_specs=[
            pl.BlockSpec((TABLE_Q, 1, NF), lambda q: (q, 0, 0)),
            pl.BlockSpec((TABLE_Q, 1, NF), lambda q: (q, 0, 0)),
            pl.BlockSpec((coarse, NF), lambda q: (0, 0)),
            pl.BlockSpec((coarse, NF), lambda q: (0, 0)),
        ],
        out_specs=pl.BlockSpec((TABLE_Q * coarse, 2 * NF), lambda q: (q, 0)),
        out_shape=jax.ShapeDtypeStruct((WIN, 2 * NF), jnp.bfloat16),
    )(high_cos, high_sin, low_cos, low_sin)


def lag_table(count):
    freq_bins = K0 + jnp.arange(NF, dtype=jnp.int32)
    shifted = (jnp.arange(LAGS, dtype=jnp.int32) - LAGS // 2) % WIN
    wrapped = freq_bins[:, None] * shifted[None, :] % WIN
    phase_angle = wrapped.astype(jnp.float32) * (two_pi / WIN)
    factor = 1.0 / math.sqrt(NF * count)
    return jnp.concatenate(
        [jnp.cos(phase_angle) * factor, -jnp.sin(phase_angle) * factor], axis=0
    ).astype(jnp.bfloat16)


def whiten(spectra):
    real_part = spectra[..., :NF]
    imag_part = spectra[..., NF:]
    power_sum = real_part * real_part + imag_part * imag_part
    freq_bins = jnp.arange(NF, dtype=jnp.int32)
    band_matrix = (jnp.abs(freq_bins[:, None] - freq_bins[None, :]) <= SPAN).astype(jnp.float32)
    smooth = jnp.einsum(
        "...f,fg->...g", power_sum, band_matrix, precision=lax.Precision.HIGHEST
    ) / (2 * SPAN + 1)
    water_level = jnp.mean(power_sum, axis=-1, keepdims=True)
    weight = lax.rsqrt(smooth + 0.5 * water_level + 1e-06)
    return (spectra * jnp.concatenate([weight, weight], axis=-1)).astype(jnp.bfloat16)


ROW_TILE = 8
J_CHUNK = 64
F_CHUNK = 128


def pair_kernel(pairs_ref, row_ref, col_ref, lags_ref, out_ref, cross_ref):
    windows = row_ref.shape[1]
    cols = col_ref.shape[2]

    for i in range(row_ref.shape[2]):
        for jc in range(cols // J_CHUNK):
            js = pl.ds(jc * J_CHUNK, J_CHUNK)
            for fc in range(NF // F_CHUNK):
                fr = pl.ds(fc * F_CHUNK, F_CHUNK)
                fi = pl.ds(NF + fc * F_CHUNK, F_CHUNK)
                acc_re = jnp.zeros((J_CHUNK, F_CHUNK), jnp.float32)
                acc_im = jnp.zeros((J_CHUNK, F_CHUNK), jnp.float32)
                for w in range(windows):
                    xr = row_ref[0, w, i : i + 1, fr]
                    xi = row_ref[0, w, i : i + 1, fi]
                    yr = col_ref[0, w, js, fr]
                    yi = col_ref[0, w, js, fi]
                    acc_re = acc_re + xr * yr + xi * yi
                    acc_im = acc_im + xi * yr - xr * yi
                rows = pl.ds(i * cols + jc * J_CHUNK, J_CHUNK)
                cross_ref[rows, fr] = acc_re.astype(jnp.bfloat16)
                cross_ref[rows, fi] = acc_im.astype(jnp.bfloat16)
    result = jnp.dot(cross_ref[...], lags_ref[...], preferred_element_type=jnp.float32)
    out_ref[0] = result.reshape(out_ref.shape[1:]).astype(out_ref.dtype)


def all_pairs(pairs, row_all, col_all, lags):
    n_pairs = pairs.shape[0]
    windows, rows, cols = row_all.shape[1], row_all.shape[2], col_all.shape[2]
    tiles = rows // ROW_TILE
    grid_spec = pltpu.PrefetchScalarGridSpec(
        num_scalar_prefetch=1,
        grid=(n_pairs, tiles),
        in_specs=[
            pl.BlockSpec((1, windows, ROW_TILE, 2 * NF), lambda p, t, pr: (pr[p, 0], 0, t, 0)),
            pl.BlockSpec((1, windows, cols, 2 * NF), lambda p, t, pr: (pr[p, 1], 0, 0, 0)),
            pl.BlockSpec((2 * NF, LAGS), lambda p, t, pr: (0, 0)),
        ],
        out_specs=pl.BlockSpec((1, ROW_TILE, cols, LAGS), lambda p, t, pr: (p, t, 0, 0)),
        scratch_shapes=[pltpu.VMEM((ROW_TILE * cols, 2 * NF), jnp.bfloat16)],
    )
    flops = n_pairs * rows * cols * (2 * NF * windows * 4 + 2 * 2 * NF * LAGS)
    return pl.pallas_call(
        pair_kernel,
        grid_spec=grid_spec,
        out_shape=jax.ShapeDtypeStruct((n_pairs, rows, cols, LAGS), jnp.bfloat16),
        compiler_params=pltpu.CompilerParams(
            dimension_semantics=("arbitrary", "arbitrary"),
            vmem_limit_bytes=48 * 1024 * 1024,
        ),
        cost_estimate=pl.CostEstimate(
            flops=flops,
            transcendentals=0,
            bytes_accessed=n_pairs * (rows + cols) * windows * 2 * NF * 4 + n_pairs * rows * cols * LAGS * 2,
        ),
    )(pairs, row_all, col_all, lags)


def exchange(value, axes, sizes, moves):
    pairs = []
    for source in itertools.product(*[range(s) for s in sizes]):
        target = moves(source)
        if target is None:
            continue
        pairs.append((linear(source, sizes), linear(target, sizes)))
    if not pairs:
        return None
    return lax.ppermute(value, axes, pairs)


def linear(coord, sizes):
    index = 0
    for c, s in zip(coord, sizes):
        index = index * s + c
    return index


def on_device(signal, offsets, pair_list):
    channels_here = signal.shape[0]
    samples_here = signal.shape[1]
    w_dev = samples_here // STEP
    n_tm = lax.axis_size("tm")
    n_prow = lax.axis_size("prow")
    n_pcol = lax.axis_size("pcol")
    tm_index = lax.axis_index("tm")
    prow_index = lax.axis_index("prow")
    pcol_index = lax.axis_index("pcol")
    dft_table = forward_table()
    head_samples = signal[:, :HALO]
    next_head = from_behind(head_samples, "tm", -1)
    extended = jnp.concatenate([signal, next_head], axis=1)

    segments = [
        lax.dynamic_slice_in_dim(extended, window * STEP + offsets[tm_index * w_dev + window], WIN, 1)
        for window in range(w_dev)
    ]
    stacked = jnp.concatenate(segments, axis=0)
    spectra = jnp.dot(stacked, dft_table, preferred_element_type=jnp.float32)
    spectra = spectra.reshape(w_dev, channels_here, 2 * NF)
    whitened = whiten(spectra)
    half_rows = channels_here // n_tm

    row_windows = [lax.dynamic_slice_in_dim(whitened, tm_index * half_rows, half_rows, 1)]
    for e in range(1, n_tm):
        half = (tm_index - e + n_tm) % n_tm
        payload = lax.dynamic_slice_in_dim(whitened, half * half_rows, half_rows, 1)
        row_windows.append(exchange(payload, ("tm",), (n_tm,), lambda s, e=e: ((s[0] - e) % n_tm,)))
    row_own = jnp.concatenate(row_windows, axis=0)
    row_slots = [row_own]
    for d in range(1, n_pcol):
        row_slots.append(exchange(row_own, ("pcol",), (n_pcol,), lambda s, d=d: ((s[0] - d) % n_pcol,)))
    row_all = jnp.stack(row_slots, axis=0)

    col_slots = []
    for d in range(n_prow):
        if d == 0:
            near = whitened
        else:
            near = exchange(whitened, ("prow",), (n_prow,), lambda s, d=d: (s[0] - d,) if s[0] - d >= 0 else None)
        per_tm = [near]
        for e in range(1, n_tm):
            per_tm.append(exchange(near, ("tm",), (n_tm,), lambda s, e=e: ((s[0] - e) % n_tm,)))
        col_slots.append(jnp.concatenate(per_tm, axis=0))
    col_all = jnp.stack(col_slots, axis=0)

    lags = lag_table(n_tm * w_dev)
    local_pairs = pair_list[0, 0]
    row_slot = (local_pairs[:, 0] - pcol_index + n_pcol) % n_pcol
    col_slot = jnp.clip(local_pairs[:, 1] - prow_index, 0, n_prow - 1)
    pairs = jnp.stack([row_slot, col_slot], axis=1).astype(jnp.int32)
    result = all_pairs(pairs, row_all.astype(jnp.float32), col_all.astype(jnp.float32), lags)
    return result.reshape(1, 1, NP, half_rows, channels_here, LAGS)


def solution(mesh):
    placed = (P(("prow", "pcol"), "tm"), P(), P("prow", "pcol", None, None))
    return jax.shard_map(
        on_device,
        mesh=mesh,
        in_specs=placed,
        out_specs=P("prow", "pcol", None, "tm", None, None),
        check_vma=False,
    )
```

```python
import itertools
import math

import jax
import jax.numpy as jnp
from jax import lax
from jax.sharding import PartitionSpec as P
from jax.experimental import pallas as pl
from jax.experimental.pallas import tpu as pltpu

WIN = 7680
NF = 384
K0 = 32
LAGS = 256
SPAN = 4
NP = 4
STEP = 3840
HALO = 4352


two_pi = 2.0 * math.pi


def from_behind(value, axis, steps):
    count = lax.axis_size(axis)
    initial, last = (max(0, -steps), min(count, count - steps))
    return lax.ppermute(value, axis, [(source, source + steps) for source in range(initial, last)])


TABLE_Q = 12


def table_kernel(high_cos_ref, high_sin_ref, low_cos_ref, low_sin_ref, out_ref):
    coarse = low_cos_ref.shape[0]
    lc = low_cos_ref[...]
    ls = low_sin_ref[...]
    for qq in range(TABLE_Q):
        hc = high_cos_ref[qq]
        hs = high_sin_ref[qq]
        first = (pl.program_id(0) * TABLE_Q + qq) * coarse
        sample = (first + lax.broadcasted_iota(jnp.int32, (coarse, 1), 0)).astype(jnp.float32)
        taper = 0.5 - 0.5 * jnp.cos(sample * (two_pi / WIN))
        rows = pl.ds(qq * coarse, coarse)
        out_ref[rows, :NF] = (taper * (hc * lc - hs * ls)).astype(out_ref.dtype)
        out_ref[rows, NF:] = (-(taper * (hs * lc + hc * ls))).astype(out_ref.dtype)


def forward_table():
    coarse = 128
    n_coarse = WIN // coarse
    freq_bins = K0 + jnp.arange(NF, dtype=jnp.int32)
    scale = two_pi / WIN
    high_idx = (jnp.arange(n_coarse, dtype=jnp.int32) * coarse)[:, None] * freq_bins[None, :] % WIN
    low_idx = jnp.arange(coarse, dtype=jnp.int32)[:, None] * freq_bins[None, :] % WIN
    high_angle = high_idx.astype(jnp.float32) * scale
    low_angle = low_idx.astype(jnp.float32) * scale
    high_cos = jnp.cos(high_angle).reshape(n_coarse, 1, NF)
    high_sin = jnp.sin(high_angle).reshape(n_coarse, 1, NF)
    low_cos, low_sin = jnp.cos(low_angle), jnp.sin(low_angle)
    return pl.pallas_call(
        table_kernel,
        grid=(n_coarse // TABLE_Q,),
        in_specs=[
            pl.BlockSpec((TABLE_Q, 1, NF), lambda q: (q, 0, 0)),
            pl.BlockSpec((TABLE_Q, 1, NF), lambda q: (q, 0, 0)),
            pl.BlockSpec((coarse, NF), lambda q: (0, 0)),
            pl.BlockSpec((coarse, NF), lambda q: (0, 0)),
        ],
        out_specs=pl.BlockSpec((TABLE_Q * coarse, 2 * NF), lambda q: (q, 0)),
        out_shape=jax.ShapeDtypeStruct((WIN, 2 * NF), jnp.bfloat16),
    )(high_cos, high_sin, low_cos, low_sin)


def lag_table(count):
    freq_bins = K0 + jnp.arange(NF, dtype=jnp.int32)
    shifted = (jnp.arange(LAGS, dtype=jnp.int32) - LAGS // 2) % WIN
    wrapped = freq_bins[:, None] * shifted[None, :] % WIN
    phase_angle = wrapped.astype(jnp.float32) * (two_pi / WIN)
    factor = 1.0 / math.sqrt(NF * count)
    return jnp.concatenate(
        [jnp.cos(phase_angle) * factor, -jnp.sin(phase_angle) * factor], axis=0
    ).astype(jnp.bfloat16)


def whiten(spectra):
    real_part = spectra[..., :NF]
    imag_part = spectra[..., NF:]
    power_sum = real_part * real_part + imag_part * imag_part
    freq_bins = jnp.arange(NF, dtype=jnp.int32)
    band_matrix = (jnp.abs(freq_bins[:, None] - freq_bins[None, :]) <= SPAN).astype(jnp.float32)
    smooth = jnp.einsum(
        "...f,fg->...g", power_sum, band_matrix, precision=lax.Precision.HIGHEST
    ) / (2 * SPAN + 1)
    water_level = jnp.mean(power_sum, axis=-1, keepdims=True)
    weight = lax.rsqrt(smooth + 0.5 * water_level + 1e-06)
    return (spectra * jnp.concatenate([weight, weight], axis=-1)).astype(jnp.bfloat16)


ROW_TILE = 8
J_CHUNK = 64
F_CHUNK = 128


def cross_tile(row_ref, col_ref, cross_ref):
    windows = row_ref.shape[1]
    cols = col_ref.shape[2]
    for i in range(row_ref.shape[2]):
        for jc in range(cols // J_CHUNK):
            js = pl.ds(jc * J_CHUNK, J_CHUNK)
            for fc in range(NF // F_CHUNK):
                fr = pl.ds(fc * F_CHUNK, F_CHUNK)
                fi = pl.ds(NF + fc * F_CHUNK, F_CHUNK)
                acc_re = jnp.zeros((J_CHUNK, F_CHUNK), jnp.float32)
                acc_im = jnp.zeros((J_CHUNK, F_CHUNK), jnp.float32)
                for w in range(windows):
                    xr = row_ref[0, w, i : i + 1, fr]
                    xi = row_ref[0, w, i : i + 1, fi]
                    yr = col_ref[0, w, js, fr]
                    yi = col_ref[0, w, js, fi]
                    acc_re = acc_re + xr * yr + xi * yi
                    acc_im = acc_im + xi * yr - xr * yi
                rows = pl.ds(i * cols + jc * J_CHUNK, J_CHUNK)
                cross_ref[rows, fr] = acc_re.astype(jnp.bfloat16)
                cross_ref[rows, fi] = acc_im.astype(jnp.bfloat16)


def pair_kernel(pairs_ref, row_ref, col_ref, lags_ref, out_ref, cross_even, cross_odd):
    step = pl.program_id(0)

    def lag_matmul(cross_ref):
        result = jnp.dot(cross_ref[...], lags_ref[...], preferred_element_type=jnp.float32)
        out_ref[0] = result.reshape(out_ref.shape[1:]).astype(out_ref.dtype)

    @pl.when(step % 2 == 0)
    def _():
        lag_matmul(cross_odd)
        cross_tile(row_ref, col_ref, cross_even)

    @pl.when(step % 2 == 1)
    def _():
        lag_matmul(cross_even)
        cross_tile(row_ref, col_ref, cross_odd)


def all_pairs(pairs, row_all, col_all, lags):
    n_pairs = pairs.shape[0]
    windows, rows, cols = row_all.shape[1], row_all.shape[2], col_all.shape[2]
    tiles = rows // ROW_TILE
    last = n_pairs * tiles - 1

    def compute_tile(s):
        return jnp.minimum(s, last)

    def written_tile(s):
        return jnp.maximum(s - 1, 0)

    grid_spec = pltpu.PrefetchScalarGridSpec(
        num_scalar_prefetch=1,
        grid=(n_pairs * tiles + 1,),
        in_specs=[
            pl.BlockSpec(
                (1, windows, ROW_TILE, 2 * NF),
                lambda s, pr: (pr[compute_tile(s) // tiles, 0], 0, compute_tile(s) % tiles, 0),
            ),
            pl.BlockSpec(
                (1, windows, cols, 2 * NF), lambda s, pr: (pr[compute_tile(s) // tiles, 1], 0, 0, 0)
            ),
            pl.BlockSpec((2 * NF, LAGS), lambda s, pr: (0, 0)),
        ],
        out_specs=pl.BlockSpec(
            (1, ROW_TILE, cols, LAGS), lambda s, pr: (written_tile(s) // tiles, written_tile(s) % tiles, 0, 0)
        ),
        scratch_shapes=[
            pltpu.VMEM((ROW_TILE * cols, 2 * NF), jnp.bfloat16),
            pltpu.VMEM((ROW_TILE * cols, 2 * NF), jnp.bfloat16),
        ],
    )
    flops = n_pairs * rows * cols * (2 * NF * windows * 4 + 2 * 2 * NF * LAGS)
    return pl.pallas_call(
        pair_kernel,
        grid_spec=grid_spec,
        out_shape=jax.ShapeDtypeStruct((n_pairs, rows, cols, LAGS), jnp.bfloat16),
        compiler_params=pltpu.CompilerParams(
            dimension_semantics=("arbitrary",),
            vmem_limit_bytes=48 * 1024 * 1024,
        ),
        cost_estimate=pl.CostEstimate(
            flops=flops,
            transcendentals=0,
            bytes_accessed=n_pairs * (rows + cols) * windows * 2 * NF * 4 + n_pairs * rows * cols * LAGS * 2,
        ),
    )(pairs, row_all, col_all, lags)


def exchange(value, axes, sizes, moves):
    pairs = []
    for source in itertools.product(*[range(s) for s in sizes]):
        target = moves(source)
        if target is None:
            continue
        pairs.append((linear(source, sizes), linear(target, sizes)))
    if not pairs:
        return None
    return lax.ppermute(value, axes, pairs)


def linear(coord, sizes):
    index = 0
    for c, s in zip(coord, sizes):
        index = index * s + c
    return index


def on_device(signal, offsets, pair_list):
    channels_here = signal.shape[0]
    samples_here = signal.shape[1]
    w_dev = samples_here // STEP
    n_tm = lax.axis_size("tm")
    n_prow = lax.axis_size("prow")
    n_pcol = lax.axis_size("pcol")
    tm_index = lax.axis_index("tm")
    prow_index = lax.axis_index("prow")
    pcol_index = lax.axis_index("pcol")
    dft_table = forward_table()
    head_samples = signal[:, :HALO]
    next_head = from_behind(head_samples, "tm", -1)
    extended = jnp.concatenate([signal, next_head], axis=1)

    segments = [
        lax.dynamic_slice_in_dim(extended, window * STEP + offsets[tm_index * w_dev + window], WIN, 1)
        for window in range(w_dev)
    ]
    stacked = jnp.concatenate(segments, axis=0)
    spectra = jnp.dot(stacked, dft_table, preferred_element_type=jnp.float32)
    spectra = spectra.reshape(w_dev, channels_here, 2 * NF)
    whitened = whiten(spectra)
    half_rows = channels_here // n_tm

    row_windows = [lax.dynamic_slice_in_dim(whitened, tm_index * half_rows, half_rows, 1)]
    for e in range(1, n_tm):
        half = (tm_index - e + n_tm) % n_tm
        payload = lax.dynamic_slice_in_dim(whitened, half * half_rows, half_rows, 1)
        row_windows.append(exchange(payload, ("tm",), (n_tm,), lambda s, e=e: ((s[0] - e) % n_tm,)))
    row_own = jnp.concatenate(row_windows, axis=0)
    row_slots = [row_own]
    for d in range(1, n_pcol):
        row_slots.append(exchange(row_own, ("pcol",), (n_pcol,), lambda s, d=d: ((s[0] - d) % n_pcol,)))
    row_all = jnp.stack(row_slots, axis=0)

    col_slots = []
    for d in range(n_prow):
        if d == 0:
            near = whitened
        else:
            near = exchange(whitened, ("prow",), (n_prow,), lambda s, d=d: (s[0] - d,) if s[0] - d >= 0 else None)
        per_tm = [near]
        for e in range(1, n_tm):
            per_tm.append(exchange(near, ("tm",), (n_tm,), lambda s, e=e: ((s[0] - e) % n_tm,)))
        col_slots.append(jnp.concatenate(per_tm, axis=0))
    col_all = jnp.stack(col_slots, axis=0)

    lags = lag_table(n_tm * w_dev)
    local_pairs = pair_list[0, 0]
    row_slot = (local_pairs[:, 0] - pcol_index + n_pcol) % n_pcol
    col_slot = jnp.clip(local_pairs[:, 1] - prow_index, 0, n_prow - 1)
    pairs = jnp.stack([row_slot, col_slot], axis=1).astype(jnp.int32)
    result = all_pairs(pairs, row_all.astype(jnp.float32), col_all.astype(jnp.float32), lags)
    return result.reshape(1, 1, NP, half_rows, channels_here, LAGS)


def solution(mesh):
    placed = (P(("prow", "pcol"), "tm"), P(), P("prow", "pcol", None, None))
    return jax.shard_map(
        on_device,
        mesh=mesh,
        in_specs=placed,
        out_specs=P("prow", "pcol", None, "tm", None, None),
        check_vma=False,
    )
```

```python
import itertools
import math

import jax
import jax.numpy as jnp
from jax import lax
from jax.sharding import PartitionSpec as P
from jax.experimental import pallas as pl
from jax.experimental.pallas import tpu as pltpu

WIN = 7680
NF = 384
K0 = 32
LAGS = 256
SPAN = 4
NP = 4
STEP = 3840
HALO = 4352


two_pi = 2.0 * math.pi


def from_behind(value, axis, steps):
    count = lax.axis_size(axis)
    initial, last = (max(0, -steps), min(count, count - steps))
    return lax.ppermute(value, axis, [(source, source + steps) for source in range(initial, last)])


TABLE_Q = 12


def table_kernel(high_cos_ref, high_sin_ref, low_cos_ref, low_sin_ref, out_ref):
    coarse = low_cos_ref.shape[0]
    lc = low_cos_ref[...]
    ls = low_sin_ref[...]
    for qq in range(TABLE_Q):
        hc = high_cos_ref[qq]
        hs = high_sin_ref[qq]
        first = (pl.program_id(0) * TABLE_Q + qq) * coarse
        sample = (first + lax.broadcasted_iota(jnp.int32, (coarse, 1), 0)).astype(jnp.float32)
        taper = 0.5 - 0.5 * jnp.cos(sample * (two_pi / WIN))
        rows = pl.ds(qq * coarse, coarse)
        out_ref[rows, :NF] = (taper * (hc * lc - hs * ls)).astype(out_ref.dtype)
        out_ref[rows, NF:] = (-(taper * (hs * lc + hc * ls))).astype(out_ref.dtype)


def forward_table():
    coarse = 128
    n_coarse = WIN // coarse
    freq_bins = K0 + jnp.arange(NF, dtype=jnp.int32)
    scale = two_pi / WIN
    high_idx = (jnp.arange(n_coarse, dtype=jnp.int32) * coarse)[:, None] * freq_bins[None, :] % WIN
    low_idx = jnp.arange(coarse, dtype=jnp.int32)[:, None] * freq_bins[None, :] % WIN
    high_angle = high_idx.astype(jnp.float32) * scale
    low_angle = low_idx.astype(jnp.float32) * scale
    high_cos = jnp.cos(high_angle).reshape(n_coarse, 1, NF)
    high_sin = jnp.sin(high_angle).reshape(n_coarse, 1, NF)
    low_cos, low_sin = jnp.cos(low_angle), jnp.sin(low_angle)
    return pl.pallas_call(
        table_kernel,
        grid=(n_coarse // TABLE_Q,),
        in_specs=[
            pl.BlockSpec((TABLE_Q, 1, NF), lambda q: (q, 0, 0)),
            pl.BlockSpec((TABLE_Q, 1, NF), lambda q: (q, 0, 0)),
            pl.BlockSpec((coarse, NF), lambda q: (0, 0)),
            pl.BlockSpec((coarse, NF), lambda q: (0, 0)),
        ],
        out_specs=pl.BlockSpec((TABLE_Q * coarse, 2 * NF), lambda q: (q, 0)),
        out_shape=jax.ShapeDtypeStruct((WIN, 2 * NF), jnp.bfloat16),
    )(high_cos, high_sin, low_cos, low_sin)


def lag_table(count):
    freq_bins = K0 + jnp.arange(NF, dtype=jnp.int32)
    shifted = (jnp.arange(LAGS, dtype=jnp.int32) - LAGS // 2) % WIN
    wrapped = freq_bins[:, None] * shifted[None, :] % WIN
    phase_angle = wrapped.astype(jnp.float32) * (two_pi / WIN)
    factor = 1.0 / math.sqrt(NF * count)
    return jnp.concatenate(
        [jnp.cos(phase_angle) * factor, -jnp.sin(phase_angle) * factor], axis=0
    ).astype(jnp.bfloat16)


def whiten(spectra):
    real_part = spectra[..., :NF]
    imag_part = spectra[..., NF:]
    power_sum = real_part * real_part + imag_part * imag_part
    freq_bins = jnp.arange(NF, dtype=jnp.int32)
    band_matrix = (jnp.abs(freq_bins[:, None] - freq_bins[None, :]) <= SPAN).astype(jnp.float32)
    smooth = jnp.einsum(
        "...f,fg->...g", power_sum, band_matrix, precision=lax.Precision.HIGHEST
    ) / (2 * SPAN + 1)
    water_level = jnp.mean(power_sum, axis=-1, keepdims=True)
    weight = lax.rsqrt(smooth + 0.5 * water_level + 1e-06)
    return (spectra * jnp.concatenate([weight, weight], axis=-1)).astype(jnp.bfloat16)


ROW_TILE = 8
J_CHUNK = 64
F_CHUNK = 128


def pair_kernel(pairs_ref, row_ref, col_ref, lags_ref, out_ref, cross_ref):
    windows = row_ref.shape[1]
    cols = col_ref.shape[2]
    for i in range(row_ref.shape[2]):
        for jc in range(cols // J_CHUNK):
            js = pl.ds(jc * J_CHUNK, J_CHUNK)
            for fc in range(NF // F_CHUNK):
                fr = pl.ds(fc * F_CHUNK, F_CHUNK)
                fi = pl.ds(NF + fc * F_CHUNK, F_CHUNK)
                fs = pl.ds(2 * NF + fc * F_CHUNK, F_CHUNK)
                acc_re = jnp.zeros((J_CHUNK, F_CHUNK), jnp.float32)
                acc_im = jnp.zeros((J_CHUNK, F_CHUNK), jnp.float32)
                for w in range(windows):
                    xr = row_ref[0, w, i : i + 1, fr]
                    xi = row_ref[0, w, i : i + 1, fi]
                    xs = row_ref[0, w, i : i + 1, fs]
                    yr = col_ref[0, w, js, fr]
                    yd = col_ref[0, w, js, fi]
                    ys = col_ref[0, w, js, fs]
                    both = yr * xs
                    acc_re = acc_re + (both - xi * yd)
                    acc_im = acc_im + (both - xr * ys)
                rows = pl.ds(i * cols + jc * J_CHUNK, J_CHUNK)
                cross_ref[rows, fr] = acc_re.astype(jnp.bfloat16)
                cross_ref[rows, fi] = acc_im.astype(jnp.bfloat16)
    result = jnp.dot(cross_ref[...], lags_ref[...], preferred_element_type=jnp.float32)
    out_ref[0] = result.reshape(out_ref.shape[1:]).astype(out_ref.dtype)


def with_sums(spectra):
    real_part = spectra[..., :NF].astype(jnp.float32)
    imag_part = spectra[..., NF:].astype(jnp.float32)
    return jnp.concatenate([real_part, imag_part, real_part + imag_part], axis=-1)


def with_differences(spectra):
    real_part = spectra[..., :NF].astype(jnp.float32)
    imag_part = spectra[..., NF:].astype(jnp.float32)
    return jnp.concatenate([real_part, real_part - imag_part, real_part + imag_part], axis=-1)


def all_pairs(pairs, row_all, col_all, lags):
    n_pairs = pairs.shape[0]
    windows, rows, cols = row_all.shape[1], row_all.shape[2], col_all.shape[2]
    tiles = rows // ROW_TILE
    grid_spec = pltpu.PrefetchScalarGridSpec(
        num_scalar_prefetch=1,
        grid=(n_pairs, tiles),
        in_specs=[
            pl.BlockSpec((1, windows, ROW_TILE, 3 * NF), lambda p, t, pr: (pr[p, 0], 0, t, 0)),
            pl.BlockSpec((1, windows, cols, 3 * NF), lambda p, t, pr: (pr[p, 1], 0, 0, 0)),
            pl.BlockSpec((2 * NF, LAGS), lambda p, t, pr: (0, 0)),
        ],
        out_specs=pl.BlockSpec((1, ROW_TILE, cols, LAGS), lambda p, t, pr: (p, t, 0, 0)),
        scratch_shapes=[pltpu.VMEM((ROW_TILE * cols, 2 * NF), jnp.bfloat16)],
    )
    flops = n_pairs * rows * cols * (2 * NF * windows * 4 + 2 * 2 * NF * LAGS)
    return pl.pallas_call(
        pair_kernel,
        grid_spec=grid_spec,
        out_shape=jax.ShapeDtypeStruct((n_pairs, rows, cols, LAGS), jnp.bfloat16),
        compiler_params=pltpu.CompilerParams(
            dimension_semantics=("arbitrary", "arbitrary"),
            vmem_limit_bytes=48 * 1024 * 1024,
        ),
        cost_estimate=pl.CostEstimate(
            flops=flops,
            transcendentals=0,
            bytes_accessed=n_pairs * (rows + cols) * windows * 2 * NF * 4 + n_pairs * rows * cols * LAGS * 2,
        ),
    )(pairs, row_all, col_all, lags)


def exchange(value, axes, sizes, moves):
    pairs = []
    for source in itertools.product(*[range(s) for s in sizes]):
        target = moves(source)
        if target is None:
            continue
        pairs.append((linear(source, sizes), linear(target, sizes)))
    if not pairs:
        return None
    return lax.ppermute(value, axes, pairs)


def linear(coord, sizes):
    index = 0
    for c, s in zip(coord, sizes):
        index = index * s + c
    return index


def on_device(signal, offsets, pair_list):
    channels_here = signal.shape[0]
    samples_here = signal.shape[1]
    w_dev = samples_here // STEP
    n_tm = lax.axis_size("tm")
    n_prow = lax.axis_size("prow")
    n_pcol = lax.axis_size("pcol")
    tm_index = lax.axis_index("tm")
    prow_index = lax.axis_index("prow")
    pcol_index = lax.axis_index("pcol")
    dft_table = forward_table()
    head_samples = signal[:, :HALO]
    next_head = from_behind(head_samples, "tm", -1)
    extended = jnp.concatenate([signal, next_head], axis=1)

    segments = [
        lax.dynamic_slice_in_dim(extended, window * STEP + offsets[tm_index * w_dev + window], WIN, 1)
        for window in range(w_dev)
    ]
    stacked = jnp.concatenate(segments, axis=0)
    spectra = jnp.dot(stacked, dft_table, preferred_element_type=jnp.float32)
    spectra = spectra.reshape(w_dev, channels_here, 2 * NF)
    whitened = whiten(spectra)
    half_rows = channels_here // n_tm

    row_windows = [lax.dynamic_slice_in_dim(whitened, tm_index * half_rows, half_rows, 1)]
    for e in range(1, n_tm):
        half = (tm_index - e + n_tm) % n_tm
        payload = lax.dynamic_slice_in_dim(whitened, half * half_rows, half_rows, 1)
        row_windows.append(exchange(payload, ("tm",), (n_tm,), lambda s, e=e: ((s[0] - e) % n_tm,)))
    row_own = jnp.concatenate(row_windows, axis=0)
    row_slots = [row_own]
    for d in range(1, n_pcol):
        row_slots.append(exchange(row_own, ("pcol",), (n_pcol,), lambda s, d=d: ((s[0] - d) % n_pcol,)))
    row_all = jnp.stack(row_slots, axis=0)

    col_slots = []
    for d in range(n_prow):
        if d == 0:
            near = whitened
        else:
            near = exchange(whitened, ("prow",), (n_prow,), lambda s, d=d: (s[0] - d,) if s[0] - d >= 0 else None)
        per_tm = [near]
        for e in range(1, n_tm):
            per_tm.append(exchange(near, ("tm",), (n_tm,), lambda s, e=e: ((s[0] - e) % n_tm,)))
        col_slots.append(jnp.concatenate(per_tm, axis=0))
    col_all = jnp.stack(col_slots, axis=0)

    lags = lag_table(n_tm * w_dev)
    local_pairs = pair_list[0, 0]
    row_slot = (local_pairs[:, 0] - pcol_index + n_pcol) % n_pcol
    col_slot = jnp.clip(local_pairs[:, 1] - prow_index, 0, n_prow - 1)
    pairs = jnp.stack([row_slot, col_slot], axis=1).astype(jnp.int32)
    result = all_pairs(pairs, with_sums(row_all), with_differences(col_all), lags)
    return result.reshape(1, 1, NP, half_rows, channels_here, LAGS)


def solution(mesh):
    placed = (P(("prow", "pcol"), "tm"), P(), P("prow", "pcol", None, None))
    return jax.shard_map(
        on_device,
        mesh=mesh,
        in_specs=placed,
        out_specs=P("prow", "pcol", None, "tm", None, None),
        check_vma=False,
    )
```

```python
import itertools
import math

import jax
import jax.numpy as jnp
from jax import lax
from jax.sharding import PartitionSpec as P
from jax.experimental import pallas as pl
from jax.experimental.pallas import tpu as pltpu

WIN = 7680
NF = 384
K0 = 32
LAGS = 256
SPAN = 4
NP = 4
STEP = 3840
HALO = 4352


two_pi = 2.0 * math.pi


def from_behind(value, axis, steps):
    count = lax.axis_size(axis)
    initial, last = (max(0, -steps), min(count, count - steps))
    return lax.ppermute(value, axis, [(source, source + steps) for source in range(initial, last)])


TABLE_Q = 12


def table_kernel(high_cos_ref, high_sin_ref, low_cos_ref, low_sin_ref, out_ref):
    coarse = low_cos_ref.shape[0]
    lc = low_cos_ref[...]
    ls = low_sin_ref[...]
    for qq in range(TABLE_Q):
        hc = high_cos_ref[qq]
        hs = high_sin_ref[qq]
        first = (pl.program_id(0) * TABLE_Q + qq) * coarse
        sample = (first + lax.broadcasted_iota(jnp.int32, (coarse, 1), 0)).astype(jnp.float32)
        taper = 0.5 - 0.5 * jnp.cos(sample * (two_pi / WIN))
        rows = pl.ds(qq * coarse, coarse)
        out_ref[rows, :NF] = (taper * (hc * lc - hs * ls)).astype(out_ref.dtype)
        out_ref[rows, NF:] = (-(taper * (hs * lc + hc * ls))).astype(out_ref.dtype)


def forward_table():
    coarse = 128
    n_coarse = WIN // coarse
    freq_bins = K0 + jnp.arange(NF, dtype=jnp.int32)
    scale = two_pi / WIN
    high_idx = (jnp.arange(n_coarse, dtype=jnp.int32) * coarse)[:, None] * freq_bins[None, :] % WIN
    low_idx = jnp.arange(coarse, dtype=jnp.int32)[:, None] * freq_bins[None, :] % WIN
    high_angle = high_idx.astype(jnp.float32) * scale
    low_angle = low_idx.astype(jnp.float32) * scale
    high_cos = jnp.cos(high_angle).reshape(n_coarse, 1, NF)
    high_sin = jnp.sin(high_angle).reshape(n_coarse, 1, NF)
    low_cos, low_sin = jnp.cos(low_angle), jnp.sin(low_angle)
    return pl.pallas_call(
        table_kernel,
        grid=(n_coarse // TABLE_Q,),
        in_specs=[
            pl.BlockSpec((TABLE_Q, 1, NF), lambda q: (q, 0, 0)),
            pl.BlockSpec((TABLE_Q, 1, NF), lambda q: (q, 0, 0)),
            pl.BlockSpec((coarse, NF), lambda q: (0, 0)),
            pl.BlockSpec((coarse, NF), lambda q: (0, 0)),
        ],
        out_specs=pl.BlockSpec((TABLE_Q * coarse, 2 * NF), lambda q: (q, 0)),
        out_shape=jax.ShapeDtypeStruct((WIN, 2 * NF), jnp.bfloat16),
    )(high_cos, high_sin, low_cos, low_sin)


def lag_table(count):
    freq_bins = K0 + jnp.arange(NF, dtype=jnp.int32)
    shifted = (jnp.arange(LAGS, dtype=jnp.int32) - LAGS // 2) % WIN
    wrapped = freq_bins[:, None] * shifted[None, :] % WIN
    phase_angle = wrapped.astype(jnp.float32) * (two_pi / WIN)
    factor = 1.0 / math.sqrt(NF * count)
    return jnp.concatenate(
        [jnp.cos(phase_angle) * factor, -jnp.sin(phase_angle) * factor], axis=0
    ).astype(jnp.bfloat16)


def whiten(spectra):
    real_part = spectra[..., :NF]
    imag_part = spectra[..., NF:]
    power_sum = real_part * real_part + imag_part * imag_part
    freq_bins = jnp.arange(NF, dtype=jnp.int32)
    band_matrix = (jnp.abs(freq_bins[:, None] - freq_bins[None, :]) <= SPAN).astype(jnp.float32)
    smooth = jnp.einsum(
        "...f,fg->...g", power_sum, band_matrix, precision=lax.Precision.HIGHEST
    ) / (2 * SPAN + 1)
    water_level = jnp.mean(power_sum, axis=-1, keepdims=True)
    weight = lax.rsqrt(smooth + 0.5 * water_level + 1e-06)
    return (spectra * jnp.concatenate([weight, weight], axis=-1)).astype(jnp.bfloat16)


ROW_TILE = 8
J_CHUNK = 64
F_CHUNK = 128


def pair_kernel(pairs_ref, row_ref, col_ref, lags_ref, out_ref, cross_ref, row32_ref, col32_ref):
    windows = row_ref.shape[1]
    cols = col_ref.shape[2]

    @pl.when(pl.program_id(1) == 0)
    def _():
        for w in range(windows):
            col_real = col_ref[0, w, :, :NF].astype(jnp.float32)
            col_imag = col_ref[0, w, :, NF:].astype(jnp.float32)
            col32_ref[w, :, :NF] = col_real
            col32_ref[w, :, NF : 2 * NF] = col_real - col_imag
            col32_ref[w, :, 2 * NF :] = col_real + col_imag

    for w in range(windows):
        row_real = row_ref[0, w, :, :NF].astype(jnp.float32)
        row_imag = row_ref[0, w, :, NF:].astype(jnp.float32)
        row32_ref[w, :, :NF] = row_real
        row32_ref[w, :, NF : 2 * NF] = row_imag
        row32_ref[w, :, 2 * NF :] = row_real + row_imag

    for i in range(row_ref.shape[2]):
        for jc in range(cols // J_CHUNK):
            js = pl.ds(jc * J_CHUNK, J_CHUNK)
            for fc in range(NF // F_CHUNK):
                fr = pl.ds(fc * F_CHUNK, F_CHUNK)
                fi = pl.ds(NF + fc * F_CHUNK, F_CHUNK)
                fs = pl.ds(2 * NF + fc * F_CHUNK, F_CHUNK)
                acc_re = jnp.zeros((J_CHUNK, F_CHUNK), jnp.float32)
                acc_im = jnp.zeros((J_CHUNK, F_CHUNK), jnp.float32)
                for w in range(windows):
                    xr = row32_ref[w, i : i + 1, fr]
                    xi = row32_ref[w, i : i + 1, fi]
                    xs = row32_ref[w, i : i + 1, fs]
                    yr = col32_ref[w, js, fr]
                    yd = col32_ref[w, js, fi]
                    ys = col32_ref[w, js, fs]
                    both = yr * xs
                    acc_re = acc_re + (both - xi * yd)
                    acc_im = acc_im + (both - xr * ys)
                rows = pl.ds(i * cols + jc * J_CHUNK, J_CHUNK)
                cross_ref[rows, fr] = acc_re.astype(jnp.bfloat16)
                cross_ref[rows, fi] = acc_im.astype(jnp.bfloat16)
    result = jnp.dot(cross_ref[...], lags_ref[...], preferred_element_type=jnp.float32)
    out_ref[0] = result.reshape(out_ref.shape[1:]).astype(out_ref.dtype)


def all_pairs(pairs, row_all, col_all, lags):
    n_pairs = pairs.shape[0]
    windows, rows, cols = row_all.shape[1], row_all.shape[2], col_all.shape[2]
    tiles = rows // ROW_TILE
    grid_spec = pltpu.PrefetchScalarGridSpec(
        num_scalar_prefetch=1,
        grid=(n_pairs, tiles),
        in_specs=[
            pl.BlockSpec((1, windows, ROW_TILE, 2 * NF), lambda p, t, pr: (pr[p, 0], 0, t, 0)),
            pl.BlockSpec((1, windows, cols, 2 * NF), lambda p, t, pr: (pr[p, 1], 0, 0, 0)),
            pl.BlockSpec((2 * NF, LAGS), lambda p, t, pr: (0, 0)),
        ],
        out_specs=pl.BlockSpec((1, ROW_TILE, cols, LAGS), lambda p, t, pr: (p, t, 0, 0)),
        scratch_shapes=[
            pltpu.VMEM((ROW_TILE * cols, 2 * NF), jnp.bfloat16),
            pltpu.VMEM((windows, ROW_TILE, 3 * NF), jnp.float32),
            pltpu.VMEM((windows, cols, 3 * NF), jnp.float32),
        ],
    )
    flops = n_pairs * rows * cols * (2 * NF * windows * 4 + 2 * 2 * NF * LAGS)
    return pl.pallas_call(
        pair_kernel,
        grid_spec=grid_spec,
        out_shape=jax.ShapeDtypeStruct((n_pairs, rows, cols, LAGS), jnp.bfloat16),
        compiler_params=pltpu.CompilerParams(
            dimension_semantics=("arbitrary", "arbitrary"),
            vmem_limit_bytes=48 * 1024 * 1024,
        ),
        cost_estimate=pl.CostEstimate(
            flops=flops,
            transcendentals=0,
            bytes_accessed=n_pairs * (rows + cols) * windows * 2 * NF * 2 + n_pairs * rows * cols * LAGS * 2,
        ),
    )(pairs, row_all, col_all, lags)


def exchange(value, axes, sizes, moves):
    pairs = []
    for source in itertools.product(*[range(s) for s in sizes]):
        target = moves(source)
        if target is None:
            continue
        pairs.append((linear(source, sizes), linear(target, sizes)))
    if not pairs:
        return None
    return lax.ppermute(value, axes, pairs)


def linear(coord, sizes):
    index = 0
    for c, s in zip(coord, sizes):
        index = index * s + c
    return index


def on_device(signal, offsets, pair_list):
    channels_here = signal.shape[0]
    samples_here = signal.shape[1]
    w_dev = samples_here // STEP
    n_tm = lax.axis_size("tm")
    n_prow = lax.axis_size("prow")
    n_pcol = lax.axis_size("pcol")
    tm_index = lax.axis_index("tm")
    prow_index = lax.axis_index("prow")
    pcol_index = lax.axis_index("pcol")
    dft_table = forward_table()
    head_samples = signal[:, :HALO]
    next_head = from_behind(head_samples, "tm", -1)
    extended = jnp.concatenate([signal, next_head], axis=1)

    segments = [
        lax.dynamic_slice_in_dim(extended, window * STEP + offsets[tm_index * w_dev + window], WIN, 1)
        for window in range(w_dev)
    ]
    stacked = jnp.concatenate(segments, axis=0)
    spectra = jnp.dot(stacked, dft_table, preferred_element_type=jnp.float32)
    spectra = spectra.reshape(w_dev, channels_here, 2 * NF)
    whitened = whiten(spectra)
    half_rows = channels_here // n_tm

    row_windows = [lax.dynamic_slice_in_dim(whitened, tm_index * half_rows, half_rows, 1)]
    for e in range(1, n_tm):
        half = (tm_index - e + n_tm) % n_tm
        payload = lax.dynamic_slice_in_dim(whitened, half * half_rows, half_rows, 1)
        row_windows.append(exchange(payload, ("tm",), (n_tm,), lambda s, e=e: ((s[0] - e) % n_tm,)))
    row_own = jnp.concatenate(row_windows, axis=0)
    row_slots = [row_own]
    for d in range(1, n_pcol):
        row_slots.append(exchange(row_own, ("pcol",), (n_pcol,), lambda s, d=d: ((s[0] - d) % n_pcol,)))
    row_all = jnp.stack(row_slots, axis=0)

    col_slots = []
    for d in range(n_prow):
        if d == 0:
            near = whitened
        else:
            near = exchange(whitened, ("prow",), (n_prow,), lambda s, d=d: (s[0] - d,) if s[0] - d >= 0 else None)
        per_tm = [near]
        for e in range(1, n_tm):
            per_tm.append(exchange(near, ("tm",), (n_tm,), lambda s, e=e: ((s[0] - e) % n_tm,)))
        col_slots.append(jnp.concatenate(per_tm, axis=0))
    col_all = jnp.stack(col_slots, axis=0)

    lags = lag_table(n_tm * w_dev)
    local_pairs = pair_list[0, 0]
    row_slot = (local_pairs[:, 0] - pcol_index + n_pcol) % n_pcol
    col_slot = jnp.clip(local_pairs[:, 1] - prow_index, 0, n_prow - 1)
    pairs = jnp.stack([row_slot, col_slot], axis=1).astype(jnp.int32)
    result = all_pairs(pairs, row_all, col_all, lags)
    return result.reshape(1, 1, NP, half_rows, channels_here, LAGS)


def solution(mesh):
    placed = (P(("prow", "pcol"), "tm"), P(), P("prow", "pcol", None, None))
    return jax.shard_map(
        on_device,
        mesh=mesh,
        in_specs=placed,
        out_specs=P("prow", "pcol", None, "tm", None, None),
        check_vma=False,
    )
```

```python
import itertools
import math

import jax
import jax.numpy as jnp
from jax import lax
from jax.sharding import PartitionSpec as P
from jax.experimental import pallas as pl
from jax.experimental.pallas import tpu as pltpu

WIN = 7680
NF = 384
K0 = 32
LAGS = 256
SPAN = 4
NP = 4
STEP = 3840
HALO = 4352


two_pi = 2.0 * math.pi


def from_behind(value, axis, steps):
    count = lax.axis_size(axis)
    initial, last = (max(0, -steps), min(count, count - steps))
    return lax.ppermute(value, axis, [(source, source + steps) for source in range(initial, last)])


TABLE_Q = 12


def table_kernel(high_cos_ref, high_sin_ref, low_cos_ref, low_sin_ref, out_ref):
    coarse = low_cos_ref.shape[0]
    lc = low_cos_ref[...]
    ls = low_sin_ref[...]
    for qq in range(TABLE_Q):
        hc = high_cos_ref[qq]
        hs = high_sin_ref[qq]
        first = (pl.program_id(0) * TABLE_Q + qq) * coarse
        sample = (first + lax.broadcasted_iota(jnp.int32, (coarse, 1), 0)).astype(jnp.float32)
        taper = 0.5 - 0.5 * jnp.cos(sample * (two_pi / WIN))
        rows = pl.ds(qq * coarse, coarse)
        out_ref[rows, :NF] = (taper * (hc * lc - hs * ls)).astype(out_ref.dtype)
        out_ref[rows, NF:] = (-(taper * (hs * lc + hc * ls))).astype(out_ref.dtype)


def forward_table():
    coarse = 128
    n_coarse = WIN // coarse
    freq_bins = K0 + jnp.arange(NF, dtype=jnp.int32)
    scale = two_pi / WIN
    high_idx = (jnp.arange(n_coarse, dtype=jnp.int32) * coarse)[:, None] * freq_bins[None, :] % WIN
    low_idx = jnp.arange(coarse, dtype=jnp.int32)[:, None] * freq_bins[None, :] % WIN
    high_angle = high_idx.astype(jnp.float32) * scale
    low_angle = low_idx.astype(jnp.float32) * scale
    high_cos = jnp.cos(high_angle).reshape(n_coarse, 1, NF)
    high_sin = jnp.sin(high_angle).reshape(n_coarse, 1, NF)
    low_cos, low_sin = jnp.cos(low_angle), jnp.sin(low_angle)
    return pl.pallas_call(
        table_kernel,
        grid=(n_coarse // TABLE_Q,),
        in_specs=[
            pl.BlockSpec((TABLE_Q, 1, NF), lambda q: (q, 0, 0)),
            pl.BlockSpec((TABLE_Q, 1, NF), lambda q: (q, 0, 0)),
            pl.BlockSpec((coarse, NF), lambda q: (0, 0)),
            pl.BlockSpec((coarse, NF), lambda q: (0, 0)),
        ],
        out_specs=pl.BlockSpec((TABLE_Q * coarse, 2 * NF), lambda q: (q, 0)),
        out_shape=jax.ShapeDtypeStruct((WIN, 2 * NF), jnp.bfloat16),
    )(high_cos, high_sin, low_cos, low_sin)


def lag_table(count):
    freq_bins = K0 + jnp.arange(NF, dtype=jnp.int32)
    shifted = (jnp.arange(LAGS, dtype=jnp.int32) - LAGS // 2) % WIN
    wrapped = freq_bins[:, None] * shifted[None, :] % WIN
    phase_angle = wrapped.astype(jnp.float32) * (two_pi / WIN)
    factor = 1.0 / math.sqrt(NF * count)
    return jnp.concatenate(
        [jnp.cos(phase_angle) * factor, -jnp.sin(phase_angle) * factor], axis=0
    ).astype(jnp.bfloat16)


def whiten(spectra):
    real_part = spectra[..., :NF]
    imag_part = spectra[..., NF:]
    power_sum = real_part * real_part + imag_part * imag_part
    freq_bins = jnp.arange(NF, dtype=jnp.int32)
    band_matrix = (jnp.abs(freq_bins[:, None] - freq_bins[None, :]) <= SPAN).astype(jnp.float32)
    smooth = jnp.einsum(
        "...f,fg->...g", power_sum, band_matrix, precision=lax.Precision.HIGHEST
    ) / (2 * SPAN + 1)
    water_level = jnp.mean(power_sum, axis=-1, keepdims=True)
    weight = lax.rsqrt(smooth + 0.5 * water_level + 1e-06)
    return (spectra * jnp.concatenate([weight, weight], axis=-1)).astype(jnp.bfloat16)


ROW_TILE = 8
J_CHUNK = 64
F_CHUNK = 128


def pair_kernel(pairs_ref, row_ref, col_ref, lags_ref, out_ref, cross_ref, row32_ref, col32_ref):
    windows = row_ref.shape[1]
    cols = col_ref.shape[2]

    @pl.when(pl.program_id(1) == 0)
    def _():
        for w in range(windows):
            col_real = col_ref[0, w, :, :NF].astype(jnp.float32)
            col_imag = col_ref[0, w, :, NF:].astype(jnp.float32)
            col32_ref[w, :, :NF] = col_real
            col32_ref[w, :, NF : 2 * NF] = col_real - col_imag
            col32_ref[w, :, 2 * NF :] = col_real + col_imag

    for w in range(windows):
        row_real = row_ref[0, w, :, :NF].astype(jnp.float32)
        row_imag = row_ref[0, w, :, NF:].astype(jnp.float32)
        row32_ref[w, :, :NF] = row_real
        row32_ref[w, :, NF : 2 * NF] = row_imag
        row32_ref[w, :, 2 * NF :] = row_real + row_imag

    for i in range(row_ref.shape[2]):
        for jc in range(cols // J_CHUNK):
            js = pl.ds(jc * J_CHUNK, J_CHUNK)
            for fc in range(NF // F_CHUNK):
                fr = pl.ds(fc * F_CHUNK, F_CHUNK)
                fi = pl.ds(NF + fc * F_CHUNK, F_CHUNK)
                fs = pl.ds(2 * NF + fc * F_CHUNK, F_CHUNK)
                acc_re = jnp.zeros((J_CHUNK, F_CHUNK), jnp.float32)
                acc_im = jnp.zeros((J_CHUNK, F_CHUNK), jnp.float32)
                for w in range(windows):
                    xr = row32_ref[w, i : i + 1, fr]
                    xi = row32_ref[w, i : i + 1, fi]
                    xs = row32_ref[w, i : i + 1, fs]
                    yr = col32_ref[w, js, fr]
                    yd = col32_ref[w, js, fi]
                    ys = col32_ref[w, js, fs]
                    both = yr * xs
                    acc_re = acc_re + (both - xi * yd)
                    acc_im = acc_im + (both - xr * ys)
                rows = pl.ds(i * cols + jc * J_CHUNK, J_CHUNK)
                cross_ref[rows, fr] = acc_re.astype(jnp.bfloat16)
                cross_ref[rows, fi] = acc_im.astype(jnp.bfloat16)
    result = jnp.dot(cross_ref[...], lags_ref[...], preferred_element_type=jnp.float32)
    out_ref[0] = result.reshape(out_ref.shape[1:]).astype(out_ref.dtype)


def all_pairs(pairs, row_all, col_all, lags):
    n_pairs = pairs.shape[0]
    windows, rows, cols = row_all.shape[1], row_all.shape[2], col_all.shape[2]
    tiles = rows // ROW_TILE
    grid_spec = pltpu.PrefetchScalarGridSpec(
        num_scalar_prefetch=1,
        grid=(n_pairs, tiles),
        in_specs=[
            pl.BlockSpec((1, windows, ROW_TILE, 2 * NF), lambda p, t, pr: (pr[p, 0], 0, t, 0)),
            pl.BlockSpec((1, windows, cols, 2 * NF), lambda p, t, pr: (pr[p, 1], 0, 0, 0)),
            pl.BlockSpec((2 * NF, LAGS), lambda p, t, pr: (0, 0)),
        ],
        out_specs=pl.BlockSpec((1, ROW_TILE, cols, LAGS), lambda p, t, pr: (p, t, 0, 0)),
        scratch_shapes=[
            pltpu.VMEM((ROW_TILE * cols, 2 * NF), jnp.bfloat16),
            pltpu.VMEM((windows, ROW_TILE, 3 * NF), jnp.float32),
            pltpu.VMEM((windows, cols, 3 * NF), jnp.float32),
        ],
    )
    flops = n_pairs * rows * cols * (2 * NF * windows * 4 + 2 * 2 * NF * LAGS)
    return pl.pallas_call(
        pair_kernel,
        grid_spec=grid_spec,
        out_shape=jax.ShapeDtypeStruct((n_pairs, rows, cols, LAGS), jnp.bfloat16),
        compiler_params=pltpu.CompilerParams(
            dimension_semantics=("arbitrary", "arbitrary"),
            vmem_limit_bytes=48 * 1024 * 1024,
        ),
        cost_estimate=pl.CostEstimate(
            flops=flops,
            transcendentals=0,
            bytes_accessed=n_pairs * (rows + cols) * windows * 2 * NF * 2 + n_pairs * rows * cols * LAGS * 2,
        ),
    )(pairs, row_all, col_all, lags)


def exchange(value, axes, sizes, moves):
    pairs = []
    for source in itertools.product(*[range(s) for s in sizes]):
        target = moves(source)
        if target is None:
            continue
        pairs.append((linear(source, sizes), linear(target, sizes)))
    if not pairs:
        return None
    return lax.ppermute(value, axes, pairs)


def linear(coord, sizes):
    index = 0
    for c, s in zip(coord, sizes):
        index = index * s + c
    return index


def on_device(signal, offsets, pair_list):
    channels_here = signal.shape[0]
    samples_here = signal.shape[1]
    w_dev = samples_here // STEP
    n_tm = lax.axis_size("tm")
    n_prow = lax.axis_size("prow")
    n_pcol = lax.axis_size("pcol")
    tm_index = lax.axis_index("tm")
    prow_index = lax.axis_index("prow")
    pcol_index = lax.axis_index("pcol")
    dft_table = forward_table()
    head_samples = signal[:, :HALO]
    next_head = from_behind(head_samples, "tm", -1)
    extended = jnp.concatenate([signal, next_head], axis=1)

    segments = [
        lax.dynamic_slice_in_dim(extended, window * STEP + offsets[tm_index * w_dev + window], WIN, 1)
        for window in range(w_dev)
    ]
    stacked = jnp.concatenate(segments, axis=0)
    spectra = jnp.dot(stacked, dft_table, preferred_element_type=jnp.float32)
    spectra = spectra.reshape(w_dev, channels_here, 2 * NF)
    whitened = whiten(spectra)
    half_rows = channels_here // n_tm

    row_windows = [lax.dynamic_slice_in_dim(whitened, tm_index * half_rows, half_rows, 1)]
    for e in range(1, n_tm):
        half = (tm_index - e + n_tm) % n_tm
        payload = lax.dynamic_slice_in_dim(whitened, half * half_rows, half_rows, 1)
        row_windows.append(exchange(payload, ("tm",), (n_tm,), lambda s, e=e: ((s[0] - e) % n_tm,)))
    row_own = jnp.concatenate(row_windows, axis=0)
    row_slots = [row_own]
    for d in range(1, n_pcol):
        row_slots.append(exchange(row_own, ("pcol",), (n_pcol,), lambda s, d=d: ((s[0] - d) % n_pcol,)))
    row_all = jnp.stack(row_slots, axis=0)

    col_slots = []
    for d in range(n_prow):
        if d == 0:
            near = whitened
        else:
            near = exchange(
                near, ("prow",), (n_prow,), lambda s, d=d: (s[0] - 1,) if 1 <= s[0] <= n_prow - d else None
            )
        per_tm = [near]
        for e in range(1, n_tm):
            per_tm.append(exchange(near, ("tm",), (n_tm,), lambda s, e=e: ((s[0] - e) % n_tm,)))
        col_slots.append(jnp.concatenate(per_tm, axis=0))
    col_all = jnp.stack(col_slots, axis=0)

    lags = lag_table(n_tm * w_dev)
    local_pairs = pair_list[0, 0]
    row_slot = (local_pairs[:, 0] - pcol_index + n_pcol) % n_pcol
    col_slot = jnp.clip(local_pairs[:, 1] - prow_index, 0, n_prow - 1)
    pairs = jnp.stack([row_slot, col_slot], axis=1).astype(jnp.int32)
    result = all_pairs(pairs, row_all, col_all, lags)
    return result.reshape(1, 1, NP, half_rows, channels_here, LAGS)


def solution(mesh):
    placed = (P(("prow", "pcol"), "tm"), P(), P("prow", "pcol", None, None))
    return jax.shard_map(
        on_device,
        mesh=mesh,
        in_specs=placed,
        out_specs=P("prow", "pcol", None, "tm", None, None),
        check_vma=False,
    )
```

```python
import itertools
import math

import jax
import jax.numpy as jnp
from jax import lax
from jax.sharding import PartitionSpec as P
from jax.experimental import pallas as pl
from jax.experimental.pallas import tpu as pltpu

WIN = 7680
NF = 384
K0 = 32
LAGS = 256
SPAN = 4
NP = 4
STEP = 3840
HALO = 4352


two_pi = 2.0 * math.pi


def from_behind(value, axis, steps):
    count = lax.axis_size(axis)
    initial, last = (max(0, -steps), min(count, count - steps))
    return lax.ppermute(value, axis, [(source, source + steps) for source in range(initial, last)])


TABLE_Q = 12


def table_kernel(high_cos_ref, high_sin_ref, low_cos_ref, low_sin_ref, taper_ref, out_ref):
    coarse = low_cos_ref.shape[0]
    for qq in range(TABLE_Q):
        rows = pl.ds(qq * coarse, coarse)
        taper = taper_ref[rows, :]
        for fc in range(NF // F_CHUNK):
            lanes = pl.ds(fc * F_CHUNK, F_CHUNK)
            hc = high_cos_ref[qq, :, lanes]
            hs = high_sin_ref[qq, :, lanes]
            lc = low_cos_ref[:, lanes]
            ls = low_sin_ref[:, lanes]
            out_ref[rows, lanes] = (taper * (hc * lc - hs * ls)).astype(out_ref.dtype)
            out_ref[rows, pl.ds(NF + fc * F_CHUNK, F_CHUNK)] = (-(taper * (hs * lc + hc * ls))).astype(out_ref.dtype)


def forward_table():
    coarse = 128
    n_coarse = WIN // coarse
    freq_bins = K0 + jnp.arange(NF, dtype=jnp.int32)
    scale = two_pi / WIN
    high_idx = (jnp.arange(n_coarse, dtype=jnp.int32) * coarse)[:, None] * freq_bins[None, :] % WIN
    low_idx = jnp.arange(coarse, dtype=jnp.int32)[:, None] * freq_bins[None, :] % WIN
    high_angle = high_idx.astype(jnp.float32) * scale
    low_angle = low_idx.astype(jnp.float32) * scale
    high_cos = jnp.cos(high_angle).reshape(n_coarse, 1, NF)
    high_sin = jnp.sin(high_angle).reshape(n_coarse, 1, NF)
    low_cos, low_sin = jnp.cos(low_angle), jnp.sin(low_angle)
    sample_idx = jnp.arange(WIN, dtype=jnp.int32)
    taper_curve = 0.5 - 0.5 * jnp.cos(sample_idx.astype(jnp.float32) * (two_pi / WIN))
    taper_lanes = jnp.broadcast_to(taper_curve[:, None], (WIN, F_CHUNK))
    return pl.pallas_call(
        table_kernel,
        grid=(n_coarse // TABLE_Q,),
        in_specs=[
            pl.BlockSpec((TABLE_Q, 1, NF), lambda q: (q, 0, 0)),
            pl.BlockSpec((TABLE_Q, 1, NF), lambda q: (q, 0, 0)),
            pl.BlockSpec((coarse, NF), lambda q: (0, 0)),
            pl.BlockSpec((coarse, NF), lambda q: (0, 0)),
            pl.BlockSpec((TABLE_Q * coarse, F_CHUNK), lambda q: (q, 0)),
        ],
        out_specs=pl.BlockSpec((TABLE_Q * coarse, 2 * NF), lambda q: (q, 0)),
        out_shape=jax.ShapeDtypeStruct((WIN, 2 * NF), jnp.bfloat16),
    )(high_cos, high_sin, low_cos, low_sin, taper_lanes)


def lag_table(count):
    freq_bins = K0 + jnp.arange(NF, dtype=jnp.int32)
    shifted = (jnp.arange(LAGS, dtype=jnp.int32) - LAGS // 2) % WIN
    wrapped = freq_bins[:, None] * shifted[None, :] % WIN
    phase_angle = wrapped.astype(jnp.float32) * (two_pi / WIN)
    factor = 1.0 / math.sqrt(NF * count)
    return jnp.concatenate(
        [jnp.cos(phase_angle) * factor, -jnp.sin(phase_angle) * factor], axis=0
    ).astype(jnp.bfloat16)


def whiten(spectra):
    real_part = spectra[..., :NF]
    imag_part = spectra[..., NF:]
    power_sum = real_part * real_part + imag_part * imag_part
    freq_bins = jnp.arange(NF, dtype=jnp.int32)
    band_matrix = (jnp.abs(freq_bins[:, None] - freq_bins[None, :]) <= SPAN).astype(jnp.float32)
    smooth = jnp.einsum(
        "...f,fg->...g", power_sum, band_matrix, precision=lax.Precision.HIGHEST
    ) / (2 * SPAN + 1)
    water_level = jnp.mean(power_sum, axis=-1, keepdims=True)
    weight = lax.rsqrt(smooth + 0.5 * water_level + 1e-06)
    return (spectra * jnp.concatenate([weight, weight], axis=-1)).astype(jnp.bfloat16)


ROW_TILE = 8
J_CHUNK = 64
F_CHUNK = 128


def pair_kernel(pairs_ref, row_ref, col_ref, lags_ref, out_ref, cross_ref, row32_ref, col32_ref):
    windows = row_ref.shape[1]
    cols = col_ref.shape[2]

    @pl.when(pl.program_id(1) == 0)
    def _():
        for w in range(windows):
            col_real = col_ref[0, w, :, :NF].astype(jnp.float32)
            col_imag = col_ref[0, w, :, NF:].astype(jnp.float32)
            col32_ref[w, :, :NF] = col_real
            col32_ref[w, :, NF : 2 * NF] = col_real - col_imag
            col32_ref[w, :, 2 * NF :] = col_real + col_imag

    for w in range(windows):
        row_real = row_ref[0, w, :, :NF].astype(jnp.float32)
        row_imag = row_ref[0, w, :, NF:].astype(jnp.float32)
        row32_ref[w, :, :NF] = row_real
        row32_ref[w, :, NF : 2 * NF] = row_imag
        row32_ref[w, :, 2 * NF :] = row_real + row_imag

    for i in range(row_ref.shape[2]):
        for jc in range(cols // J_CHUNK):
            js = pl.ds(jc * J_CHUNK, J_CHUNK)
            for fc in range(NF // F_CHUNK):
                fr = pl.ds(fc * F_CHUNK, F_CHUNK)
                fi = pl.ds(NF + fc * F_CHUNK, F_CHUNK)
                fs = pl.ds(2 * NF + fc * F_CHUNK, F_CHUNK)
                acc_re = jnp.zeros((J_CHUNK, F_CHUNK), jnp.float32)
                acc_im = jnp.zeros((J_CHUNK, F_CHUNK), jnp.float32)
                for w in range(windows):
                    xr = row32_ref[w, i : i + 1, fr]
                    xi = row32_ref[w, i : i + 1, fi]
                    xs = row32_ref[w, i : i + 1, fs]
                    yr = col32_ref[w, js, fr]
                    yd = col32_ref[w, js, fi]
                    ys = col32_ref[w, js, fs]
                    both = yr * xs
                    acc_re = acc_re + (both - xi * yd)
                    acc_im = acc_im + (both - xr * ys)
                rows = pl.ds(i * cols + jc * J_CHUNK, J_CHUNK)
                cross_ref[rows, fr] = acc_re.astype(jnp.bfloat16)
                cross_ref[rows, fi] = acc_im.astype(jnp.bfloat16)
    result = jnp.dot(cross_ref[...], lags_ref[...], preferred_element_type=jnp.float32)
    out_ref[0] = result.reshape(out_ref.shape[1:]).astype(out_ref.dtype)


def all_pairs(pairs, row_all, col_all, lags):
    n_pairs = pairs.shape[0]
    windows, rows, cols = row_all.shape[1], row_all.shape[2], col_all.shape[2]
    tiles = rows // ROW_TILE
    grid_spec = pltpu.PrefetchScalarGridSpec(
        num_scalar_prefetch=1,
        grid=(n_pairs, tiles),
        in_specs=[
            pl.BlockSpec((1, windows, ROW_TILE, 2 * NF), lambda p, t, pr: (pr[p, 0], 0, t, 0)),
            pl.BlockSpec((1, windows, cols, 2 * NF), lambda p, t, pr: (pr[p, 1], 0, 0, 0)),
            pl.BlockSpec((2 * NF, LAGS), lambda p, t, pr: (0, 0)),
        ],
        out_specs=pl.BlockSpec((1, ROW_TILE, cols, LAGS), lambda p, t, pr: (p, t, 0, 0)),
        scratch_shapes=[
            pltpu.VMEM((ROW_TILE * cols, 2 * NF), jnp.bfloat16),
            pltpu.VMEM((windows, ROW_TILE, 3 * NF), jnp.float32),
            pltpu.VMEM((windows, cols, 3 * NF), jnp.float32),
        ],
    )
    flops = n_pairs * rows * cols * (2 * NF * windows * 4 + 2 * 2 * NF * LAGS)
    return pl.pallas_call(
        pair_kernel,
        grid_spec=grid_spec,
        out_shape=jax.ShapeDtypeStruct((n_pairs, rows, cols, LAGS), jnp.bfloat16),
        compiler_params=pltpu.CompilerParams(
            dimension_semantics=("arbitrary", "arbitrary"),
            vmem_limit_bytes=48 * 1024 * 1024,
        ),
        cost_estimate=pl.CostEstimate(
            flops=flops,
            transcendentals=0,
            bytes_accessed=n_pairs * (rows + cols) * windows * 2 * NF * 2 + n_pairs * rows * cols * LAGS * 2,
        ),
    )(pairs, row_all, col_all, lags)


def exchange(value, axes, sizes, moves):
    pairs = []
    for source in itertools.product(*[range(s) for s in sizes]):
        target = moves(source)
        if target is None:
            continue
        pairs.append((linear(source, sizes), linear(target, sizes)))
    if not pairs:
        return None
    return lax.ppermute(value, axes, pairs)


def linear(coord, sizes):
    index = 0
    for c, s in zip(coord, sizes):
        index = index * s + c
    return index


def on_device(signal, offsets, pair_list):
    channels_here = signal.shape[0]
    samples_here = signal.shape[1]
    w_dev = samples_here // STEP
    n_tm = lax.axis_size("tm")
    n_prow = lax.axis_size("prow")
    n_pcol = lax.axis_size("pcol")
    tm_index = lax.axis_index("tm")
    prow_index = lax.axis_index("prow")
    pcol_index = lax.axis_index("pcol")
    dft_table = forward_table()
    head_samples = signal[:, :HALO]
    next_head = from_behind(head_samples, "tm", -1)
    extended = jnp.concatenate([signal, next_head], axis=1)

    segments = [
        lax.dynamic_slice_in_dim(extended, window * STEP + offsets[tm_index * w_dev + window], WIN, 1)
        for window in range(w_dev)
    ]
    stacked = jnp.concatenate(segments, axis=0)
    spectra = jnp.dot(stacked, dft_table, preferred_element_type=jnp.float32)
    spectra = spectra.reshape(w_dev, channels_here, 2 * NF)
    whitened = whiten(spectra)
    half_rows = channels_here // n_tm

    row_windows = [lax.dynamic_slice_in_dim(whitened, tm_index * half_rows, half_rows, 1)]
    for e in range(1, n_tm):
        half = (tm_index - e + n_tm) % n_tm
        payload = lax.dynamic_slice_in_dim(whitened, half * half_rows, half_rows, 1)
        row_windows.append(exchange(payload, ("tm",), (n_tm,), lambda s, e=e: ((s[0] - e) % n_tm,)))
    row_own = jnp.concatenate(row_windows, axis=0)
    row_slots = [row_own]
    for d in range(1, n_pcol):
        row_slots.append(exchange(row_own, ("pcol",), (n_pcol,), lambda s, d=d: ((s[0] - d) % n_pcol,)))
    row_all = jnp.stack(row_slots, axis=0)

    col_slots = []
    for d in range(n_prow):
        if d == 0:
            near = whitened
        else:
            near = exchange(
                near, ("prow",), (n_prow,), lambda s, d=d: (s[0] - 1,) if 1 <= s[0] <= n_prow - d else None
            )
        per_tm = [near]
        for e in range(1, n_tm):
            per_tm.append(exchange(near, ("tm",), (n_tm,), lambda s, e=e: ((s[0] - e) % n_tm,)))
        col_slots.append(jnp.concatenate(per_tm, axis=0))
    col_all = jnp.stack(col_slots, axis=0)

    lags = lag_table(n_tm * w_dev)
    local_pairs = pair_list[0, 0]
    row_slot = (local_pairs[:, 0] - pcol_index + n_pcol) % n_pcol
    col_slot = jnp.clip(local_pairs[:, 1] - prow_index, 0, n_prow - 1)
    pairs = jnp.stack([row_slot, col_slot], axis=1).astype(jnp.int32)
    result = all_pairs(pairs, row_all, col_all, lags)
    return result.reshape(1, 1, NP, half_rows, channels_here, LAGS)


def solution(mesh):
    placed = (P(("prow", "pcol"), "tm"), P(), P("prow", "pcol", None, None))
    return jax.shard_map(
        on_device,
        mesh=mesh,
        in_specs=placed,
        out_specs=P("prow", "pcol", None, "tm", None, None),
        check_vma=False,
    )
```

```python
import itertools
import math

import jax
import jax.numpy as jnp
from jax import lax
from jax.sharding import PartitionSpec as P
from jax.experimental import pallas as pl
from jax.experimental.pallas import tpu as pltpu

WIN = 7680
NF = 384
K0 = 32
LAGS = 256
SPAN = 4
NP = 4
STEP = 3840
HALO = 4352


two_pi = 2.0 * math.pi


def from_behind(value, axis, steps):
    count = lax.axis_size(axis)
    initial, last = (max(0, -steps), min(count, count - steps))
    return lax.ppermute(value, axis, [(source, source + steps) for source in range(initial, last)])


TABLE_Q = 12


def table_kernel(high_cos_ref, high_sin_ref, low_cos_ref, low_sin_ref, taper_ref, out_ref):
    coarse = low_cos_ref.shape[0]
    for qq in range(TABLE_Q):
        rows = pl.ds(qq * coarse, coarse)
        taper = taper_ref[rows, :]
        for fc in range(NF // F_CHUNK):
            lanes = pl.ds(fc * F_CHUNK, F_CHUNK)
            hc = high_cos_ref[qq, :, lanes]
            hs = high_sin_ref[qq, :, lanes]
            lc = low_cos_ref[:, lanes]
            ls = low_sin_ref[:, lanes]
            out_ref[rows, lanes] = (taper * (hc * lc - hs * ls)).astype(out_ref.dtype)
            out_ref[rows, pl.ds(NF + fc * F_CHUNK, F_CHUNK)] = (-(taper * (hs * lc + hc * ls))).astype(out_ref.dtype)


def forward_table():
    coarse = 128
    n_coarse = WIN // coarse
    freq_bins = K0 + jnp.arange(NF, dtype=jnp.int32)
    scale = two_pi / WIN
    high_idx = (jnp.arange(n_coarse, dtype=jnp.int32) * coarse)[:, None] * freq_bins[None, :] % WIN
    low_idx = jnp.arange(coarse, dtype=jnp.int32)[:, None] * freq_bins[None, :] % WIN
    high_angle = high_idx.astype(jnp.float32) * scale
    low_angle = low_idx.astype(jnp.float32) * scale
    high_cos = jnp.cos(high_angle).reshape(n_coarse, 1, NF)
    high_sin = jnp.sin(high_angle).reshape(n_coarse, 1, NF)
    low_cos, low_sin = jnp.cos(low_angle), jnp.sin(low_angle)
    sample_idx = jnp.arange(WIN, dtype=jnp.int32)
    taper_curve = 0.5 - 0.5 * jnp.cos(sample_idx.astype(jnp.float32) * (two_pi / WIN))
    taper_lanes = jnp.broadcast_to(taper_curve[:, None], (WIN, F_CHUNK))
    return pl.pallas_call(
        table_kernel,
        grid=(n_coarse // TABLE_Q,),
        in_specs=[
            pl.BlockSpec((TABLE_Q, 1, NF), lambda q: (q, 0, 0)),
            pl.BlockSpec((TABLE_Q, 1, NF), lambda q: (q, 0, 0)),
            pl.BlockSpec((coarse, NF), lambda q: (0, 0)),
            pl.BlockSpec((coarse, NF), lambda q: (0, 0)),
            pl.BlockSpec((TABLE_Q * coarse, F_CHUNK), lambda q: (q, 0)),
        ],
        out_specs=pl.BlockSpec((TABLE_Q * coarse, 2 * NF), lambda q: (q, 0)),
        out_shape=jax.ShapeDtypeStruct((WIN, 2 * NF), jnp.bfloat16),
    )(high_cos, high_sin, low_cos, low_sin, taper_lanes)


def lag_table(count):
    freq_bins = K0 + jnp.arange(NF, dtype=jnp.int32)
    shifted = (jnp.arange(LAGS, dtype=jnp.int32) - LAGS // 2) % WIN
    wrapped = freq_bins[:, None] * shifted[None, :] % WIN
    phase_angle = wrapped.astype(jnp.float32) * (two_pi / WIN)
    factor = 1.0 / math.sqrt(NF * count)
    return jnp.concatenate(
        [jnp.cos(phase_angle) * factor, -jnp.sin(phase_angle) * factor], axis=0
    ).astype(jnp.bfloat16)


def whiten(spectra):
    real_part = spectra[..., :NF]
    imag_part = spectra[..., NF:]
    power_sum = real_part * real_part + imag_part * imag_part
    freq_bins = jnp.arange(NF, dtype=jnp.int32)
    band_matrix = (jnp.abs(freq_bins[:, None] - freq_bins[None, :]) <= SPAN).astype(jnp.float32)
    smooth = jnp.einsum(
        "...f,fg->...g", power_sum, band_matrix, precision=lax.Precision.HIGHEST
    ) / (2 * SPAN + 1)
    water_level = jnp.mean(power_sum, axis=-1, keepdims=True)
    weight = lax.rsqrt(smooth + 0.5 * water_level + 1e-06)
    return (spectra * jnp.concatenate([weight, weight], axis=-1)).astype(jnp.bfloat16)


ROW_TILE = 16
J_CHUNK = 64
F_CHUNK = 128


def pair_kernel(pairs_ref, row_ref, col_ref, lags_ref, out_ref, cross_ref, row32_ref, col32_ref):
    windows = row_ref.shape[1]
    cols = col_ref.shape[2]

    @pl.when(pl.program_id(1) == 0)
    def _():
        for w in range(windows):
            col_real = col_ref[0, w, :, :NF].astype(jnp.float32)
            col_imag = col_ref[0, w, :, NF:].astype(jnp.float32)
            col32_ref[w, :, :NF] = col_real
            col32_ref[w, :, NF : 2 * NF] = col_real - col_imag
            col32_ref[w, :, 2 * NF :] = col_real + col_imag

    for w in range(windows):
        row_real = row_ref[0, w, :, :NF].astype(jnp.float32)
        row_imag = row_ref[0, w, :, NF:].astype(jnp.float32)
        row32_ref[w, :, :NF] = row_real
        row32_ref[w, :, NF : 2 * NF] = row_imag
        row32_ref[w, :, 2 * NF :] = row_real + row_imag

    for i in range(row_ref.shape[2]):
        for jc in range(cols // J_CHUNK):
            js = pl.ds(jc * J_CHUNK, J_CHUNK)
            for fc in range(NF // F_CHUNK):
                fr = pl.ds(fc * F_CHUNK, F_CHUNK)
                fi = pl.ds(NF + fc * F_CHUNK, F_CHUNK)
                fs = pl.ds(2 * NF + fc * F_CHUNK, F_CHUNK)
                acc_re = jnp.zeros((J_CHUNK, F_CHUNK), jnp.float32)
                acc_im = jnp.zeros((J_CHUNK, F_CHUNK), jnp.float32)
                for w in range(windows):
                    xr = row32_ref[w, i : i + 1, fr]
                    xi = row32_ref[w, i : i + 1, fi]
                    xs = row32_ref[w, i : i + 1, fs]
                    yr = col32_ref[w, js, fr]
                    yd = col32_ref[w, js, fi]
                    ys = col32_ref[w, js, fs]
                    both = yr * xs
                    acc_re = acc_re + (both - xi * yd)
                    acc_im = acc_im + (both - xr * ys)
                rows = pl.ds(i * cols + jc * J_CHUNK, J_CHUNK)
                cross_ref[rows, fr] = acc_re.astype(jnp.bfloat16)
                cross_ref[rows, fi] = acc_im.astype(jnp.bfloat16)
    result = jnp.dot(cross_ref[...], lags_ref[...], preferred_element_type=jnp.float32)
    out_ref[0] = result.reshape(out_ref.shape[1:]).astype(out_ref.dtype)


def all_pairs(pairs, row_all, col_all, lags):
    n_pairs = pairs.shape[0]
    windows, rows, cols = row_all.shape[1], row_all.shape[2], col_all.shape[2]
    tiles = rows // ROW_TILE
    grid_spec = pltpu.PrefetchScalarGridSpec(
        num_scalar_prefetch=1,
        grid=(n_pairs, tiles),
        in_specs=[
            pl.BlockSpec((1, windows, ROW_TILE, 2 * NF), lambda p, t, pr: (pr[p, 0], 0, t, 0)),
            pl.BlockSpec((1, windows, cols, 2 * NF), lambda p, t, pr: (pr[p, 1], 0, 0, 0)),
            pl.BlockSpec((2 * NF, LAGS), lambda p, t, pr: (0, 0)),
        ],
        out_specs=pl.BlockSpec((1, ROW_TILE, cols, LAGS), lambda p, t, pr: (p, t, 0, 0)),
        scratch_shapes=[
            pltpu.VMEM((ROW_TILE * cols, 2 * NF), jnp.bfloat16),
            pltpu.VMEM((windows, ROW_TILE, 3 * NF), jnp.float32),
            pltpu.VMEM((windows, cols, 3 * NF), jnp.float32),
        ],
    )
    flops = n_pairs * rows * cols * (2 * NF * windows * 4 + 2 * 2 * NF * LAGS)
    return pl.pallas_call(
        pair_kernel,
        grid_spec=grid_spec,
        out_shape=jax.ShapeDtypeStruct((n_pairs, rows, cols, LAGS), jnp.bfloat16),
        compiler_params=pltpu.CompilerParams(
            dimension_semantics=("arbitrary", "arbitrary"),
            vmem_limit_bytes=48 * 1024 * 1024,
        ),
        cost_estimate=pl.CostEstimate(
            flops=flops,
            transcendentals=0,
            bytes_accessed=n_pairs * (rows + cols) * windows * 2 * NF * 2 + n_pairs * rows * cols * LAGS * 2,
        ),
    )(pairs, row_all, col_all, lags)


def exchange(value, axes, sizes, moves):
    pairs = []
    for source in itertools.product(*[range(s) for s in sizes]):
        target = moves(source)
        if target is None:
            continue
        pairs.append((linear(source, sizes), linear(target, sizes)))
    if not pairs:
        return None
    return lax.ppermute(value, axes, pairs)


def linear(coord, sizes):
    index = 0
    for c, s in zip(coord, sizes):
        index = index * s + c
    return index


def on_device(signal, offsets, pair_list):
    channels_here = signal.shape[0]
    samples_here = signal.shape[1]
    w_dev = samples_here // STEP
    n_tm = lax.axis_size("tm")
    n_prow = lax.axis_size("prow")
    n_pcol = lax.axis_size("pcol")
    tm_index = lax.axis_index("tm")
    prow_index = lax.axis_index("prow")
    pcol_index = lax.axis_index("pcol")
    dft_table = forward_table()
    head_samples = signal[:, :HALO]
    next_head = from_behind(head_samples, "tm", -1)
    extended = jnp.concatenate([signal, next_head], axis=1)

    segments = [
        lax.dynamic_slice_in_dim(extended, window * STEP + offsets[tm_index * w_dev + window], WIN, 1)
        for window in range(w_dev)
    ]
    stacked = jnp.concatenate(segments, axis=0)
    spectra = jnp.dot(stacked, dft_table, preferred_element_type=jnp.float32)
    spectra = spectra.reshape(w_dev, channels_here, 2 * NF)
    whitened = whiten(spectra)
    half_rows = channels_here // n_tm

    row_windows = [lax.dynamic_slice_in_dim(whitened, tm_index * half_rows, half_rows, 1)]
    for e in range(1, n_tm):
        half = (tm_index - e + n_tm) % n_tm
        payload = lax.dynamic_slice_in_dim(whitened, half * half_rows, half_rows, 1)
        row_windows.append(exchange(payload, ("tm",), (n_tm,), lambda s, e=e: ((s[0] - e) % n_tm,)))
    row_own = jnp.concatenate(row_windows, axis=0)
    row_slots = [row_own]
    for d in range(1, n_pcol):
        row_slots.append(exchange(row_own, ("pcol",), (n_pcol,), lambda s, d=d: ((s[0] - d) % n_pcol,)))
    row_all = jnp.stack(row_slots, axis=0)

    col_slots = []
    for d in range(n_prow):
        if d == 0:
            near = whitened
        else:
            near = exchange(
                near, ("prow",), (n_prow,), lambda s, d=d: (s[0] - 1,) if 1 <= s[0] <= n_prow - d else None
            )
        per_tm = [near]
        for e in range(1, n_tm):
            per_tm.append(exchange(near, ("tm",), (n_tm,), lambda s, e=e: ((s[0] - e) % n_tm,)))
        col_slots.append(jnp.concatenate(per_tm, axis=0))
    col_all = jnp.stack(col_slots, axis=0)

    lags = lag_table(n_tm * w_dev)
    local_pairs = pair_list[0, 0]
    row_slot = (local_pairs[:, 0] - pcol_index + n_pcol) % n_pcol
    col_slot = jnp.clip(local_pairs[:, 1] - prow_index, 0, n_prow - 1)
    pairs = jnp.stack([row_slot, col_slot], axis=1).astype(jnp.int32)
    result = all_pairs(pairs, row_all, col_all, lags)
    return result.reshape(1, 1, NP, half_rows, channels_here, LAGS)


def solution(mesh):
    placed = (P(("prow", "pcol"), "tm"), P(), P("prow", "pcol", None, None))
    return jax.shard_map(
        on_device,
        mesh=mesh,
        in_specs=placed,
        out_specs=P("prow", "pcol", None, "tm", None, None),
        check_vma=False,
    )
```

```python
import itertools
import math

import jax
import jax.numpy as jnp
from jax import lax
from jax.sharding import PartitionSpec as P
from jax.experimental import pallas as pl
from jax.experimental.pallas import tpu as pltpu

WIN = 7680
NF = 384
K0 = 32
LAGS = 256
SPAN = 4
NP = 4
STEP = 3840
HALO = 4352


two_pi = 2.0 * math.pi


def from_behind(value, axis, steps):
    count = lax.axis_size(axis)
    initial, last = (max(0, -steps), min(count, count - steps))
    return lax.ppermute(value, axis, [(source, source + steps) for source in range(initial, last)])


TABLE_Q = 12


def table_kernel(high_cos_ref, high_sin_ref, low_cos_ref, low_sin_ref, start_cos_ref, start_sin_ref,
                 step_cos_ref, step_sin_ref, out_ref):
    coarse = low_cos_ref.shape[0]
    step_cos = step_cos_ref[...]
    step_sin = step_sin_ref[...]
    for qq in range(TABLE_Q):
        rows = pl.ds(qq * coarse, coarse)
        taper = 0.5 - 0.5 * (start_cos_ref[qq] * step_cos - start_sin_ref[qq] * step_sin)
        for fc in range(NF // F_CHUNK):
            lanes = pl.ds(fc * F_CHUNK, F_CHUNK)
            hc = high_cos_ref[qq, :, lanes]
            hs = high_sin_ref[qq, :, lanes]
            lc = low_cos_ref[:, lanes]
            ls = low_sin_ref[:, lanes]
            out_ref[rows, lanes] = (taper * (hc * lc - hs * ls)).astype(out_ref.dtype)
            out_ref[rows, pl.ds(NF + fc * F_CHUNK, F_CHUNK)] = (-(taper * (hs * lc + hc * ls))).astype(out_ref.dtype)


def forward_table():
    coarse = 128
    n_coarse = WIN // coarse
    freq_bins = K0 + jnp.arange(NF, dtype=jnp.int32)
    scale = two_pi / WIN
    high_idx = (jnp.arange(n_coarse, dtype=jnp.int32) * coarse)[:, None] * freq_bins[None, :] % WIN
    low_idx = jnp.arange(coarse, dtype=jnp.int32)[:, None] * freq_bins[None, :] % WIN
    high_angle = high_idx.astype(jnp.float32) * scale
    low_angle = low_idx.astype(jnp.float32) * scale
    high_cos = jnp.cos(high_angle).reshape(n_coarse, 1, NF)
    high_sin = jnp.sin(high_angle).reshape(n_coarse, 1, NF)
    low_cos, low_sin = jnp.cos(low_angle), jnp.sin(low_angle)
    start_angle = (jnp.arange(n_coarse, dtype=jnp.int32) * coarse).astype(jnp.float32) * scale
    step_angle = jnp.arange(coarse, dtype=jnp.int32).astype(jnp.float32) * scale
    start_cos = jnp.broadcast_to(jnp.cos(start_angle)[:, None, None], (n_coarse, 1, F_CHUNK))
    start_sin = jnp.broadcast_to(jnp.sin(start_angle)[:, None, None], (n_coarse, 1, F_CHUNK))
    step_cos = jnp.broadcast_to(jnp.cos(step_angle)[:, None], (coarse, F_CHUNK))
    step_sin = jnp.broadcast_to(jnp.sin(step_angle)[:, None], (coarse, F_CHUNK))
    return pl.pallas_call(
        table_kernel,
        grid=(n_coarse // TABLE_Q,),
        in_specs=[
            pl.BlockSpec((TABLE_Q, 1, NF), lambda q: (q, 0, 0)),
            pl.BlockSpec((TABLE_Q, 1, NF), lambda q: (q, 0, 0)),
            pl.BlockSpec((coarse, NF), lambda q: (0, 0)),
            pl.BlockSpec((coarse, NF), lambda q: (0, 0)),
            pl.BlockSpec((TABLE_Q, 1, F_CHUNK), lambda q: (q, 0, 0)),
            pl.BlockSpec((TABLE_Q, 1, F_CHUNK), lambda q: (q, 0, 0)),
            pl.BlockSpec((coarse, F_CHUNK), lambda q: (0, 0)),
            pl.BlockSpec((coarse, F_CHUNK), lambda q: (0, 0)),
        ],
        out_specs=pl.BlockSpec((TABLE_Q * coarse, 2 * NF), lambda q: (q, 0)),
        out_shape=jax.ShapeDtypeStruct((WIN, 2 * NF), jnp.bfloat16),
    )(high_cos, high_sin, low_cos, low_sin, start_cos, start_sin, step_cos, step_sin)


def lag_table(count):
    freq_bins = K0 + jnp.arange(NF, dtype=jnp.int32)
    shifted = (jnp.arange(LAGS, dtype=jnp.int32) - LAGS // 2) % WIN
    wrapped = freq_bins[:, None] * shifted[None, :] % WIN
    phase_angle = wrapped.astype(jnp.float32) * (two_pi / WIN)
    factor = 1.0 / math.sqrt(NF * count)
    return jnp.concatenate(
        [jnp.cos(phase_angle) * factor, -jnp.sin(phase_angle) * factor], axis=0
    ).astype(jnp.bfloat16)


def whiten(spectra):
    real_part = spectra[..., :NF]
    imag_part = spectra[..., NF:]
    power_sum = real_part * real_part + imag_part * imag_part
    freq_bins = jnp.arange(NF, dtype=jnp.int32)
    band_matrix = (jnp.abs(freq_bins[:, None] - freq_bins[None, :]) <= SPAN).astype(jnp.float32)
    smooth = jnp.einsum(
        "...f,fg->...g", power_sum, band_matrix, precision=lax.Precision.HIGHEST
    ) / (2 * SPAN + 1)
    water_level = jnp.mean(power_sum, axis=-1, keepdims=True)
    weight = lax.rsqrt(smooth + 0.5 * water_level + 1e-06)
    return (spectra * jnp.concatenate([weight, weight], axis=-1)).astype(jnp.bfloat16)


ROW_TILE = 16
J_CHUNK = 64
F_CHUNK = 128


def pair_kernel(pairs_ref, row_ref, col_ref, lags_ref, out_ref, cross_ref, row32_ref, col32_ref):
    windows = row_ref.shape[1]
    cols = col_ref.shape[2]

    @pl.when(pl.program_id(1) == 0)
    def _():
        for w in range(windows):
            col_real = col_ref[0, w, :, :NF].astype(jnp.float32)
            col_imag = col_ref[0, w, :, NF:].astype(jnp.float32)
            col32_ref[w, :, :NF] = col_real
            col32_ref[w, :, NF : 2 * NF] = col_real - col_imag
            col32_ref[w, :, 2 * NF :] = col_real + col_imag

    for w in range(windows):
        row_real = row_ref[0, w, :, :NF].astype(jnp.float32)
        row_imag = row_ref[0, w, :, NF:].astype(jnp.float32)
        row32_ref[w, :, :NF] = row_real
        row32_ref[w, :, NF : 2 * NF] = row_imag
        row32_ref[w, :, 2 * NF :] = row_real + row_imag

    for i in range(row_ref.shape[2]):
        for jc in range(cols // J_CHUNK):
            js = pl.ds(jc * J_CHUNK, J_CHUNK)
            for fc in range(NF // F_CHUNK):
                fr = pl.ds(fc * F_CHUNK, F_CHUNK)
                fi = pl.ds(NF + fc * F_CHUNK, F_CHUNK)
                fs = pl.ds(2 * NF + fc * F_CHUNK, F_CHUNK)
                acc_re = jnp.zeros((J_CHUNK, F_CHUNK), jnp.float32)
                acc_im = jnp.zeros((J_CHUNK, F_CHUNK), jnp.float32)
                for w in range(windows):
                    xr = row32_ref[w, i : i + 1, fr]
                    xi = row32_ref[w, i : i + 1, fi]
                    xs = row32_ref[w, i : i + 1, fs]
                    yr = col32_ref[w, js, fr]
                    yd = col32_ref[w, js, fi]
                    ys = col32_ref[w, js, fs]
                    both = yr * xs
                    acc_re = acc_re + (both - xi * yd)
                    acc_im = acc_im + (both - xr * ys)
                rows = pl.ds(i * cols + jc * J_CHUNK, J_CHUNK)
                cross_ref[rows, fr] = acc_re.astype(jnp.bfloat16)
                cross_ref[rows, fi] = acc_im.astype(jnp.bfloat16)
    result = jnp.dot(cross_ref[...], lags_ref[...], preferred_element_type=jnp.float32)
    out_ref[0] = result.reshape(out_ref.shape[1:]).astype(out_ref.dtype)


def all_pairs(pairs, row_all, col_all, lags):
    n_pairs = pairs.shape[0]
    windows, rows, cols = row_all.shape[1], row_all.shape[2], col_all.shape[2]
    tiles = rows // ROW_TILE
    grid_spec = pltpu.PrefetchScalarGridSpec(
        num_scalar_prefetch=1,
        grid=(n_pairs, tiles),
        in_specs=[
            pl.BlockSpec((1, windows, ROW_TILE, 2 * NF), lambda p, t, pr: (pr[p, 0], 0, t, 0)),
            pl.BlockSpec((1, windows, cols, 2 * NF), lambda p, t, pr: (pr[p, 1], 0, 0, 0)),
            pl.BlockSpec((2 * NF, LAGS), lambda p, t, pr: (0, 0)),
        ],
        out_specs=pl.BlockSpec((1, ROW_TILE, cols, LAGS), lambda p, t, pr: (p, t, 0, 0)),
        scratch_shapes=[
            pltpu.VMEM((ROW_TILE * cols, 2 * NF), jnp.bfloat16),
            pltpu.VMEM((windows, ROW_TILE, 3 * NF), jnp.float32),
            pltpu.VMEM((windows, cols, 3 * NF), jnp.float32),
        ],
    )
    flops = n_pairs * rows * cols * (2 * NF * windows * 4 + 2 * 2 * NF * LAGS)
    return pl.pallas_call(
        pair_kernel,
        grid_spec=grid_spec,
        out_shape=jax.ShapeDtypeStruct((n_pairs, rows, cols, LAGS), jnp.bfloat16),
        compiler_params=pltpu.CompilerParams(
            dimension_semantics=("arbitrary", "arbitrary"),
            vmem_limit_bytes=48 * 1024 * 1024,
        ),
        cost_estimate=pl.CostEstimate(
            flops=flops,
            transcendentals=0,
            bytes_accessed=n_pairs * (rows + cols) * windows * 2 * NF * 2 + n_pairs * rows * cols * LAGS * 2,
        ),
    )(pairs, row_all, col_all, lags)


def exchange(value, axes, sizes, moves):
    pairs = []
    for source in itertools.product(*[range(s) for s in sizes]):
        target = moves(source)
        if target is None:
            continue
        pairs.append((linear(source, sizes), linear(target, sizes)))
    if not pairs:
        return None
    return lax.ppermute(value, axes, pairs)


def linear(coord, sizes):
    index = 0
    for c, s in zip(coord, sizes):
        index = index * s + c
    return index


def on_device(signal, offsets, pair_list):
    channels_here = signal.shape[0]
    samples_here = signal.shape[1]
    w_dev = samples_here // STEP
    n_tm = lax.axis_size("tm")
    n_prow = lax.axis_size("prow")
    n_pcol = lax.axis_size("pcol")
    tm_index = lax.axis_index("tm")
    prow_index = lax.axis_index("prow")
    pcol_index = lax.axis_index("pcol")
    dft_table = forward_table()
    head_samples = signal[:, :HALO]
    next_head = from_behind(head_samples, "tm", -1)
    extended = jnp.concatenate([signal, next_head], axis=1)

    segments = [
        lax.dynamic_slice_in_dim(extended, window * STEP + offsets[tm_index * w_dev + window], WIN, 1)
        for window in range(w_dev)
    ]
    stacked = jnp.concatenate(segments, axis=0)
    spectra = jnp.dot(stacked, dft_table, preferred_element_type=jnp.float32)
    spectra = spectra.reshape(w_dev, channels_here, 2 * NF)
    whitened = whiten(spectra)
    half_rows = channels_here // n_tm

    row_windows = [lax.dynamic_slice_in_dim(whitened, tm_index * half_rows, half_rows, 1)]
    for e in range(1, n_tm):
        half = (tm_index - e + n_tm) % n_tm
        payload = lax.dynamic_slice_in_dim(whitened, half * half_rows, half_rows, 1)
        row_windows.append(exchange(payload, ("tm",), (n_tm,), lambda s, e=e: ((s[0] - e) % n_tm,)))
    row_own = jnp.concatenate(row_windows, axis=0)
    row_slots = [row_own]
    for d in range(1, n_pcol):
        row_slots.append(exchange(row_own, ("pcol",), (n_pcol,), lambda s, d=d: ((s[0] - d) % n_pcol,)))
    row_all = jnp.stack(row_slots, axis=0)

    col_slots = []
    for d in range(n_prow):
        if d == 0:
            near = whitened
        else:
            near = exchange(
                near, ("prow",), (n_prow,), lambda s, d=d: (s[0] - 1,) if 1 <= s[0] <= n_prow - d else None
            )
        per_tm = [near]
        for e in range(1, n_tm):
            per_tm.append(exchange(near, ("tm",), (n_tm,), lambda s, e=e: ((s[0] - e) % n_tm,)))
        col_slots.append(jnp.concatenate(per_tm, axis=0))
    col_all = jnp.stack(col_slots, axis=0)

    lags = lag_table(n_tm * w_dev)
    local_pairs = pair_list[0, 0]
    row_slot = (local_pairs[:, 0] - pcol_index + n_pcol) % n_pcol
    col_slot = jnp.clip(local_pairs[:, 1] - prow_index, 0, n_prow - 1)
    pairs = jnp.stack([row_slot, col_slot], axis=1).astype(jnp.int32)
    result = all_pairs(pairs, row_all, col_all, lags)
    return result.reshape(1, 1, NP, half_rows, channels_here, LAGS)


def solution(mesh):
    placed = (P(("prow", "pcol"), "tm"), P(), P("prow", "pcol", None, None))
    return jax.shard_map(
        on_device,
        mesh=mesh,
        in_specs=placed,
        out_specs=P("prow", "pcol", None, "tm", None, None),
        check_vma=False,
    )
```

```python
import itertools
import math

import jax
import jax.numpy as jnp
from jax import lax
from jax.sharding import PartitionSpec as P
from jax.experimental import pallas as pl
from jax.experimental.pallas import tpu as pltpu

WIN = 7680
NF = 384
K0 = 32
LAGS = 256
SPAN = 4
NP = 4
STEP = 3840
HALO = 4352


two_pi = 2.0 * math.pi


def from_behind(value, axis, steps):
    count = lax.axis_size(axis)
    initial, last = (max(0, -steps), min(count, count - steps))
    return lax.ppermute(value, axis, [(source, source + steps) for source in range(initial, last)])


TABLE_Q = 12


def table_kernel(high_cos_ref, high_sin_ref, low_cos_ref, low_sin_ref, start_cos_ref, start_sin_ref,
                 step_cos_ref, step_sin_ref, out_ref):
    coarse = low_cos_ref.shape[0]
    step_cos = step_cos_ref[...]
    step_sin = step_sin_ref[...]
    for qq in range(TABLE_Q):
        rows = pl.ds(qq * coarse, coarse)
        taper = 0.5 - 0.5 * (start_cos_ref[qq] * step_cos - start_sin_ref[qq] * step_sin)
        for fc in range(NF // F_CHUNK):
            lanes = pl.ds(fc * F_CHUNK, F_CHUNK)
            hc = high_cos_ref[qq, :, lanes]
            hs = high_sin_ref[qq, :, lanes]
            lc = low_cos_ref[:, lanes]
            ls = low_sin_ref[:, lanes]
            out_ref[rows, lanes] = (taper * (hc * lc - hs * ls)).astype(out_ref.dtype)
            out_ref[rows, pl.ds(NF + fc * F_CHUNK, F_CHUNK)] = (-(taper * (hs * lc + hc * ls))).astype(out_ref.dtype)


def forward_table():
    coarse = 128
    n_coarse = WIN // coarse
    freq_bins = K0 + jnp.arange(NF, dtype=jnp.int32)
    scale = two_pi / WIN
    high_idx = (jnp.arange(n_coarse, dtype=jnp.int32) * coarse)[:, None] * freq_bins[None, :] % WIN
    low_idx = jnp.arange(coarse, dtype=jnp.int32)[:, None] * freq_bins[None, :] % WIN
    high_angle = high_idx.astype(jnp.float32) * scale
    low_angle = low_idx.astype(jnp.float32) * scale
    high_cos = jnp.cos(high_angle).reshape(n_coarse, 1, NF)
    high_sin = jnp.sin(high_angle).reshape(n_coarse, 1, NF)
    low_cos, low_sin = jnp.cos(low_angle), jnp.sin(low_angle)
    start_angle = (jnp.arange(n_coarse, dtype=jnp.int32) * coarse).astype(jnp.float32) * scale
    step_angle = jnp.arange(coarse, dtype=jnp.int32).astype(jnp.float32) * scale
    start_cos = jnp.broadcast_to(jnp.cos(start_angle)[:, None, None], (n_coarse, 1, F_CHUNK))
    start_sin = jnp.broadcast_to(jnp.sin(start_angle)[:, None, None], (n_coarse, 1, F_CHUNK))
    step_cos = jnp.broadcast_to(jnp.cos(step_angle)[:, None], (coarse, F_CHUNK))
    step_sin = jnp.broadcast_to(jnp.sin(step_angle)[:, None], (coarse, F_CHUNK))
    return pl.pallas_call(
        table_kernel,
        grid=(n_coarse // TABLE_Q,),
        in_specs=[
            pl.BlockSpec((TABLE_Q, 1, NF), lambda q: (q, 0, 0)),
            pl.BlockSpec((TABLE_Q, 1, NF), lambda q: (q, 0, 0)),
            pl.BlockSpec((coarse, NF), lambda q: (0, 0)),
            pl.BlockSpec((coarse, NF), lambda q: (0, 0)),
            pl.BlockSpec((TABLE_Q, 1, F_CHUNK), lambda q: (q, 0, 0)),
            pl.BlockSpec((TABLE_Q, 1, F_CHUNK), lambda q: (q, 0, 0)),
            pl.BlockSpec((coarse, F_CHUNK), lambda q: (0, 0)),
            pl.BlockSpec((coarse, F_CHUNK), lambda q: (0, 0)),
        ],
        out_specs=pl.BlockSpec((TABLE_Q * coarse, 2 * NF), lambda q: (q, 0)),
        out_shape=jax.ShapeDtypeStruct((WIN, 2 * NF), jnp.bfloat16),
    )(high_cos, high_sin, low_cos, low_sin, start_cos, start_sin, step_cos, step_sin)


def lag_table(count):
    freq_bins = K0 + jnp.arange(NF, dtype=jnp.int32)
    shifted = (jnp.arange(LAGS, dtype=jnp.int32) - LAGS // 2) % WIN
    wrapped = freq_bins[:, None] * shifted[None, :] % WIN
    phase_angle = wrapped.astype(jnp.float32) * (two_pi / WIN)
    factor = 1.0 / math.sqrt(NF * count)
    return jnp.concatenate(
        [jnp.cos(phase_angle) * factor, -jnp.sin(phase_angle) * factor], axis=0
    ).astype(jnp.bfloat16)


def whiten(spectra):
    real_part = spectra[..., :NF]
    imag_part = spectra[..., NF:]
    power_sum = real_part * real_part + imag_part * imag_part
    freq_bins = jnp.arange(NF, dtype=jnp.int32)
    band_matrix = (jnp.abs(freq_bins[:, None] - freq_bins[None, :]) <= SPAN).astype(jnp.float32)
    smooth = jnp.einsum(
        "...f,fg->...g", power_sum, band_matrix, precision=lax.Precision.HIGHEST
    ) / (2 * SPAN + 1)
    water_level = jnp.mean(power_sum, axis=-1, keepdims=True)
    weight = lax.rsqrt(smooth + 0.5 * water_level + 1e-06)
    return (spectra * jnp.concatenate([weight, weight], axis=-1)).astype(jnp.bfloat16)


ROW_TILE = 32
J_CHUNK = 64
F_CHUNK = 128


def pair_kernel(pairs_ref, row_ref, col_ref, lags_ref, out_ref, cross_ref, row32_ref, col32_ref):
    windows = row_ref.shape[1]
    cols = col_ref.shape[2]

    @pl.when(pl.program_id(1) == 0)
    def _():
        for w in range(windows):
            col_real = col_ref[0, w, :, :NF].astype(jnp.float32)
            col_imag = col_ref[0, w, :, NF:].astype(jnp.float32)
            col32_ref[w, :, :NF] = col_real
            col32_ref[w, :, NF : 2 * NF] = col_real - col_imag
            col32_ref[w, :, 2 * NF :] = col_real + col_imag

    for w in range(windows):
        row_real = row_ref[0, w, :, :NF].astype(jnp.float32)
        row_imag = row_ref[0, w, :, NF:].astype(jnp.float32)
        row32_ref[w, :, :NF] = row_real
        row32_ref[w, :, NF : 2 * NF] = row_imag
        row32_ref[w, :, 2 * NF :] = row_real + row_imag

    for i in range(row_ref.shape[2]):
        for jc in range(cols // J_CHUNK):
            js = pl.ds(jc * J_CHUNK, J_CHUNK)
            for fc in range(NF // F_CHUNK):
                fr = pl.ds(fc * F_CHUNK, F_CHUNK)
                fi = pl.ds(NF + fc * F_CHUNK, F_CHUNK)
                fs = pl.ds(2 * NF + fc * F_CHUNK, F_CHUNK)
                acc_re = jnp.zeros((J_CHUNK, F_CHUNK), jnp.float32)
                acc_im = jnp.zeros((J_CHUNK, F_CHUNK), jnp.float32)
                for w in range(windows):
                    xr = row32_ref[w, i : i + 1, fr]
                    xi = row32_ref[w, i : i + 1, fi]
                    xs = row32_ref[w, i : i + 1, fs]
                    yr = col32_ref[w, js, fr]
                    yd = col32_ref[w, js, fi]
                    ys = col32_ref[w, js, fs]
                    both = yr * xs
                    acc_re = acc_re + (both - xi * yd)
                    acc_im = acc_im + (both - xr * ys)
                rows = pl.ds(i * cols + jc * J_CHUNK, J_CHUNK)
                cross_ref[rows, fr] = acc_re.astype(jnp.bfloat16)
                cross_ref[rows, fi] = acc_im.astype(jnp.bfloat16)
    result = jnp.dot(cross_ref[...], lags_ref[...], preferred_element_type=jnp.float32)
    out_ref[0] = result.reshape(out_ref.shape[1:]).astype(out_ref.dtype)


def all_pairs(pairs, row_all, col_all, lags):
    n_pairs = pairs.shape[0]
    windows, rows, cols = row_all.shape[1], row_all.shape[2], col_all.shape[2]
    tiles = rows // ROW_TILE
    grid_spec = pltpu.PrefetchScalarGridSpec(
        num_scalar_prefetch=1,
        grid=(n_pairs, tiles),
        in_specs=[
            pl.BlockSpec((1, windows, ROW_TILE, 2 * NF), lambda p, t, pr: (pr[p, 0], 0, t, 0)),
            pl.BlockSpec((1, windows, cols, 2 * NF), lambda p, t, pr: (pr[p, 1], 0, 0, 0)),
            pl.BlockSpec((2 * NF, LAGS), lambda p, t, pr: (0, 0)),
        ],
        out_specs=pl.BlockSpec((1, ROW_TILE, cols, LAGS), lambda p, t, pr: (p, t, 0, 0)),
        scratch_shapes=[
            pltpu.VMEM((ROW_TILE * cols, 2 * NF), jnp.bfloat16),
            pltpu.VMEM((windows, ROW_TILE, 3 * NF), jnp.float32),
            pltpu.VMEM((windows, cols, 3 * NF), jnp.float32),
        ],
    )
    flops = n_pairs * rows * cols * (2 * NF * windows * 4 + 2 * 2 * NF * LAGS)
    return pl.pallas_call(
        pair_kernel,
        grid_spec=grid_spec,
        out_shape=jax.ShapeDtypeStruct((n_pairs, rows, cols, LAGS), jnp.bfloat16),
        compiler_params=pltpu.CompilerParams(
            dimension_semantics=("arbitrary", "arbitrary"),
            vmem_limit_bytes=48 * 1024 * 1024,
        ),
        cost_estimate=pl.CostEstimate(
            flops=flops,
            transcendentals=0,
            bytes_accessed=n_pairs * (rows + cols) * windows * 2 * NF * 2 + n_pairs * rows * cols * LAGS * 2,
        ),
    )(pairs, row_all, col_all, lags)


def exchange(value, axes, sizes, moves):
    pairs = []
    for source in itertools.product(*[range(s) for s in sizes]):
        target = moves(source)
        if target is None:
            continue
        pairs.append((linear(source, sizes), linear(target, sizes)))
    if not pairs:
        return None
    return lax.ppermute(value, axes, pairs)


def linear(coord, sizes):
    index = 0
    for c, s in zip(coord, sizes):
        index = index * s + c
    return index


def on_device(signal, offsets, pair_list):
    channels_here = signal.shape[0]
    samples_here = signal.shape[1]
    w_dev = samples_here // STEP
    n_tm = lax.axis_size("tm")
    n_prow = lax.axis_size("prow")
    n_pcol = lax.axis_size("pcol")
    tm_index = lax.axis_index("tm")
    prow_index = lax.axis_index("prow")
    pcol_index = lax.axis_index("pcol")
    dft_table = forward_table()
    head_samples = signal[:, :HALO]
    next_head = from_behind(head_samples, "tm", -1)
    extended = jnp.concatenate([signal, next_head], axis=1)

    segments = [
        lax.dynamic_slice_in_dim(extended, window * STEP + offsets[tm_index * w_dev + window], WIN, 1)
        for window in range(w_dev)
    ]
    stacked = jnp.concatenate(segments, axis=0)
    spectra = jnp.dot(stacked, dft_table, preferred_element_type=jnp.float32)
    spectra = spectra.reshape(w_dev, channels_here, 2 * NF)
    whitened = whiten(spectra)
    half_rows = channels_here // n_tm

    row_windows = [lax.dynamic_slice_in_dim(whitened, tm_index * half_rows, half_rows, 1)]
    for e in range(1, n_tm):
        half = (tm_index - e + n_tm) % n_tm
        payload = lax.dynamic_slice_in_dim(whitened, half * half_rows, half_rows, 1)
        row_windows.append(exchange(payload, ("tm",), (n_tm,), lambda s, e=e: ((s[0] - e) % n_tm,)))
    row_own = jnp.concatenate(row_windows, axis=0)
    row_slots = [row_own]
    for d in range(1, n_pcol):
        row_slots.append(exchange(row_own, ("pcol",), (n_pcol,), lambda s, d=d: ((s[0] - d) % n_pcol,)))
    row_all = jnp.stack(row_slots, axis=0)

    col_slots = []
    for d in range(n_prow):
        if d == 0:
            near = whitened
        else:
            near = exchange(
                near, ("prow",), (n_prow,), lambda s, d=d: (s[0] - 1,) if 1 <= s[0] <= n_prow - d else None
            )
        per_tm = [near]
        for e in range(1, n_tm):
            per_tm.append(exchange(near, ("tm",), (n_tm,), lambda s, e=e: ((s[0] - e) % n_tm,)))
        col_slots.append(jnp.concatenate(per_tm, axis=0))
    col_all = jnp.stack(col_slots, axis=0)

    lags = lag_table(n_tm * w_dev)
    local_pairs = pair_list[0, 0]
    row_slot = (local_pairs[:, 0] - pcol_index + n_pcol) % n_pcol
    col_slot = jnp.clip(local_pairs[:, 1] - prow_index, 0, n_prow - 1)
    pairs = jnp.stack([row_slot, col_slot], axis=1).astype(jnp.int32)
    result = all_pairs(pairs, row_all, col_all, lags)
    return result.reshape(1, 1, NP, half_rows, channels_here, LAGS)


def solution(mesh):
    placed = (P(("prow", "pcol"), "tm"), P(), P("prow", "pcol", None, None))
    return jax.shard_map(
        on_device,
        mesh=mesh,
        in_specs=placed,
        out_specs=P("prow", "pcol", None, "tm", None, None),
        check_vma=False,
    )
```

```python
import itertools
import math

import jax
import jax.numpy as jnp
from jax import lax
from jax.sharding import PartitionSpec as P
from jax.experimental import pallas as pl
from jax.experimental.pallas import tpu as pltpu

WIN = 7680
NF = 384
K0 = 32
LAGS = 256
SPAN = 4
NP = 4
STEP = 3840
HALO = 4352


two_pi = 2.0 * math.pi


def from_behind(value, axis, steps):
    count = lax.axis_size(axis)
    initial, last = (max(0, -steps), min(count, count - steps))
    return lax.ppermute(value, axis, [(source, source + steps) for source in range(initial, last)])


TABLE_Q = 12


def table_kernel(high_cos_ref, high_sin_ref, low_cos_ref, low_sin_ref, start_cos_ref, start_sin_ref,
                 step_cos_ref, step_sin_ref, out_ref):
    coarse = low_cos_ref.shape[0]
    step_cos = step_cos_ref[...]
    step_sin = step_sin_ref[...]
    for qq in range(TABLE_Q):
        rows = pl.ds(qq * coarse, coarse)
        taper = 0.5 - 0.5 * (start_cos_ref[qq] * step_cos - start_sin_ref[qq] * step_sin)
        for fc in range(NF // F_CHUNK):
            lanes = pl.ds(fc * F_CHUNK, F_CHUNK)
            hc = high_cos_ref[qq, :, lanes]
            hs = high_sin_ref[qq, :, lanes]
            lc = low_cos_ref[:, lanes]
            ls = low_sin_ref[:, lanes]
            out_ref[rows, lanes] = (taper * (hc * lc - hs * ls)).astype(out_ref.dtype)
            out_ref[rows, pl.ds(NF + fc * F_CHUNK, F_CHUNK)] = (-(taper * (hs * lc + hc * ls))).astype(out_ref.dtype)


def forward_table():
    coarse = 128
    n_coarse = WIN // coarse
    freq_bins = K0 + jnp.arange(NF, dtype=jnp.int32)
    scale = two_pi / WIN
    high_idx = (jnp.arange(n_coarse, dtype=jnp.int32) * coarse)[:, None] * freq_bins[None, :] % WIN
    low_idx = jnp.arange(coarse, dtype=jnp.int32)[:, None] * freq_bins[None, :] % WIN
    high_angle = high_idx.astype(jnp.float32) * scale
    low_angle = low_idx.astype(jnp.float32) * scale
    high_cos = jnp.cos(high_angle).reshape(n_coarse, 1, NF)
    high_sin = jnp.sin(high_angle).reshape(n_coarse, 1, NF)
    low_cos, low_sin = jnp.cos(low_angle), jnp.sin(low_angle)
    start_angle = (jnp.arange(n_coarse, dtype=jnp.int32) * coarse).astype(jnp.float32) * scale
    step_angle = jnp.arange(coarse, dtype=jnp.int32).astype(jnp.float32) * scale
    start_cos = jnp.broadcast_to(jnp.cos(start_angle)[:, None, None], (n_coarse, 1, F_CHUNK))
    start_sin = jnp.broadcast_to(jnp.sin(start_angle)[:, None, None], (n_coarse, 1, F_CHUNK))
    step_cos = jnp.broadcast_to(jnp.cos(step_angle)[:, None], (coarse, F_CHUNK))
    step_sin = jnp.broadcast_to(jnp.sin(step_angle)[:, None], (coarse, F_CHUNK))
    return pl.pallas_call(
        table_kernel,
        grid=(n_coarse // TABLE_Q,),
        in_specs=[
            pl.BlockSpec((TABLE_Q, 1, NF), lambda q: (q, 0, 0)),
            pl.BlockSpec((TABLE_Q, 1, NF), lambda q: (q, 0, 0)),
            pl.BlockSpec((coarse, NF), lambda q: (0, 0)),
            pl.BlockSpec((coarse, NF), lambda q: (0, 0)),
            pl.BlockSpec((TABLE_Q, 1, F_CHUNK), lambda q: (q, 0, 0)),
            pl.BlockSpec((TABLE_Q, 1, F_CHUNK), lambda q: (q, 0, 0)),
            pl.BlockSpec((coarse, F_CHUNK), lambda q: (0, 0)),
            pl.BlockSpec((coarse, F_CHUNK), lambda q: (0, 0)),
        ],
        out_specs=pl.BlockSpec((TABLE_Q * coarse, 2 * NF), lambda q: (q, 0)),
        out_shape=jax.ShapeDtypeStruct((WIN, 2 * NF), jnp.bfloat16),
    )(high_cos, high_sin, low_cos, low_sin, start_cos, start_sin, step_cos, step_sin)


def lag_table(count):
    freq_bins = K0 + jnp.arange(NF, dtype=jnp.int32)
    shifted = (jnp.arange(LAGS, dtype=jnp.int32) - LAGS // 2) % WIN
    wrapped = freq_bins[:, None] * shifted[None, :] % WIN
    phase_angle = wrapped.astype(jnp.float32) * (two_pi / WIN)
    factor = 1.0 / math.sqrt(NF * count)
    return jnp.concatenate(
        [jnp.cos(phase_angle) * factor, -jnp.sin(phase_angle) * factor], axis=0
    ).astype(jnp.bfloat16)


def whiten(spectra):
    real_part = spectra[..., :NF]
    imag_part = spectra[..., NF:]
    power_sum = real_part * real_part + imag_part * imag_part
    freq_bins = jnp.arange(NF, dtype=jnp.int32)
    band_matrix = (jnp.abs(freq_bins[:, None] - freq_bins[None, :]) <= SPAN).astype(jnp.float32)
    smooth = jnp.einsum(
        "...f,fg->...g", power_sum, band_matrix, precision=lax.Precision.HIGHEST
    ) / (2 * SPAN + 1)
    water_level = jnp.mean(power_sum, axis=-1, keepdims=True)
    weight = lax.rsqrt(smooth + 0.5 * water_level + 1e-06)
    return (spectra * jnp.concatenate([weight, weight], axis=-1)).astype(jnp.bfloat16)


ROW_TILE = 16
J_CHUNK = 64
F_CHUNK = 128


def pair_kernel(pairs_ref, row_ref, col_ref, lags_ref, out_ref, cross_ref, row32_ref, col32_ref):
    windows = row_ref.shape[1]
    cols = col_ref.shape[2]

    @pl.when(pl.program_id(1) == 0)
    def _():
        for w in range(windows):
            col_real = col_ref[0, w, :, :NF].astype(jnp.float32)
            col_imag = col_ref[0, w, :, NF:].astype(jnp.float32)
            col32_ref[w, :, :NF] = col_real
            col32_ref[w, :, NF : 2 * NF] = col_real - col_imag
            col32_ref[w, :, 2 * NF :] = col_real + col_imag

    for w in range(windows):
        row_real = row_ref[0, w, :, :NF].astype(jnp.float32)
        row_imag = row_ref[0, w, :, NF:].astype(jnp.float32)
        row32_ref[w, :, :NF] = row_real
        row32_ref[w, :, NF : 2 * NF] = row_imag
        row32_ref[w, :, 2 * NF :] = row_real + row_imag

    for i in range(row_ref.shape[2]):
        for jc in range(cols // J_CHUNK):
            js = pl.ds(jc * J_CHUNK, J_CHUNK)
            for fc in range(NF // F_CHUNK):
                fr = pl.ds(fc * F_CHUNK, F_CHUNK)
                fi = pl.ds(NF + fc * F_CHUNK, F_CHUNK)
                fs = pl.ds(2 * NF + fc * F_CHUNK, F_CHUNK)
                acc_both = jnp.zeros((J_CHUNK, F_CHUNK), jnp.float32)
                acc_re = jnp.zeros((J_CHUNK, F_CHUNK), jnp.float32)
                acc_im = jnp.zeros((J_CHUNK, F_CHUNK), jnp.float32)
                for w in range(windows):
                    xr = row32_ref[w, i : i + 1, fr]
                    xi = row32_ref[w, i : i + 1, fi]
                    xs = row32_ref[w, i : i + 1, fs]
                    yr = col32_ref[w, js, fr]
                    yd = col32_ref[w, js, fi]
                    ys = col32_ref[w, js, fs]
                    acc_both = acc_both + yr * xs
                    acc_re = acc_re + xi * yd
                    acc_im = acc_im + xr * ys
                acc_re = acc_both - acc_re
                acc_im = acc_both - acc_im
                rows = pl.ds(i * cols + jc * J_CHUNK, J_CHUNK)
                cross_ref[rows, fr] = acc_re.astype(jnp.bfloat16)
                cross_ref[rows, fi] = acc_im.astype(jnp.bfloat16)
    result = jnp.dot(cross_ref[...], lags_ref[...], preferred_element_type=jnp.float32)
    out_ref[0] = result.reshape(out_ref.shape[1:]).astype(out_ref.dtype)


def all_pairs(pairs, row_all, col_all, lags):
    n_pairs = pairs.shape[0]
    windows, rows, cols = row_all.shape[1], row_all.shape[2], col_all.shape[2]
    tiles = rows // ROW_TILE
    grid_spec = pltpu.PrefetchScalarGridSpec(
        num_scalar_prefetch=1,
        grid=(n_pairs, tiles),
        in_specs=[
            pl.BlockSpec((1, windows, ROW_TILE, 2 * NF), lambda p, t, pr: (pr[p, 0], 0, t, 0)),
            pl.BlockSpec((1, windows, cols, 2 * NF), lambda p, t, pr: (pr[p, 1], 0, 0, 0)),
            pl.BlockSpec((2 * NF, LAGS), lambda p, t, pr: (0, 0)),
        ],
        out_specs=pl.BlockSpec((1, ROW_TILE, cols, LAGS), lambda p, t, pr: (p, t, 0, 0)),
        scratch_shapes=[
            pltpu.VMEM((ROW_TILE * cols, 2 * NF), jnp.bfloat16),
            pltpu.VMEM((windows, ROW_TILE, 3 * NF), jnp.float32),
            pltpu.VMEM((windows, cols, 3 * NF), jnp.float32),
        ],
    )
    flops = n_pairs * rows * cols * (2 * NF * windows * 4 + 2 * 2 * NF * LAGS)
    return pl.pallas_call(
        pair_kernel,
        grid_spec=grid_spec,
        out_shape=jax.ShapeDtypeStruct((n_pairs, rows, cols, LAGS), jnp.bfloat16),
        compiler_params=pltpu.CompilerParams(
            dimension_semantics=("arbitrary", "arbitrary"),
            vmem_limit_bytes=48 * 1024 * 1024,
        ),
        cost_estimate=pl.CostEstimate(
            flops=flops,
            transcendentals=0,
            bytes_accessed=n_pairs * (rows + cols) * windows * 2 * NF * 2 + n_pairs * rows * cols * LAGS * 2,
        ),
    )(pairs, row_all, col_all, lags)


def exchange(value, axes, sizes, moves):
    pairs = []
    for source in itertools.product(*[range(s) for s in sizes]):
        target = moves(source)
        if target is None:
            continue
        pairs.append((linear(source, sizes), linear(target, sizes)))
    if not pairs:
        return None
    return lax.ppermute(value, axes, pairs)


def linear(coord, sizes):
    index = 0
    for c, s in zip(coord, sizes):
        index = index * s + c
    return index


def on_device(signal, offsets, pair_list):
    channels_here = signal.shape[0]
    samples_here = signal.shape[1]
    w_dev = samples_here // STEP
    n_tm = lax.axis_size("tm")
    n_prow = lax.axis_size("prow")
    n_pcol = lax.axis_size("pcol")
    tm_index = lax.axis_index("tm")
    prow_index = lax.axis_index("prow")
    pcol_index = lax.axis_index("pcol")
    dft_table = forward_table()
    head_samples = signal[:, :HALO]
    next_head = from_behind(head_samples, "tm", -1)
    extended = jnp.concatenate([signal, next_head], axis=1)

    segments = [
        lax.dynamic_slice_in_dim(extended, window * STEP + offsets[tm_index * w_dev + window], WIN, 1)
        for window in range(w_dev)
    ]
    stacked = jnp.concatenate(segments, axis=0)
    spectra = jnp.dot(stacked, dft_table, preferred_element_type=jnp.float32)
    spectra = spectra.reshape(w_dev, channels_here, 2 * NF)
    whitened = whiten(spectra)
    half_rows = channels_here // n_tm

    row_windows = [lax.dynamic_slice_in_dim(whitened, tm_index * half_rows, half_rows, 1)]
    for e in range(1, n_tm):
        half = (tm_index - e + n_tm) % n_tm
        payload = lax.dynamic_slice_in_dim(whitened, half * half_rows, half_rows, 1)
        row_windows.append(exchange(payload, ("tm",), (n_tm,), lambda s, e=e: ((s[0] - e) % n_tm,)))
    row_own = jnp.concatenate(row_windows, axis=0)
    row_slots = [row_own]
    for d in range(1, n_pcol):
        row_slots.append(exchange(row_own, ("pcol",), (n_pcol,), lambda s, d=d: ((s[0] - d) % n_pcol,)))
    row_all = jnp.stack(row_slots, axis=0)

    col_slots = []
    for d in range(n_prow):
        if d == 0:
            near = whitened
        else:
            near = exchange(
                near, ("prow",), (n_prow,), lambda s, d=d: (s[0] - 1,) if 1 <= s[0] <= n_prow - d else None
            )
        per_tm = [near]
        for e in range(1, n_tm):
            per_tm.append(exchange(near, ("tm",), (n_tm,), lambda s, e=e: ((s[0] - e) % n_tm,)))
        col_slots.append(jnp.concatenate(per_tm, axis=0))
    col_all = jnp.stack(col_slots, axis=0)

    lags = lag_table(n_tm * w_dev)
    local_pairs = pair_list[0, 0]
    row_slot = (local_pairs[:, 0] - pcol_index + n_pcol) % n_pcol
    col_slot = jnp.clip(local_pairs[:, 1] - prow_index, 0, n_prow - 1)
    pairs = jnp.stack([row_slot, col_slot], axis=1).astype(jnp.int32)
    result = all_pairs(pairs, row_all, col_all, lags)
    return result.reshape(1, 1, NP, half_rows, channels_here, LAGS)


def solution(mesh):
    placed = (P(("prow", "pcol"), "tm"), P(), P("prow", "pcol", None, None))
    return jax.shard_map(
        on_device,
        mesh=mesh,
        in_specs=placed,
        out_specs=P("prow", "pcol", None, "tm", None, None),
        check_vma=False,
    )
```

```python
import itertools
import math

import jax
import jax.numpy as jnp
from jax import lax
from jax.sharding import PartitionSpec as P
from jax.experimental import pallas as pl
from jax.experimental.pallas import tpu as pltpu

WIN = 7680
NF = 384
K0 = 32
LAGS = 256
SPAN = 4
NP = 4
STEP = 3840
HALO = 4352


two_pi = 2.0 * math.pi


def from_behind(value, axis, steps):
    count = lax.axis_size(axis)
    initial, last = (max(0, -steps), min(count, count - steps))
    return lax.ppermute(value, axis, [(source, source + steps) for source in range(initial, last)])


TABLE_Q = 12


def table_kernel(high_cos_ref, high_sin_ref, low_cos_ref, low_sin_ref, start_cos_ref, start_sin_ref,
                 step_cos_ref, step_sin_ref, out_ref):
    coarse = low_cos_ref.shape[0]
    step_cos = step_cos_ref[...]
    step_sin = step_sin_ref[...]
    for qq in range(TABLE_Q):
        rows = pl.ds(qq * coarse, coarse)
        taper = 0.5 - 0.5 * (start_cos_ref[qq] * step_cos - start_sin_ref[qq] * step_sin)
        for fc in range(NF // F_CHUNK):
            lanes = pl.ds(fc * F_CHUNK, F_CHUNK)
            hc = high_cos_ref[qq, :, lanes]
            hs = high_sin_ref[qq, :, lanes]
            lc = low_cos_ref[:, lanes]
            ls = low_sin_ref[:, lanes]
            out_ref[rows, lanes] = (taper * (hc * lc - hs * ls)).astype(out_ref.dtype)
            out_ref[rows, pl.ds(NF + fc * F_CHUNK, F_CHUNK)] = (-(taper * (hs * lc + hc * ls))).astype(out_ref.dtype)


def forward_table():
    coarse = 128
    n_coarse = WIN // coarse
    freq_bins = K0 + jnp.arange(NF, dtype=jnp.int32)
    scale = two_pi / WIN
    high_idx = (jnp.arange(n_coarse, dtype=jnp.int32) * coarse)[:, None] * freq_bins[None, :] % WIN
    low_idx = jnp.arange(coarse, dtype=jnp.int32)[:, None] * freq_bins[None, :] % WIN
    high_angle = high_idx.astype(jnp.float32) * scale
    low_angle = low_idx.astype(jnp.float32) * scale
    high_cos = jnp.cos(high_angle).reshape(n_coarse, 1, NF)
    high_sin = jnp.sin(high_angle).reshape(n_coarse, 1, NF)
    low_cos, low_sin = jnp.cos(low_angle), jnp.sin(low_angle)
    start_angle = (jnp.arange(n_coarse, dtype=jnp.int32) * coarse).astype(jnp.float32) * scale
    step_angle = jnp.arange(coarse, dtype=jnp.int32).astype(jnp.float32) * scale
    start_cos = jnp.broadcast_to(jnp.cos(start_angle)[:, None, None], (n_coarse, 1, F_CHUNK))
    start_sin = jnp.broadcast_to(jnp.sin(start_angle)[:, None, None], (n_coarse, 1, F_CHUNK))
    step_cos = jnp.broadcast_to(jnp.cos(step_angle)[:, None], (coarse, F_CHUNK))
    step_sin = jnp.broadcast_to(jnp.sin(step_angle)[:, None], (coarse, F_CHUNK))
    return pl.pallas_call(
        table_kernel,
        grid=(n_coarse // TABLE_Q,),
        in_specs=[
            pl.BlockSpec((TABLE_Q, 1, NF), lambda q: (q, 0, 0)),
            pl.BlockSpec((TABLE_Q, 1, NF), lambda q: (q, 0, 0)),
            pl.BlockSpec((coarse, NF), lambda q: (0, 0)),
            pl.BlockSpec((coarse, NF), lambda q: (0, 0)),
            pl.BlockSpec((TABLE_Q, 1, F_CHUNK), lambda q: (q, 0, 0)),
            pl.BlockSpec((TABLE_Q, 1, F_CHUNK), lambda q: (q, 0, 0)),
            pl.BlockSpec((coarse, F_CHUNK), lambda q: (0, 0)),
            pl.BlockSpec((coarse, F_CHUNK), lambda q: (0, 0)),
        ],
        out_specs=pl.BlockSpec((TABLE_Q * coarse, 2 * NF), lambda q: (q, 0)),
        out_shape=jax.ShapeDtypeStruct((WIN, 2 * NF), jnp.bfloat16),
    )(high_cos, high_sin, low_cos, low_sin, start_cos, start_sin, step_cos, step_sin)


def lag_table(count):
    freq_bins = K0 + jnp.arange(NF, dtype=jnp.int32)
    shifted = (jnp.arange(LAGS, dtype=jnp.int32) - LAGS // 2) % WIN
    wrapped = freq_bins[:, None] * shifted[None, :] % WIN
    phase_angle = wrapped.astype(jnp.float32) * (two_pi / WIN)
    factor = 1.0 / math.sqrt(NF * count)
    return jnp.concatenate(
        [jnp.cos(phase_angle) * factor, -jnp.sin(phase_angle) * factor], axis=0
    ).astype(jnp.bfloat16)


def whiten(spectra):
    real_part = spectra[..., :NF]
    imag_part = spectra[..., NF:]
    power_sum = real_part * real_part + imag_part * imag_part
    freq_bins = jnp.arange(NF, dtype=jnp.int32)
    band_matrix = (jnp.abs(freq_bins[:, None] - freq_bins[None, :]) <= SPAN).astype(jnp.float32)
    smooth = jnp.einsum(
        "...f,fg->...g", power_sum, band_matrix, precision=lax.Precision.HIGHEST
    ) / (2 * SPAN + 1)
    water_level = jnp.mean(power_sum, axis=-1, keepdims=True)
    weight = lax.rsqrt(smooth + 0.5 * water_level + 1e-06)
    return (spectra * jnp.concatenate([weight, weight], axis=-1)).astype(jnp.bfloat16)


ROW_TILE = 16
J_CHUNK = 32
F_CHUNK = 128


def pair_kernel(pairs_ref, row_ref, col_ref, lags_ref, out_ref, cross_ref, row32_ref, col32_ref):
    windows = row_ref.shape[1]
    cols = col_ref.shape[2]

    @pl.when(pl.program_id(1) == 0)
    def _():
        for w in range(windows):
            col_real = col_ref[0, w, :, :NF].astype(jnp.float32)
            col_imag = col_ref[0, w, :, NF:].astype(jnp.float32)
            col32_ref[w, :, :NF] = col_real
            col32_ref[w, :, NF : 2 * NF] = col_real - col_imag
            col32_ref[w, :, 2 * NF :] = col_real + col_imag

    for w in range(windows):
        row_real = row_ref[0, w, :, :NF].astype(jnp.float32)
        row_imag = row_ref[0, w, :, NF:].astype(jnp.float32)
        row32_ref[w, :, :NF] = row_real
        row32_ref[w, :, NF : 2 * NF] = row_imag
        row32_ref[w, :, 2 * NF :] = row_real + row_imag

    for i in range(row_ref.shape[2]):
        for jc in range(cols // J_CHUNK):
            js = pl.ds(jc * J_CHUNK, J_CHUNK)
            for fc in range(NF // F_CHUNK):
                fr = pl.ds(fc * F_CHUNK, F_CHUNK)
                fi = pl.ds(NF + fc * F_CHUNK, F_CHUNK)
                fs = pl.ds(2 * NF + fc * F_CHUNK, F_CHUNK)
                acc_both = jnp.zeros((J_CHUNK, F_CHUNK), jnp.float32)
                acc_re = jnp.zeros((J_CHUNK, F_CHUNK), jnp.float32)
                acc_im = jnp.zeros((J_CHUNK, F_CHUNK), jnp.float32)
                for w in range(windows):
                    xr = row32_ref[w, i : i + 1, fr]
                    xi = row32_ref[w, i : i + 1, fi]
                    xs = row32_ref[w, i : i + 1, fs]
                    yr = col32_ref[w, js, fr]
                    yd = col32_ref[w, js, fi]
                    ys = col32_ref[w, js, fs]
                    acc_both = acc_both + yr * xs
                    acc_re = acc_re + xi * yd
                    acc_im = acc_im + xr * ys
                acc_re = acc_both - acc_re
                acc_im = acc_both - acc_im
                rows = pl.ds(i * cols + jc * J_CHUNK, J_CHUNK)
                cross_ref[rows, fr] = acc_re.astype(jnp.bfloat16)
                cross_ref[rows, fi] = acc_im.astype(jnp.bfloat16)
    result = jnp.dot(cross_ref[...], lags_ref[...], preferred_element_type=jnp.float32)
    out_ref[0] = result.reshape(out_ref.shape[1:]).astype(out_ref.dtype)


def all_pairs(pairs, row_all, col_all, lags):
    n_pairs = pairs.shape[0]
    windows, rows, cols = row_all.shape[1], row_all.shape[2], col_all.shape[2]
    tiles = rows // ROW_TILE
    grid_spec = pltpu.PrefetchScalarGridSpec(
        num_scalar_prefetch=1,
        grid=(n_pairs, tiles),
        in_specs=[
            pl.BlockSpec((1, windows, ROW_TILE, 2 * NF), lambda p, t, pr: (pr[p, 0], 0, t, 0)),
            pl.BlockSpec((1, windows, cols, 2 * NF), lambda p, t, pr: (pr[p, 1], 0, 0, 0)),
            pl.BlockSpec((2 * NF, LAGS), lambda p, t, pr: (0, 0)),
        ],
        out_specs=pl.BlockSpec((1, ROW_TILE, cols, LAGS), lambda p, t, pr: (p, t, 0, 0)),
        scratch_shapes=[
            pltpu.VMEM((ROW_TILE * cols, 2 * NF), jnp.bfloat16),
            pltpu.VMEM((windows, ROW_TILE, 3 * NF), jnp.float32),
            pltpu.VMEM((windows, cols, 3 * NF), jnp.float32),
        ],
    )
    flops = n_pairs * rows * cols * (2 * NF * windows * 4 + 2 * 2 * NF * LAGS)
    return pl.pallas_call(
        pair_kernel,
        grid_spec=grid_spec,
        out_shape=jax.ShapeDtypeStruct((n_pairs, rows, cols, LAGS), jnp.bfloat16),
        compiler_params=pltpu.CompilerParams(
            dimension_semantics=("arbitrary", "arbitrary"),
            vmem_limit_bytes=48 * 1024 * 1024,
        ),
        cost_estimate=pl.CostEstimate(
            flops=flops,
            transcendentals=0,
            bytes_accessed=n_pairs * (rows + cols) * windows * 2 * NF * 2 + n_pairs * rows * cols * LAGS * 2,
        ),
    )(pairs, row_all, col_all, lags)


def exchange(value, axes, sizes, moves):
    pairs = []
    for source in itertools.product(*[range(s) for s in sizes]):
        target = moves(source)
        if target is None:
            continue
        pairs.append((linear(source, sizes), linear(target, sizes)))
    if not pairs:
        return None
    return lax.ppermute(value, axes, pairs)


def linear(coord, sizes):
    index = 0
    for c, s in zip(coord, sizes):
        index = index * s + c
    return index


def on_device(signal, offsets, pair_list):
    channels_here = signal.shape[0]
    samples_here = signal.shape[1]
    w_dev = samples_here // STEP
    n_tm = lax.axis_size("tm")
    n_prow = lax.axis_size("prow")
    n_pcol = lax.axis_size("pcol")
    tm_index = lax.axis_index("tm")
    prow_index = lax.axis_index("prow")
    pcol_index = lax.axis_index("pcol")
    dft_table = forward_table()
    head_samples = signal[:, :HALO]
    next_head = from_behind(head_samples, "tm", -1)
    extended = jnp.concatenate([signal, next_head], axis=1)

    segments = [
        lax.dynamic_slice_in_dim(extended, window * STEP + offsets[tm_index * w_dev + window], WIN, 1)
        for window in range(w_dev)
    ]
    stacked = jnp.concatenate(segments, axis=0)
    spectra = jnp.dot(stacked, dft_table, preferred_element_type=jnp.float32)
    spectra = spectra.reshape(w_dev, channels_here, 2 * NF)
    whitened = whiten(spectra)
    half_rows = channels_here // n_tm

    row_windows = [lax.dynamic_slice_in_dim(whitened, tm_index * half_rows, half_rows, 1)]
    for e in range(1, n_tm):
        half = (tm_index - e + n_tm) % n_tm
        payload = lax.dynamic_slice_in_dim(whitened, half * half_rows, half_rows, 1)
        row_windows.append(exchange(payload, ("tm",), (n_tm,), lambda s, e=e: ((s[0] - e) % n_tm,)))
    row_own = jnp.concatenate(row_windows, axis=0)
    row_slots = [row_own]
    for d in range(1, n_pcol):
        row_slots.append(exchange(row_own, ("pcol",), (n_pcol,), lambda s, d=d: ((s[0] - d) % n_pcol,)))
    row_all = jnp.stack(row_slots, axis=0)

    col_slots = []
    for d in range(n_prow):
        if d == 0:
            near = whitened
        else:
            near = exchange(
                near, ("prow",), (n_prow,), lambda s, d=d: (s[0] - 1,) if 1 <= s[0] <= n_prow - d else None
            )
        per_tm = [near]
        for e in range(1, n_tm):
            per_tm.append(exchange(near, ("tm",), (n_tm,), lambda s, e=e: ((s[0] - e) % n_tm,)))
        col_slots.append(jnp.concatenate(per_tm, axis=0))
    col_all = jnp.stack(col_slots, axis=0)

    lags = lag_table(n_tm * w_dev)
    local_pairs = pair_list[0, 0]
    row_slot = (local_pairs[:, 0] - pcol_index + n_pcol) % n_pcol
    col_slot = jnp.clip(local_pairs[:, 1] - prow_index, 0, n_prow - 1)
    pairs = jnp.stack([row_slot, col_slot], axis=1).astype(jnp.int32)
    result = all_pairs(pairs, row_all, col_all, lags)
    return result.reshape(1, 1, NP, half_rows, channels_here, LAGS)


def solution(mesh):
    placed = (P(("prow", "pcol"), "tm"), P(), P("prow", "pcol", None, None))
    return jax.shard_map(
        on_device,
        mesh=mesh,
        in_specs=placed,
        out_specs=P("prow", "pcol", None, "tm", None, None),
        check_vma=False,
    )
```

```python
import itertools
import math

import jax
import jax.numpy as jnp
from jax import lax
from jax.sharding import PartitionSpec as P
from jax.experimental import pallas as pl
from jax.experimental.pallas import tpu as pltpu

WIN = 7680
NF = 384
K0 = 32
LAGS = 256
SPAN = 4
NP = 4
STEP = 3840
HALO = 4352


two_pi = 2.0 * math.pi


def from_behind(value, axis, steps):
    count = lax.axis_size(axis)
    initial, last = (max(0, -steps), min(count, count - steps))
    return lax.ppermute(value, axis, [(source, source + steps) for source in range(initial, last)])


TABLE_Q = 12


def table_kernel(high_cos_ref, high_sin_ref, low_cos_ref, low_sin_ref, start_cos_ref, start_sin_ref,
                 step_cos_ref, step_sin_ref, out_ref):
    coarse = low_cos_ref.shape[0]
    step_cos = step_cos_ref[...]
    step_sin = step_sin_ref[...]
    for qq in range(TABLE_Q):
        rows = pl.ds(qq * coarse, coarse)
        taper = 0.5 - 0.5 * (start_cos_ref[qq] * step_cos - start_sin_ref[qq] * step_sin)
        for fc in range(NF // F_CHUNK):
            lanes = pl.ds(fc * F_CHUNK, F_CHUNK)
            hc = high_cos_ref[qq, :, lanes]
            hs = high_sin_ref[qq, :, lanes]
            lc = low_cos_ref[:, lanes]
            ls = low_sin_ref[:, lanes]
            out_ref[rows, lanes] = (taper * (hc * lc - hs * ls)).astype(out_ref.dtype)
            out_ref[rows, pl.ds(NF + fc * F_CHUNK, F_CHUNK)] = (-(taper * (hs * lc + hc * ls))).astype(out_ref.dtype)


def forward_table():
    coarse = 128
    n_coarse = WIN // coarse
    freq_bins = K0 + jnp.arange(NF, dtype=jnp.int32)
    scale = two_pi / WIN
    high_idx = (jnp.arange(n_coarse, dtype=jnp.int32) * coarse)[:, None] * freq_bins[None, :] % WIN
    low_idx = jnp.arange(coarse, dtype=jnp.int32)[:, None] * freq_bins[None, :] % WIN
    high_angle = high_idx.astype(jnp.float32) * scale
    low_angle = low_idx.astype(jnp.float32) * scale
    high_cos = jnp.cos(high_angle).reshape(n_coarse, 1, NF)
    high_sin = jnp.sin(high_angle).reshape(n_coarse, 1, NF)
    low_cos, low_sin = jnp.cos(low_angle), jnp.sin(low_angle)
    start_angle = (jnp.arange(n_coarse, dtype=jnp.int32) * coarse).astype(jnp.float32) * scale
    step_angle = jnp.arange(coarse, dtype=jnp.int32).astype(jnp.float32) * scale
    start_cos = jnp.broadcast_to(jnp.cos(start_angle)[:, None, None], (n_coarse, 1, F_CHUNK))
    start_sin = jnp.broadcast_to(jnp.sin(start_angle)[:, None, None], (n_coarse, 1, F_CHUNK))
    step_cos = jnp.broadcast_to(jnp.cos(step_angle)[:, None], (coarse, F_CHUNK))
    step_sin = jnp.broadcast_to(jnp.sin(step_angle)[:, None], (coarse, F_CHUNK))
    return pl.pallas_call(
        table_kernel,
        grid=(n_coarse // TABLE_Q,),
        in_specs=[
            pl.BlockSpec((TABLE_Q, 1, NF), lambda q: (q, 0, 0)),
            pl.BlockSpec((TABLE_Q, 1, NF), lambda q: (q, 0, 0)),
            pl.BlockSpec((coarse, NF), lambda q: (0, 0)),
            pl.BlockSpec((coarse, NF), lambda q: (0, 0)),
            pl.BlockSpec((TABLE_Q, 1, F_CHUNK), lambda q: (q, 0, 0)),
            pl.BlockSpec((TABLE_Q, 1, F_CHUNK), lambda q: (q, 0, 0)),
            pl.BlockSpec((coarse, F_CHUNK), lambda q: (0, 0)),
            pl.BlockSpec((coarse, F_CHUNK), lambda q: (0, 0)),
        ],
        out_specs=pl.BlockSpec((TABLE_Q * coarse, 2 * NF), lambda q: (q, 0)),
        out_shape=jax.ShapeDtypeStruct((WIN, 2 * NF), jnp.bfloat16),
    )(high_cos, high_sin, low_cos, low_sin, start_cos, start_sin, step_cos, step_sin)


def lag_table(count):
    freq_bins = K0 + jnp.arange(NF, dtype=jnp.int32)
    shifted = (jnp.arange(LAGS, dtype=jnp.int32) - LAGS // 2) % WIN
    wrapped = freq_bins[:, None] * shifted[None, :] % WIN
    phase_angle = wrapped.astype(jnp.float32) * (two_pi / WIN)
    factor = 1.0 / math.sqrt(NF * count)
    return jnp.concatenate(
        [jnp.cos(phase_angle) * factor, -jnp.sin(phase_angle) * factor], axis=0
    ).astype(jnp.bfloat16)


def whiten(spectra):
    real_part = spectra[..., :NF]
    imag_part = spectra[..., NF:]
    power_sum = real_part * real_part + imag_part * imag_part
    freq_bins = jnp.arange(NF, dtype=jnp.int32)
    band_matrix = (jnp.abs(freq_bins[:, None] - freq_bins[None, :]) <= SPAN).astype(jnp.float32)
    smooth = jnp.einsum(
        "...f,fg->...g", power_sum, band_matrix, precision=lax.Precision.HIGHEST
    ) / (2 * SPAN + 1)
    water_level = jnp.mean(power_sum, axis=-1, keepdims=True)
    weight = lax.rsqrt(smooth + 0.5 * water_level + 1e-06)
    return (spectra * jnp.concatenate([weight, weight], axis=-1)).astype(jnp.bfloat16)


ROW_TILE = 16
J_CHUNK = 16
F_CHUNK = 384


def pair_kernel(pairs_ref, row_ref, col_ref, lags_ref, out_ref, cross_ref, row32_ref, col32_ref):
    windows = row_ref.shape[1]
    cols = col_ref.shape[2]

    @pl.when(pl.program_id(1) == 0)
    def _():
        for w in range(windows):
            col_real = col_ref[0, w, :, :NF].astype(jnp.float32)
            col_imag = col_ref[0, w, :, NF:].astype(jnp.float32)
            col32_ref[w, :, :NF] = col_real
            col32_ref[w, :, NF : 2 * NF] = col_real - col_imag
            col32_ref[w, :, 2 * NF :] = col_real + col_imag

    for w in range(windows):
        row_real = row_ref[0, w, :, :NF].astype(jnp.float32)
        row_imag = row_ref[0, w, :, NF:].astype(jnp.float32)
        row32_ref[w, :, :NF] = row_real
        row32_ref[w, :, NF : 2 * NF] = row_imag
        row32_ref[w, :, 2 * NF :] = row_real + row_imag

    for i in range(row_ref.shape[2]):
        for jc in range(cols // J_CHUNK):
            js = pl.ds(jc * J_CHUNK, J_CHUNK)
            for fc in range(NF // F_CHUNK):
                fr = pl.ds(fc * F_CHUNK, F_CHUNK)
                fi = pl.ds(NF + fc * F_CHUNK, F_CHUNK)
                fs = pl.ds(2 * NF + fc * F_CHUNK, F_CHUNK)
                acc_both = jnp.zeros((J_CHUNK, F_CHUNK), jnp.float32)
                acc_re = jnp.zeros((J_CHUNK, F_CHUNK), jnp.float32)
                acc_im = jnp.zeros((J_CHUNK, F_CHUNK), jnp.float32)
                for w in range(windows):
                    xr = row32_ref[w, i : i + 1, fr]
                    xi = row32_ref[w, i : i + 1, fi]
                    xs = row32_ref[w, i : i + 1, fs]
                    yr = col32_ref[w, js, fr]
                    yd = col32_ref[w, js, fi]
                    ys = col32_ref[w, js, fs]
                    acc_both = acc_both + yr * xs
                    acc_re = acc_re + xi * yd
                    acc_im = acc_im + xr * ys
                acc_re = acc_both - acc_re
                acc_im = acc_both - acc_im
                rows = pl.ds(i * cols + jc * J_CHUNK, J_CHUNK)
                cross_ref[rows, fr] = acc_re.astype(jnp.bfloat16)
                cross_ref[rows, fi] = acc_im.astype(jnp.bfloat16)
    result = jnp.dot(cross_ref[...], lags_ref[...], preferred_element_type=jnp.float32)
    out_ref[0] = result.reshape(out_ref.shape[1:]).astype(out_ref.dtype)


def all_pairs(pairs, row_all, col_all, lags):
    n_pairs = pairs.shape[0]
    windows, rows, cols = row_all.shape[1], row_all.shape[2], col_all.shape[2]
    tiles = rows // ROW_TILE
    grid_spec = pltpu.PrefetchScalarGridSpec(
        num_scalar_prefetch=1,
        grid=(n_pairs, tiles),
        in_specs=[
            pl.BlockSpec((1, windows, ROW_TILE, 2 * NF), lambda p, t, pr: (pr[p, 0], 0, t, 0)),
            pl.BlockSpec((1, windows, cols, 2 * NF), lambda p, t, pr: (pr[p, 1], 0, 0, 0)),
            pl.BlockSpec((2 * NF, LAGS), lambda p, t, pr: (0, 0)),
        ],
        out_specs=pl.BlockSpec((1, ROW_TILE, cols, LAGS), lambda p, t, pr: (p, t, 0, 0)),
        scratch_shapes=[
            pltpu.VMEM((ROW_TILE * cols, 2 * NF), jnp.bfloat16),
            pltpu.VMEM((windows, ROW_TILE, 3 * NF), jnp.float32),
            pltpu.VMEM((windows, cols, 3 * NF), jnp.float32),
        ],
    )
    flops = n_pairs * rows * cols * (2 * NF * windows * 4 + 2 * 2 * NF * LAGS)
    return pl.pallas_call(
        pair_kernel,
        grid_spec=grid_spec,
        out_shape=jax.ShapeDtypeStruct((n_pairs, rows, cols, LAGS), jnp.bfloat16),
        compiler_params=pltpu.CompilerParams(
            dimension_semantics=("arbitrary", "arbitrary"),
            vmem_limit_bytes=48 * 1024 * 1024,
        ),
        cost_estimate=pl.CostEstimate(
            flops=flops,
            transcendentals=0,
            bytes_accessed=n_pairs * (rows + cols) * windows * 2 * NF * 2 + n_pairs * rows * cols * LAGS * 2,
        ),
    )(pairs, row_all, col_all, lags)


def exchange(value, axes, sizes, moves):
    pairs = []
    for source in itertools.product(*[range(s) for s in sizes]):
        target = moves(source)
        if target is None:
            continue
        pairs.append((linear(source, sizes), linear(target, sizes)))
    if not pairs:
        return None
    return lax.ppermute(value, axes, pairs)


def linear(coord, sizes):
    index = 0
    for c, s in zip(coord, sizes):
        index = index * s + c
    return index


def on_device(signal, offsets, pair_list):
    channels_here = signal.shape[0]
    samples_here = signal.shape[1]
    w_dev = samples_here // STEP
    n_tm = lax.axis_size("tm")
    n_prow = lax.axis_size("prow")
    n_pcol = lax.axis_size("pcol")
    tm_index = lax.axis_index("tm")
    prow_index = lax.axis_index("prow")
    pcol_index = lax.axis_index("pcol")
    dft_table = forward_table()
    head_samples = signal[:, :HALO]
    next_head = from_behind(head_samples, "tm", -1)
    extended = jnp.concatenate([signal, next_head], axis=1)

    segments = [
        lax.dynamic_slice_in_dim(extended, window * STEP + offsets[tm_index * w_dev + window], WIN, 1)
        for window in range(w_dev)
    ]
    stacked = jnp.concatenate(segments, axis=0)
    spectra = jnp.dot(stacked, dft_table, preferred_element_type=jnp.float32)
    spectra = spectra.reshape(w_dev, channels_here, 2 * NF)
    whitened = whiten(spectra)
    half_rows = channels_here // n_tm

    row_windows = [lax.dynamic_slice_in_dim(whitened, tm_index * half_rows, half_rows, 1)]
    for e in range(1, n_tm):
        half = (tm_index - e + n_tm) % n_tm
        payload = lax.dynamic_slice_in_dim(whitened, half * half_rows, half_rows, 1)
        row_windows.append(exchange(payload, ("tm",), (n_tm,), lambda s, e=e: ((s[0] - e) % n_tm,)))
    row_own = jnp.concatenate(row_windows, axis=0)
    row_slots = [row_own]
    for d in range(1, n_pcol):
        row_slots.append(exchange(row_own, ("pcol",), (n_pcol,), lambda s, d=d: ((s[0] - d) % n_pcol,)))
    row_all = jnp.stack(row_slots, axis=0)

    col_slots = []
    for d in range(n_prow):
        if d == 0:
            near = whitened
        else:
            near = exchange(
                near, ("prow",), (n_prow,), lambda s, d=d: (s[0] - 1,) if 1 <= s[0] <= n_prow - d else None
            )
        per_tm = [near]
        for e in range(1, n_tm):
            per_tm.append(exchange(near, ("tm",), (n_tm,), lambda s, e=e: ((s[0] - e) % n_tm,)))
        col_slots.append(jnp.concatenate(per_tm, axis=0))
    col_all = jnp.stack(col_slots, axis=0)

    lags = lag_table(n_tm * w_dev)
    local_pairs = pair_list[0, 0]
    row_slot = (local_pairs[:, 0] - pcol_index + n_pcol) % n_pcol
    col_slot = jnp.clip(local_pairs[:, 1] - prow_index, 0, n_prow - 1)
    pairs = jnp.stack([row_slot, col_slot], axis=1).astype(jnp.int32)
    result = all_pairs(pairs, row_all, col_all, lags)
    return result.reshape(1, 1, NP, half_rows, channels_here, LAGS)


def solution(mesh):
    placed = (P(("prow", "pcol"), "tm"), P(), P("prow", "pcol", None, None))
    return jax.shard_map(
        on_device,
        mesh=mesh,
        in_specs=placed,
        out_specs=P("prow", "pcol", None, "tm", None, None),
        check_vma=False,
    )
```
